512 devices in a mesh: px: 32 (over y, x), py: 16 (over z, core).
Axes of the slice: x: 4, y: 8, z: 8, core: 2. Of those that a mesh axis runs over, the one named last changes fastest.
Arguments:
- solution: float32 [32, 16, 16, 136], P('px', 'py'), may hold values from -6 to 6
- residual: float32 [32, 16, 16, 136], P('px', 'py')
- direction: float32 [32, 16, 16, 136], P('px', 'py'), may hold values from -6 to 6
- rz_previous: float32 [16], replicated, may hold values from 34816 to 278528
- dual_inverse: bfloat16 [32, 16, 272, 272], P('px', 'py'), as said below
- dual_schur: bfloat16 [32, 16, 272, 272], P('px', 'py'), as said below
- coupling: bfloat16 [32, 16, 8, 272], P('px', 'py'), may hold values from -0.375 to 0.375
- coarse_inverse: float32 [32, 16, 2, 2], P('px', 'py'), as said below
- matching: int32 [32, 16, 2, 68], P('px', 'py'), may hold values from 0 to 67, as said below
- patch_counts: int32 [32, 16], P('px', 'py'), may hold values from 1 to 1, as said below
Outputs:
- new_solution: float32 [32, 16, 16, 136], P('px', 'py')
- new_residual: float32 [32, 16, 16, 136], P('px', 'py')
- new_direction: float32 [32, 16, 16, 136], P('px', 'py')
- rz_current: float32 [16], replicated
- residual_sq: float32 [16], replicated
The draws below stay inside these ranges and needn't reach their ends.
Inputs may be any that keep to these rules, and one draw needn't show every extreme that they name: `matching`: each row is 0 to 67 in order, or with the order of its 34 node pairs reversed (components kept). `patch_counts`: some device holds 1 active patches. `dual_inverse`: each block symmetric positive definite. `dual_schur`: each block symmetric positive definite. `coarse_inverse`: each 2 x 2 block symmetric positive definite.
All inputs are finite; a program needn't handle non-finite values.
Results may differ from the reference program's by a relative error of at most 0.0016.
Values sent between devices are 32-bit elements; how exact they have to be, the bound alone decides.
No kernel may reach another device: no remote copies, remote signals or barrier semaphores. Data moves between devices by JAX's collectives and lax.ppermute only.
A program may use at most 64 MiB of HBM per device.

```python
import math
import jax
import jax.numpy as jnp
from jax import lax

SIDE = 68
CORNER_DOFS = 8
CASES = 16
ROWS_DEV = 1
COLS_DEV = 1
DUAL = 272
EDGES = 136
PATCH_ROWS = 32
PATCH_COLS = 16
N_PX = 32
N_PY = 16


def spd_blocks(key):
    identity = jnp.eye(DUAL, dtype=jnp.float32)

    def one_row(row_number):
        row_key = jax.random.fold_in(key, row_number)
        keys = jax.random.split(row_key, 3)
        factor = jax.random.randint(keys[0], (PATCH_COLS, DUAL, DUAL), -4, 5).astype(jnp.float32)
        gram = jnp.einsum('pab,pcb->pac', factor, factor, precision=lax.Precision.HIGHEST)
        diagonal = jax.random.uniform(keys[1], (PATCH_COLS, DUAL), jnp.float32, 0.5, 1.5)
        scales = jnp.exp(jax.random.uniform(keys[2], (PATCH_COLS, 1, 1), jnp.float32, math.log(0.5), math.log(2.0)))
        full_block = (gram * (0.15 / DUAL) + diagonal[:, :, None] * identity) * scales
        return full_block.astype(jnp.bfloat16)
    return lax.map(one_row, jnp.arange(PATCH_ROWS))


def draw_dual_inverse(key, part):
    return spd_blocks(jax.random.fold_in(key, 11))


def draw_dual_schur(key, part):
    return spd_blocks(jax.random.fold_in(key, 23))


def draw_residual(key, part):
    keys = jax.random.split(jax.random.fold_in(key, 5), 2)
    shape = (PATCH_ROWS, PATCH_COLS, CASES, 2 * SIDE)
    base = jax.random.truncated_normal(keys[0], -4.0, 4.0, shape, jnp.float32)
    row_scale = 1.0 + 2.0 * jnp.arange(PATCH_ROWS, dtype=jnp.float32) / max(PATCH_ROWS - 1, 1)
    patch_scale = jnp.exp(jax.random.uniform(keys[1], (PATCH_ROWS, PATCH_COLS, 1, 1), jnp.float32, 0.0, math.log(4.0)))
    return (base * row_scale[:, None, None, None] * patch_scale).astype(jnp.float32)


def draw_coarse_inverse(key, part):
    keys = jax.random.split(jax.random.fold_in(key, 7), 3)
    first = jax.random.uniform(keys[0], (PATCH_ROWS, PATCH_COLS), jnp.float32, 1.0, 2.0)
    second = jax.random.uniform(keys[1], (PATCH_ROWS, PATCH_COLS), jnp.float32, 1.0, 2.0)
    mixed = jax.random.uniform(keys[2], (PATCH_ROWS, PATCH_COLS), jnp.float32, -0.5, 0.5)
    return jnp.stack([jnp.stack([first, mixed], -1), jnp.stack([mixed, second], -1)], -2)


def draw_matching(key, part):
    flips = jax.random.randint(jax.random.fold_in(key, 3), (PATCH_ROWS, PATCH_COLS, 2, 1), 0, 2)
    position = jnp.arange(SIDE, dtype=jnp.int32)
    reversed_order = 2 * (SIDE // 2 - 1 - position // 2) + position % 2
    return jnp.where(flips == 1, reversed_order, position).astype(jnp.int32)


def draw_patch_counts(key, part):
    keys = jax.random.split(jax.random.fold_in(key, 13), 2)
    counts = jax.random.randint(keys[0], (N_PX, N_PY), 1, ROWS_DEV * COLS_DEV + 1)
    chosen = jax.random.randint(keys[1], (), 0, N_PX * N_PY)
    flat_index = jnp.arange(N_PX * N_PY).reshape(N_PX, N_PY)
    return jnp.where(flat_index == chosen, ROWS_DEV * COLS_DEV, counts).astype(jnp.int32)


def level_of(key, dims, shards, smallest, high):
    factor_of, own = 1.0, jax.random.fold_in(key, 6)
    for dim, parts in shards:
        steps = jnp.exp(jax.random.uniform(jax.random.fold_in(own, dim), (parts,), jnp.float32, smallest / len(shards), high / len(shards)))
        factor_of = factor_of * jnp.repeat(steps, dims[dim] // parts).reshape([-1 if axis == dim else 1 for axis in range(len(dims))])
    return factor_of


def scatter_about(own_key, shape, scale, limit, cuts=(), kind=jnp.bfloat16):
    drawn = scale * jax.random.normal(own_key, shape, jnp.float32)
    if cuts:
        drawn = drawn * level_of(own_key, shape, cuts, -0.22, 0.18)
    return jnp.clip(drawn, -limit, limit).astype(kind)


def setup_inputs(seed: int = 0) -> dict:
    streams_of = jax.random.split(jax.random.key(seed), 11)
    solution = scatter_about(streams_of[0], (PATCH_ROWS, PATCH_COLS, CASES, EDGES), 1.0, 6.0, ((0, 32), (1, 16)), jnp.float32)
    residual = draw_residual(jax.random.fold_in(streams_of[10], 71), 0)
    direction = scatter_about(streams_of[2], (PATCH_ROWS, PATCH_COLS, CASES, EDGES), 1.0, 6.0, ((0, 32), (1, 16)), jnp.float32)
    rz_previous = jnp.clip(jnp.exp(jax.random.uniform(streams_of[3], (CASES,), jnp.float32, math.log(34816.0), math.log(278528.0))), 34816.0, 278528.0)
    dual_inverse = draw_dual_inverse(jax.random.fold_in(streams_of[10], 71), 0)
    dual_schur = draw_dual_schur(jax.random.fold_in(streams_of[10], 71), 0)
    coupling = scatter_about(streams_of[6], (PATCH_ROWS, PATCH_COLS, CORNER_DOFS, DUAL), DUAL ** -0.5, 0.375, ((0, 32), (1, 16)))
    coarse_inverse = draw_coarse_inverse(jax.random.fold_in(streams_of[10], 71), 0)
    matching = draw_matching(jax.random.fold_in(streams_of[10], 71), 0)
    patch_counts = draw_patch_counts(jax.random.fold_in(streams_of[10], 71), 0)
    return dict(solution=solution, residual=residual, direction=direction, rz_previous=rz_previous, dual_inverse=dual_inverse, dual_schur=dual_schur, coupling=coupling, coarse_inverse=coarse_inverse, matching=matching, patch_counts=patch_counts)


def from_before(values, along):
    zero_part = jnp.zeros_like(lax.slice_in_dim(values, 0, 1, axis=along))
    kept = lax.slice_in_dim(values, 0, values.shape[along] - 1, axis=along)
    return jnp.concatenate([zero_part, kept], along)


def from_after(values, along):
    zero_part = jnp.zeros_like(lax.slice_in_dim(values, 0, 1, axis=along))
    kept = lax.slice_in_dim(values, 1, values.shape[along], axis=along)
    return jnp.concatenate([kept, zero_part], along)


def permute_side(values, order):
    return jnp.take_along_axis(values, jnp.broadcast_to(order[:, :, None, :], values.shape), axis=3)


def spread_b(vector, matching):
    east_part = vector[..., :SIDE]
    north_part = vector[..., SIDE:]
    east_perm = permute_side(east_part, matching[:, :, 0])
    north_perm = permute_side(north_part, matching[:, :, 1])
    return jnp.concatenate([east_part, north_part, -from_before(east_perm, 1), -from_before(north_perm, 0)], 3)


def jump_b(side_values, matching, edge_mask):
    west_side = side_values[..., 2 * SIDE:3 * SIDE]
    south_side = side_values[..., 3 * SIDE:]
    east_term = permute_side(from_after(west_side, 1), matching[:, :, 0])
    north_term = permute_side(from_after(south_side, 0), matching[:, :, 1])
    joined = jnp.concatenate([side_values[..., :SIDE] - east_term, side_values[..., SIDE:2 * SIDE] - north_term], 3)
    return joined * edge_mask


def patch_products(matrices, vectors):
    def one_row(pair):
        return jnp.einsum("pab,pcb->pca", pair[0].astype(jnp.float32), pair[1].astype(jnp.float32),
                          precision=lax.Precision.HIGHEST)
    return lax.map(one_row, (matrices, vectors))


def reference(solution, residual, direction, rz_previous, dual_inverse, dual_schur, coupling, coarse_inverse, matching, patch_counts):
    grid_row = jnp.arange(PATCH_ROWS)
    grid_col = jnp.arange(PATCH_COLS)
    local_slot = (grid_row % ROWS_DEV)[:, None] * COLS_DEV + (grid_col % COLS_DEV)[None, :]
    block_count = jnp.repeat(jnp.repeat(patch_counts, ROWS_DEV, axis=0), COLS_DEV, axis=1)
    active = (local_slot < block_count).astype(jnp.float32)[:, :, None, None]
    edge_index = jnp.arange(2 * SIDE)
    edge_ok = jnp.where(edge_index[None, None, :] < SIDE,
                        (grid_col < PATCH_COLS - 1)[None, :, None] & (grid_row >= 0)[:, None, None],
                        (grid_row < PATCH_ROWS - 1)[:, None, None] & (grid_col >= 0)[None, :, None])
    edge_mask = active * edge_ok[:, :, None, :].astype(jnp.float32)
    vertex_mask = ((grid_row >= 1)[:, None] & (grid_col >= 1)[None, :]).astype(jnp.float32)[:, :, None, None]
    coupling_wide = coupling.astype(jnp.float32)

    def operator(vector):
        spread = spread_b(vector, matching).astype(jnp.bfloat16)
        inner_part = patch_products(dual_inverse, spread) * active
        corner = jnp.einsum("rpkb,rpcb->rpck", coupling_wide, spread.astype(jnp.float32),
                            precision=lax.Precision.HIGHEST) * active
        assembled = (corner[..., 0:2] + from_before(corner[..., 2:4], 1) + from_before(corner[..., 4:6], 0)
                     + from_before(from_before(corner[..., 6:8], 1), 0)) * vertex_mask
        coarse = jnp.einsum("rpxy,rpcy->rpcx", coarse_inverse, assembled, precision=lax.Precision.HIGHEST)
        corners_back = jnp.concatenate([coarse, from_after(coarse, 1), from_after(coarse, 0),
                                        from_after(from_after(coarse, 1), 0)], 3)
        correction = jnp.einsum("rpkb,rpck->rpcb", coupling_wide, corners_back, precision=lax.Precision.HIGHEST)
        return jump_b((inner_part + correction) * active, matching, edge_mask)

    def precondition(vector):
        spread = spread_b(0.5 * vector, matching).astype(jnp.bfloat16)
        side_values = patch_products(dual_schur, spread) * active
        return 0.5 * jump_b(side_values, matching, edge_mask)

    start_sol = solution * edge_mask
    start_res = residual * edge_mask
    start_dir = direction * edge_mask
    precond = precondition(start_res)
    rz_current = jnp.sum(start_res * precond, axis=(0, 1, 3))
    step_ratio = rz_current / rz_previous
    new_direction = precond + step_ratio[None, None, :, None] * start_dir
    image = operator(new_direction)
    curvature = jnp.sum(new_direction * image, axis=(0, 1, 3))
    step_length = rz_current / curvature
    new_solution = start_sol + step_length[None, None, :, None] * new_direction
    new_residual = start_res - step_length[None, None, :, None] * image
    residual_sq = jnp.sum(new_residual * new_residual, axis=(0, 1, 3))
    return new_solution, new_residual, new_direction, rz_current, residual_sq
```

```python
import jax
import jax.numpy as jnp
from jax import lax
from jax.sharding import PartitionSpec as P

SIDE = 68


def passed_along(value, axis, by):
    peers = lax.axis_size(axis)
    pairs = [(i, i + by) for i in range(peers) if 0 <= i + by < peers]
    return lax.ppermute(value, axis, pairs)


def all_sum(value):
    for axis in ("py", "px"):
        peers = lax.axis_size(axis)
        if peers & (peers - 1):
            value = lax.psum(value, axis)
            continue
        step = 1
        while step < peers:
            value = value + lax.ppermute(value, axis, [(i, i ^ step) for i in range(peers)])
            step *= 2
    return value


def permute_side(values, flip):
    shape = values.shape
    pairs = values.reshape(shape[:-1] + (shape[-1] // 2, 2))
    reversed_pairs = jnp.flip(pairs, axis=-2).reshape(shape)
    return jnp.where(flip[:, :, None, None], reversed_pairs, values)


def on_device(
    solution,
    residual,
    direction,
    rz_previous,
    dual_inverse,
    dual_schur,
    coupling,
    coarse_inverse,
    matching,
    patch_counts,
):
    rows_here = solution.shape[0]
    cols_here = solution.shape[1]
    total_rows = rows_here * lax.axis_size("px")
    total_cols = cols_here * lax.axis_size("py")
    grid_row = lax.axis_index("px") * rows_here + jnp.arange(rows_here)
    grid_col = lax.axis_index("py") * cols_here + jnp.arange(cols_here)
    local_slot = jnp.arange(rows_here)[:, None] * cols_here + jnp.arange(cols_here)[None, :]
    count_here = patch_counts[0, 0]
    active = (local_slot < count_here).astype(jnp.float32)[:, :, None, None]
    edge_index = jnp.arange(2 * SIDE)
    edge_ok = jnp.where(
        edge_index[None, None, :] < SIDE,
        (grid_col < total_cols - 1)[None, :, None] & (grid_row >= 0)[:, None, None],
        (grid_row < total_rows - 1)[:, None, None] & (grid_col >= 0)[None, :, None],
    )
    edge_mask = active * edge_ok[:, :, None, :].astype(jnp.float32)
    vertex_mask = ((grid_row >= 1)[:, None] & (grid_col >= 1)[None, :]).astype(jnp.float32)[
        :, :, None, None
    ]
    east_flip = matching[:, :, 0, 0] != 0
    north_flip = matching[:, :, 1, 0] != 0

    def spread_parts(vector):
        east_part = vector[..., :SIDE]
        north_part = vector[..., SIDE:]
        east_perm = permute_side(east_part, east_flip)
        north_perm = permute_side(north_part, north_flip)
        west_edge = passed_along(east_perm, "py", 1)
        from_west = jnp.concatenate([west_edge, east_perm[:, :-1]], 1)
        south_edge = passed_along(north_perm, "px", 1)
        from_south = jnp.concatenate([south_edge, north_perm[:-1]], 0)
        return east_part, north_part, from_west, from_south

    def spread_of(parts):
        east_part, north_part, from_west, from_south = parts
        return jnp.concatenate([east_part, north_part, -from_west, -from_south], 3)

    def jump_b(side_values):
        west_side = side_values[..., 2 * SIDE : 3 * SIDE]
        south_side = side_values[..., 3 * SIDE :]
        east_edge = passed_along(west_side, "py", -1)
        from_east = jnp.concatenate([west_side[:, 1:], east_edge], 1)
        north_edge = passed_along(south_side, "px", -1)
        from_north = jnp.concatenate([south_side[1:], north_edge], 0)
        east_term = permute_side(from_east, east_flip)
        north_term = permute_side(from_north, north_flip)
        joined = jnp.concatenate(
            [side_values[..., :SIDE] - east_term, side_values[..., SIDE : 2 * SIDE] - north_term], 3
        )
        return joined * edge_mask

    def patch_products(matrices, vectors):
        return (
            jnp.einsum("rpab,rpcb->rpca", matrices, vectors, preferred_element_type=jnp.float32)
            * active
        )

    start_sol = solution * edge_mask
    start_res = residual * edge_mask
    start_dir = direction * edge_mask
    dir_parts = spread_parts(start_dir)
    spread = spread_of(spread_parts(0.5 * start_res)).astype(jnp.bfloat16)
    side_values = patch_products(dual_schur, spread)
    precond = 0.5 * jump_b(side_values)
    precond_parts = spread_parts(precond)
    rz_current = all_sum(jnp.sum(start_res * precond, axis=(0, 1, 3)))
    step_ratio = rz_current / rz_previous
    ratio = step_ratio[None, None, :, None]
    new_direction = precond + ratio * start_dir
    spread = spread_of(
        tuple(p + ratio * d for p, d in zip(precond_parts, dir_parts))
    ).astype(jnp.bfloat16)
    inner_part = patch_products(dual_inverse, spread)
    corner = (
        jnp.einsum("rpkb,rpcb->rpck", coupling, spread, preferred_element_type=jnp.float32) * active
    )
    flat_corner = corner.reshape(rows_here, cols_here, -1)
    west_column = passed_along(flat_corner, "py", 1)
    with_west = jnp.concatenate([west_column, flat_corner], 1)
    south_row = passed_along(with_west, "px", 1)
    extended = jnp.concatenate([south_row, with_west], 0)
    extended = extended.reshape(rows_here + 1, cols_here + 1, corner.shape[2], corner.shape[3])
    assembled = (
        extended[1:, 1:, :, 0:2]
        + extended[1:, :-1, :, 2:4]
        + extended[:-1, 1:, :, 4:6]
        + extended[:-1, :-1, :, 6:8]
    ) * vertex_mask
    coarse = jnp.einsum(
        "rpxy,rpcy->rpcx", coarse_inverse, assembled, precision=lax.Precision.HIGHEST
    )
    flat_coarse = coarse.reshape(rows_here, cols_here, -1)
    east_column = passed_along(flat_coarse, "py", -1)
    with_east = jnp.concatenate([flat_coarse, east_column], 1)
    north_row = passed_along(with_east, "px", -1)
    beside_all = jnp.concatenate([with_east, north_row], 0)
    beside_all = beside_all.reshape(rows_here + 1, cols_here + 1, coarse.shape[2], 2)
    corners_back = jnp.concatenate(
        [beside_all[:-1, :-1], beside_all[:-1, 1:], beside_all[1:, :-1], beside_all[1:, 1:]], 3
    )
    correction = jnp.einsum(
        "rpkb,rpck->rpcb",
        coupling.astype(jnp.float32),
        corners_back,
        precision=lax.Precision.HIGHEST,
    )
    image = jump_b((inner_part + correction) * active)
    curvature = all_sum(jnp.sum(new_direction * image, axis=(0, 1, 3)))
    step_length = rz_current / curvature
    new_solution = start_sol + step_length[None, None, :, None] * new_direction
    new_residual = start_res - step_length[None, None, :, None] * image
    residual_sq = all_sum(jnp.sum(new_residual * new_residual, axis=(0, 1, 3)))
    return (new_solution, new_residual, new_direction, rz_current, residual_sq)


def solution(mesh):
    in_specs = (
        P("px", "py", None, None),
        P("px", "py", None, None),
        P("px", "py", None, None),
        P(),
        P("px", "py", None, None),
        P("px", "py", None, None),
        P("px", "py", None, None),
        P("px", "py", None, None),
        P("px", "py", None, None),
        P("px", "py"),
    )
    out_specs = (
        P("px", "py", None, None),
        P("px", "py", None, None),
        P("px", "py", None, None),
        P(),
        P(),
    )
    return jax.shard_map(
        on_device, mesh=mesh, in_specs=in_specs, out_specs=out_specs, check_vma=False
    )
```

```python
import jax
import jax.numpy as jnp
from jax import lax
from jax.sharding import PartitionSpec as P

SIDE = 68


def passed_along(value, axis, by):
    peers = lax.axis_size(axis)
    pairs = [(i, i + by) for i in range(peers) if 0 <= i + by < peers]
    return lax.ppermute(value, axis, pairs)


def all_sum(value):
    for axis in ("py", "px"):
        peers = lax.axis_size(axis)
        if peers & (peers - 1):
            value = lax.psum(value, axis)
            continue
        step = 1
        while step < peers:
            value = value + lax.ppermute(value, axis, [(i, i ^ step) for i in range(peers)])
            step *= 2
    return value


def two_sum(a, b):
    total = a + b
    back = total - a
    return total, (a - (total - back)) + (b - back)


def split_float(a):
    scaled = 4097.0 * a
    high = scaled - (scaled - a)
    return high, a - high


def two_prod(a, b):
    product = a * b
    a_high, a_low = split_float(a)
    b_high, b_low = split_float(b)
    error = ((a_high * b_high - product) + a_high * b_low + a_low * b_high) + a_low * b_low
    return product, error


def df_add(x, y):
    total, error = two_sum(x[0], y[0])
    error = error + (x[1] + y[1])
    high = total + error
    return high, error - (high - total)


def df_scale(x, factor):
    product, error = two_prod(x[0], factor)
    error = error + x[1] * factor
    high = product + error
    return high, error - (high - product)


def df_case_sums(a, b):
    a = jnp.moveaxis(a, 2, 0).reshape(a.shape[2], -1)
    b = jnp.moveaxis(b, 2, 0).reshape(b.shape[2], -1)
    high, low = two_prod(a, b)
    while high.shape[1] > 1:
        if high.shape[1] % 2:
            high = jnp.pad(high, ((0, 0), (0, 1)))
            low = jnp.pad(low, ((0, 0), (0, 1)))
        half = high.shape[1] // 2
        high, low = df_add((high[:, :half], low[:, :half]), (high[:, half:], low[:, half:]))
    return high[:, 0], low[:, 0]


def all_sum_mixed(plain, pairs):
    for axis in ("py", "px"):
        peers = lax.axis_size(axis)
        step = 1
        while step < peers:
            packed = jnp.stack([plain] + [part for pair in pairs for part in pair])
            other = lax.ppermute(packed, axis, [(i, i ^ step) for i in range(peers)])
            plain = plain + other[0]
            pairs = [
                df_add(pair, (other[1 + 2 * k], other[2 + 2 * k])) for k, pair in enumerate(pairs)
            ]
            step *= 2
    return plain, pairs


def permute_side(values, flip):
    shape = values.shape
    pairs = values.reshape(shape[:-1] + (shape[-1] // 2, 2))
    reversed_pairs = jnp.flip(pairs, axis=-2).reshape(shape)
    return jnp.where(flip[:, :, None, None], reversed_pairs, values)


def on_device(
    solution,
    residual,
    direction,
    rz_previous,
    dual_inverse,
    dual_schur,
    coupling,
    coarse_inverse,
    matching,
    patch_counts,
):
    rows_here = solution.shape[0]
    cols_here = solution.shape[1]
    total_rows = rows_here * lax.axis_size("px")
    total_cols = cols_here * lax.axis_size("py")
    grid_row = lax.axis_index("px") * rows_here + jnp.arange(rows_here)
    grid_col = lax.axis_index("py") * cols_here + jnp.arange(cols_here)
    local_slot = jnp.arange(rows_here)[:, None] * cols_here + jnp.arange(cols_here)[None, :]
    count_here = patch_counts[0, 0]
    active = (local_slot < count_here).astype(jnp.float32)[:, :, None, None]
    edge_index = jnp.arange(2 * SIDE)
    edge_ok = jnp.where(
        edge_index[None, None, :] < SIDE,
        (grid_col < total_cols - 1)[None, :, None] & (grid_row >= 0)[:, None, None],
        (grid_row < total_rows - 1)[:, None, None] & (grid_col >= 0)[None, :, None],
    )
    edge_mask = active * edge_ok[:, :, None, :].astype(jnp.float32)
    vertex_mask = ((grid_row >= 1)[:, None] & (grid_col >= 1)[None, :]).astype(jnp.float32)[
        :, :, None, None
    ]
    east_flip = matching[:, :, 0, 0] != 0
    north_flip = matching[:, :, 1, 0] != 0

    def spread_parts(vector):
        east_part = vector[..., :SIDE]
        north_part = vector[..., SIDE:]
        east_perm = permute_side(east_part, east_flip)
        north_perm = permute_side(north_part, north_flip)
        west_edge = passed_along(east_perm, "py", 1)
        from_west = jnp.concatenate([west_edge, east_perm[:, :-1]], 1)
        south_edge = passed_along(north_perm, "px", 1)
        from_south = jnp.concatenate([south_edge, north_perm[:-1]], 0)
        return east_part, north_part, from_west, from_south

    def spread_of(parts):
        east_part, north_part, from_west, from_south = parts
        return jnp.concatenate([east_part, north_part, -from_west, -from_south], 3)

    def jump_b(side_values):
        west_side = side_values[..., 2 * SIDE : 3 * SIDE]
        south_side = side_values[..., 3 * SIDE :]
        east_edge = passed_along(west_side, "py", -1)
        from_east = jnp.concatenate([west_side[:, 1:], east_edge], 1)
        north_edge = passed_along(south_side, "px", -1)
        from_north = jnp.concatenate([south_side[1:], north_edge], 0)
        east_term = permute_side(from_east, east_flip)
        north_term = permute_side(from_north, north_flip)
        joined = jnp.concatenate(
            [side_values[..., :SIDE] - east_term, side_values[..., SIDE : 2 * SIDE] - north_term], 3
        )
        return joined * edge_mask

    def patch_products(matrices, vectors):
        return (
            jnp.einsum("rpab,rpcb->rpca", matrices, vectors, preferred_element_type=jnp.float32)
            * active
        )

    start_sol = solution * edge_mask
    start_res = residual * edge_mask
    start_dir = direction * edge_mask
    dir_parts = spread_parts(start_dir)
    spread = spread_of(spread_parts(0.5 * start_res)).astype(jnp.bfloat16)
    side_values = patch_products(dual_schur, spread)
    precond = 0.5 * jump_b(side_values)
    precond_parts = spread_parts(precond)
    rz_current = all_sum(jnp.sum(start_res * precond, axis=(0, 1, 3)))
    step_ratio = rz_current / rz_previous
    ratio = step_ratio[None, None, :, None]
    new_direction = precond + ratio * start_dir
    spread = spread_of(
        tuple(p + ratio * d for p, d in zip(precond_parts, dir_parts))
    ).astype(jnp.bfloat16)
    inner_part = patch_products(dual_inverse, spread)
    corner = (
        jnp.einsum("rpkb,rpcb->rpck", coupling, spread, preferred_element_type=jnp.float32) * active
    )
    flat_corner = corner.reshape(rows_here, cols_here, -1)
    west_column = passed_along(flat_corner, "py", 1)
    with_west = jnp.concatenate([west_column, flat_corner], 1)
    south_row = passed_along(with_west, "px", 1)
    extended = jnp.concatenate([south_row, with_west], 0)
    extended = extended.reshape(rows_here + 1, cols_here + 1, corner.shape[2], corner.shape[3])
    assembled = (
        extended[1:, 1:, :, 0:2]
        + extended[1:, :-1, :, 2:4]
        + extended[:-1, 1:, :, 4:6]
        + extended[:-1, :-1, :, 6:8]
    ) * vertex_mask
    coarse = jnp.einsum(
        "rpxy,rpcy->rpcx", coarse_inverse, assembled, precision=lax.Precision.HIGHEST
    )
    flat_coarse = coarse.reshape(rows_here, cols_here, -1)
    east_column = passed_along(flat_coarse, "py", -1)
    with_east = jnp.concatenate([flat_coarse, east_column], 1)
    north_row = passed_along(with_east, "px", -1)
    beside_all = jnp.concatenate([with_east, north_row], 0)
    beside_all = beside_all.reshape(rows_here + 1, cols_here + 1, coarse.shape[2], 2)
    corners_back = jnp.concatenate(
        [beside_all[:-1, :-1], beside_all[:-1, 1:], beside_all[1:, :-1], beside_all[1:, 1:]], 3
    )
    correction = jnp.einsum(
        "rpkb,rpck->rpcb",
        coupling.astype(jnp.float32),
        corners_back,
        precision=lax.Precision.HIGHEST,
    )
    image = jump_b((inner_part + correction) * active)
    curvature, (res_res, res_img, img_img) = all_sum_mixed(
        jnp.sum(new_direction * image, axis=(0, 1, 3)),
        [df_case_sums(start_res, start_res), df_case_sums(start_res, image), df_case_sums(image, image)],
    )
    step_length = rz_current / curvature
    new_solution = start_sol + step_length[None, None, :, None] * new_direction
    new_residual = start_res - step_length[None, None, :, None] * image
    cross = df_scale(res_img, -2.0 * step_length)
    square = df_scale(df_scale(img_img, step_length), step_length)
    merged = df_add(df_add(res_res, cross), square)
    merged_sq = merged[0] + merged[1]
    scale = res_res[0] + step_length * step_length * img_img[0]
    trusted = jnp.all(jnp.isfinite(scale) & (merged_sq > 0) & (scale <= 1e7 * merged_sq))
    residual_sq = lax.cond(
        trusted,
        lambda: merged_sq,
        lambda: all_sum(jnp.sum(new_residual * new_residual, axis=(0, 1, 3))),
    )
    return (new_solution, new_residual, new_direction, rz_current, residual_sq)


def solution(mesh):
    in_specs = (
        P("px", "py", None, None),
        P("px", "py", None, None),
        P("px", "py", None, None),
        P(),
        P("px", "py", None, None),
        P("px", "py", None, None),
        P("px", "py", None, None),
        P("px", "py", None, None),
        P("px", "py", None, None),
        P("px", "py"),
    )
    out_specs = (
        P("px", "py", None, None),
        P("px", "py", None, None),
        P("px", "py", None, None),
        P(),
        P(),
    )
    return jax.shard_map(
        on_device, mesh=mesh, in_specs=in_specs, out_specs=out_specs, check_vma=False
    )
```

```python
import jax
import jax.numpy as jnp
from jax import lax
from jax.sharding import PartitionSpec as P

SIDE = 68


def passed_along(value, axis, by):
    peers = lax.axis_size(axis)
    pairs = [(i, i + by) for i in range(peers) if 0 <= i + by < peers]
    return lax.ppermute(value, axis, pairs)


def all_sum(value):
    for axis in ("py", "px"):
        peers = lax.axis_size(axis)
        if peers & (peers - 1):
            value = lax.psum(value, axis)
            continue
        step = 1
        while step < peers:
            value = value + lax.ppermute(value, axis, [(i, i ^ step) for i in range(peers)])
            step *= 2
    return value


def two_sum(a, b):
    total = a + b
    back = total - a
    return total, (a - (total - back)) + (b - back)


def split_float(a):
    scaled = 4097.0 * a
    high = scaled - (scaled - a)
    return high, a - high


def two_prod(a, b):
    product = a * b
    a_high, a_low = split_float(a)
    b_high, b_low = split_float(b)
    error = ((a_high * b_high - product) + a_high * b_low + a_low * b_high) + a_low * b_low
    return product, error


def df_add(x, y):
    total, error = two_sum(x[0], y[0])
    error = error + (x[1] + y[1])
    high = total + error
    return high, error - (high - total)


def df_scale(x, factor):
    product, error = two_prod(x[0], factor)
    error = error + x[1] * factor
    high = product + error
    return high, error - (high - product)


def df_case_sums(a, b):
    a = jnp.moveaxis(a, 2, 0).reshape(a.shape[2], -1)
    b = jnp.moveaxis(b, 2, 0).reshape(b.shape[2], -1)
    high, low = two_prod(a, b)
    while high.shape[1] > 1:
        if high.shape[1] % 2:
            high = jnp.pad(high, ((0, 0), (0, 1)))
            low = jnp.pad(low, ((0, 0), (0, 1)))
        half = high.shape[1] // 2
        high, low = df_add((high[:, :half], low[:, :half]), (high[:, half:], low[:, half:]))
    return high[:, 0], low[:, 0]


def all_sum_mixed(plain, pairs):
    for axis in ("py", "px"):
        peers = lax.axis_size(axis)
        step = 1
        while step < peers:
            packed = jnp.stack([plain] + [part for pair in pairs for part in pair])
            other = lax.ppermute(packed, axis, [(i, i ^ step) for i in range(peers)])
            plain = plain + other[0]
            pairs = [
                df_add(pair, (other[1 + 2 * k], other[2 + 2 * k])) for k, pair in enumerate(pairs)
            ]
            step *= 2
    return plain, pairs


def permute_side(values, flip):
    shape = values.shape
    pairs = values.reshape(shape[:-1] + (shape[-1] // 2, 2))
    reversed_pairs = jnp.flip(pairs, axis=-2).reshape(shape)
    return jnp.where(flip[:, :, None, None], reversed_pairs, values)


def on_device(
    solution,
    residual,
    direction,
    rz_previous,
    dual_inverse,
    dual_schur,
    coupling,
    coarse_inverse,
    matching,
    patch_counts,
):
    rows_here = solution.shape[0]
    cols_here = solution.shape[1]
    total_rows = rows_here * lax.axis_size("px")
    total_cols = cols_here * lax.axis_size("py")
    grid_row = lax.axis_index("px") * rows_here + jnp.arange(rows_here)
    grid_col = lax.axis_index("py") * cols_here + jnp.arange(cols_here)
    local_slot = jnp.arange(rows_here)[:, None] * cols_here + jnp.arange(cols_here)[None, :]
    count_here = patch_counts[0, 0]
    active = (local_slot < count_here).astype(jnp.float32)[:, :, None, None]
    edge_index = jnp.arange(2 * SIDE)
    edge_ok = jnp.where(
        edge_index[None, None, :] < SIDE,
        (grid_col < total_cols - 1)[None, :, None] & (grid_row >= 0)[:, None, None],
        (grid_row < total_rows - 1)[:, None, None] & (grid_col >= 0)[None, :, None],
    )
    edge_mask = active * edge_ok[:, :, None, :].astype(jnp.float32)
    vertex_mask = ((grid_row >= 1)[:, None] & (grid_col >= 1)[None, :]).astype(jnp.float32)[
        :, :, None, None
    ]
    east_flip = matching[:, :, 0, 0] != 0
    north_flip = matching[:, :, 1, 0] != 0

    def spread_parts(vector):
        east_part = vector[..., :SIDE]
        north_part = vector[..., SIDE:]
        east_perm = permute_side(east_part, east_flip)
        north_perm = permute_side(north_part, north_flip)
        west_edge = passed_along(east_perm, "py", 1)
        from_west = jnp.concatenate([west_edge, east_perm[:, :-1]], 1)
        south_edge = passed_along(north_perm, "px", 1)
        from_south = jnp.concatenate([south_edge, north_perm[:-1]], 0)
        return east_part, north_part, from_west, from_south

    def spread_of(parts):
        east_part, north_part, from_west, from_south = parts
        return jnp.concatenate([east_part, north_part, -from_west, -from_south], 3)

    def jump_b(side_values):
        west_side = side_values[..., 2 * SIDE : 3 * SIDE]
        south_side = side_values[..., 3 * SIDE :]
        east_edge = passed_along(west_side, "py", -1)
        from_east = jnp.concatenate([west_side[:, 1:], east_edge], 1)
        north_edge = passed_along(south_side, "px", -1)
        from_north = jnp.concatenate([south_side[1:], north_edge], 0)
        east_term = permute_side(from_east, east_flip)
        north_term = permute_side(from_north, north_flip)
        joined = jnp.concatenate(
            [side_values[..., :SIDE] - east_term, side_values[..., SIDE : 2 * SIDE] - north_term], 3
        )
        return joined * edge_mask

    def patch_products(matrices, vectors):
        return (
            jnp.einsum("rpab,rpcb->rpca", matrices, vectors, preferred_element_type=jnp.float32)
            * active
        )

    def spread_pair(first, second):
        east_perm = jnp.stack(
            [permute_side(first[..., :SIDE], east_flip), permute_side(second[..., :SIDE], east_flip)]
        )
        north_perm = jnp.stack(
            [permute_side(first[..., SIDE:], north_flip), permute_side(second[..., SIDE:], north_flip)]
        )
        west_edge = passed_along(east_perm, "py", 1)
        from_west = jnp.concatenate([west_edge, east_perm[:, :, :-1]], 2)
        south_edge = passed_along(north_perm, "px", 1)
        from_south = jnp.concatenate([south_edge, north_perm[:, :-1]], 1)
        return [
            (field[..., :SIDE], field[..., SIDE:], from_west[k], from_south[k])
            for k, field in enumerate((first, second))
        ]

    def jump_and_spread(side_values):
        east_side = side_values[..., :SIDE]
        north_side = side_values[..., SIDE : 2 * SIDE]
        west_side = side_values[..., 2 * SIDE : 3 * SIDE]
        south_side = side_values[..., 3 * SIDE :]
        ones = jnp.broadcast_to(active, east_side.shape)
        east_edge = passed_along(west_side, "py", -1)
        from_east = jnp.concatenate([west_side[:, 1:], east_edge], 1)
        north_edge = passed_along(south_side, "px", -1)
        from_north = jnp.concatenate([south_side[1:], north_edge], 0)
        east_perm_side = permute_side(east_side, east_flip)
        north_perm_side = permute_side(north_side, north_flip)
        west_sent = passed_along(jnp.stack([east_perm_side, ones]), "py", 1)
        south_sent = passed_along(jnp.stack([north_perm_side, ones]), "px", 1)
        east_term = permute_side(from_east, east_flip)
        north_term = permute_side(from_north, north_flip)
        joined = jnp.concatenate([east_side - east_term, north_side - north_term], 3)
        half_jump = 0.5 * (joined * edge_mask)
        west_edge = 0.5 * ((west_sent[0] - west_side[:, :1]) * west_sent[1])
        south_edge = 0.5 * ((south_sent[0] - south_side[:1]) * south_sent[1])
        local_east = permute_side(half_jump[..., :SIDE], east_flip)
        local_north = permute_side(half_jump[..., SIDE:], north_flip)
        from_west = jnp.concatenate([west_edge, local_east[:, :-1]], 1)
        from_south = jnp.concatenate([south_edge, local_north[:-1]], 0)
        return half_jump, (half_jump[..., :SIDE], half_jump[..., SIDE:], from_west, from_south)

    start_sol = solution * edge_mask
    start_res = residual * edge_mask
    start_dir = direction * edge_mask
    res_parts, dir_parts = spread_pair(0.5 * start_res, start_dir)
    spread = spread_of(res_parts).astype(jnp.bfloat16)
    side_values = patch_products(dual_schur, spread)
    precond, precond_parts = jump_and_spread(side_values)
    rz_current = all_sum(jnp.sum(start_res * precond, axis=(0, 1, 3)))
    step_ratio = rz_current / rz_previous
    ratio = step_ratio[None, None, :, None]
    new_direction = precond + ratio * start_dir
    spread = spread_of(
        tuple(p + ratio * d for p, d in zip(precond_parts, dir_parts))
    ).astype(jnp.bfloat16)
    inner_part = patch_products(dual_inverse, spread)
    corner = (
        jnp.einsum("rpkb,rpcb->rpck", coupling, spread, preferred_element_type=jnp.float32) * active
    )
    flat_corner = corner.reshape(rows_here, cols_here, -1)
    west_column = passed_along(flat_corner, "py", 1)
    with_west = jnp.concatenate([west_column, flat_corner], 1)
    south_row = passed_along(with_west, "px", 1)
    extended = jnp.concatenate([south_row, with_west], 0)
    extended = extended.reshape(rows_here + 1, cols_here + 1, corner.shape[2], corner.shape[3])
    assembled = (
        extended[1:, 1:, :, 0:2]
        + extended[1:, :-1, :, 2:4]
        + extended[:-1, 1:, :, 4:6]
        + extended[:-1, :-1, :, 6:8]
    ) * vertex_mask
    coarse = jnp.einsum(
        "rpxy,rpcy->rpcx", coarse_inverse, assembled, precision=lax.Precision.HIGHEST
    )
    flat_coarse = coarse.reshape(rows_here, cols_here, -1)
    east_column = passed_along(flat_coarse, "py", -1)
    with_east = jnp.concatenate([flat_coarse, east_column], 1)
    north_row = passed_along(with_east, "px", -1)
    beside_all = jnp.concatenate([with_east, north_row], 0)
    beside_all = beside_all.reshape(rows_here + 1, cols_here + 1, coarse.shape[2], 2)
    corners_back = jnp.concatenate(
        [beside_all[:-1, :-1], beside_all[:-1, 1:], beside_all[1:, :-1], beside_all[1:, 1:]], 3
    )
    correction = jnp.einsum(
        "rpkb,rpck->rpcb",
        coupling.astype(jnp.float32),
        corners_back,
        precision=lax.Precision.HIGHEST,
    )
    image = jump_b((inner_part + correction) * active)
    curvature, (res_res, res_img, img_img) = all_sum_mixed(
        jnp.sum(new_direction * image, axis=(0, 1, 3)),
        [df_case_sums(start_res, start_res), df_case_sums(start_res, image), df_case_sums(image, image)],
    )
    step_length = rz_current / curvature
    new_solution = start_sol + step_length[None, None, :, None] * new_direction
    new_residual = start_res - step_length[None, None, :, None] * image
    cross = df_scale(res_img, -2.0 * step_length)
    square = df_scale(df_scale(img_img, step_length), step_length)
    merged = df_add(df_add(res_res, cross), square)
    merged_sq = merged[0] + merged[1]
    scale = res_res[0] + step_length * step_length * img_img[0]
    trusted = jnp.all(jnp.isfinite(scale) & (merged_sq > 0) & (scale <= 1e7 * merged_sq))
    residual_sq = lax.cond(
        trusted,
        lambda: merged_sq,
        lambda: all_sum(jnp.sum(new_residual * new_residual, axis=(0, 1, 3))),
    )
    return (new_solution, new_residual, new_direction, rz_current, residual_sq)


def solution(mesh):
    in_specs = (
        P("px", "py", None, None),
        P("px", "py", None, None),
        P("px", "py", None, None),
        P(),
        P("px", "py", None, None),
        P("px", "py", None, None),
        P("px", "py", None, None),
        P("px", "py", None, None),
        P("px", "py", None, None),
        P("px", "py"),
    )
    out_specs = (
        P("px", "py", None, None),
        P("px", "py", None, None),
        P("px", "py", None, None),
        P(),
        P(),
    )
    return jax.shard_map(
        on_device, mesh=mesh, in_specs=in_specs, out_specs=out_specs, check_vma=False
    )
```

```python
import jax
import jax.numpy as jnp
from jax import lax
from jax.sharding import PartitionSpec as P

SIDE = 68


def passed_along(value, axis, by):
    peers = lax.axis_size(axis)
    pairs = [(i, i + by) for i in range(peers) if 0 <= i + by < peers]
    return lax.ppermute(value, axis, pairs)


def exchanged_together(moves):
    values = lax.optimization_barrier(tuple(value for value, _, _ in moves))
    received = tuple(passed_along(value, axis, by) for value, (_, axis, by) in zip(values, moves))
    return lax.optimization_barrier(received)


def all_sum(value):
    for axis in ("py", "px"):
        peers = lax.axis_size(axis)
        if peers & (peers - 1):
            value = lax.psum(value, axis)
            continue
        step = 1
        while step < peers:
            value = value + lax.ppermute(value, axis, [(i, i ^ step) for i in range(peers)])
            step *= 2
    return value


def two_sum(a, b):
    total = a + b
    back = total - a
    return total, (a - (total - back)) + (b - back)


def split_float(a):
    scaled = 4097.0 * a
    high = scaled - (scaled - a)
    return high, a - high


def two_prod(a, b):
    product = a * b
    a_high, a_low = split_float(a)
    b_high, b_low = split_float(b)
    error = ((a_high * b_high - product) + a_high * b_low + a_low * b_high) + a_low * b_low
    return product, error


def df_add(x, y):
    total, error = two_sum(x[0], y[0])
    error = error + (x[1] + y[1])
    high = total + error
    return high, error - (high - total)


def df_scale(x, factor):
    product, error = two_prod(x[0], factor)
    error = error + x[1] * factor
    high = product + error
    return high, error - (high - product)


def df_case_sums(a, b):
    a = jnp.moveaxis(a, 2, 0).reshape(a.shape[2], -1)
    b = jnp.moveaxis(b, 2, 0).reshape(b.shape[2], -1)
    high, low = two_prod(a, b)
    while high.shape[1] > 1:
        if high.shape[1] % 2:
            high = jnp.pad(high, ((0, 0), (0, 1)))
            low = jnp.pad(low, ((0, 0), (0, 1)))
        half = high.shape[1] // 2
        high, low = df_add((high[:, :half], low[:, :half]), (high[:, half:], low[:, half:]))
    return high[:, 0], low[:, 0]


def all_sum_mixed(plain, pairs):
    for axis in ("py", "px"):
        peers = lax.axis_size(axis)
        step = 1
        while step < peers:
            packed = jnp.stack([plain] + [part for pair in pairs for part in pair])
            other = lax.ppermute(packed, axis, [(i, i ^ step) for i in range(peers)])
            plain = plain + other[0]
            pairs = [
                df_add(pair, (other[1 + 2 * k], other[2 + 2 * k])) for k, pair in enumerate(pairs)
            ]
            step *= 2
    return plain, pairs


def permute_side(values, flip):
    shape = values.shape
    pairs = values.reshape(shape[:-1] + (shape[-1] // 2, 2))
    reversed_pairs = jnp.flip(pairs, axis=-2).reshape(shape)
    return jnp.where(flip[:, :, None, None], reversed_pairs, values)


def on_device(
    solution,
    residual,
    direction,
    rz_previous,
    dual_inverse,
    dual_schur,
    coupling,
    coarse_inverse,
    matching,
    patch_counts,
):
    rows_here = solution.shape[0]
    cols_here = solution.shape[1]
    total_rows = rows_here * lax.axis_size("px")
    total_cols = cols_here * lax.axis_size("py")
    grid_row = lax.axis_index("px") * rows_here + jnp.arange(rows_here)
    grid_col = lax.axis_index("py") * cols_here + jnp.arange(cols_here)
    local_slot = jnp.arange(rows_here)[:, None] * cols_here + jnp.arange(cols_here)[None, :]
    count_here = patch_counts[0, 0]
    active = (local_slot < count_here).astype(jnp.float32)[:, :, None, None]
    edge_index = jnp.arange(2 * SIDE)
    edge_ok = jnp.where(
        edge_index[None, None, :] < SIDE,
        (grid_col < total_cols - 1)[None, :, None] & (grid_row >= 0)[:, None, None],
        (grid_row < total_rows - 1)[:, None, None] & (grid_col >= 0)[None, :, None],
    )
    edge_mask = active * edge_ok[:, :, None, :].astype(jnp.float32)
    vertex_mask = ((grid_row >= 1)[:, None] & (grid_col >= 1)[None, :]).astype(jnp.float32)[
        :, :, None, None
    ]
    east_flip = matching[:, :, 0, 0] != 0
    north_flip = matching[:, :, 1, 0] != 0

    def spread_parts(vector):
        east_part = vector[..., :SIDE]
        north_part = vector[..., SIDE:]
        east_perm = permute_side(east_part, east_flip)
        north_perm = permute_side(north_part, north_flip)
        west_edge = passed_along(east_perm, "py", 1)
        from_west = jnp.concatenate([west_edge, east_perm[:, :-1]], 1)
        south_edge = passed_along(north_perm, "px", 1)
        from_south = jnp.concatenate([south_edge, north_perm[:-1]], 0)
        return east_part, north_part, from_west, from_south

    def spread_of(parts):
        east_part, north_part, from_west, from_south = parts
        return jnp.concatenate([east_part, north_part, -from_west, -from_south], 3)

    def jump_b(side_values):
        west_side = side_values[..., 2 * SIDE : 3 * SIDE]
        south_side = side_values[..., 3 * SIDE :]
        east_edge, north_edge = exchanged_together(
            [(west_side, "py", -1), (south_side, "px", -1)]
        )
        from_east = jnp.concatenate([west_side[:, 1:], east_edge], 1)
        from_north = jnp.concatenate([south_side[1:], north_edge], 0)
        east_term = permute_side(from_east, east_flip)
        north_term = permute_side(from_north, north_flip)
        joined = jnp.concatenate(
            [side_values[..., :SIDE] - east_term, side_values[..., SIDE : 2 * SIDE] - north_term], 3
        )
        return joined * edge_mask

    def patch_products(matrices, vectors):
        return (
            jnp.einsum("rpab,rpcb->rpca", matrices, vectors, preferred_element_type=jnp.float32)
            * active
        )

    def spread_pair(first, second):
        east_perm = jnp.stack(
            [permute_side(first[..., :SIDE], east_flip), permute_side(second[..., :SIDE], east_flip)]
        )
        north_perm = jnp.stack(
            [permute_side(first[..., SIDE:], north_flip), permute_side(second[..., SIDE:], north_flip)]
        )
        west_edge = passed_along(east_perm, "py", 1)
        from_west = jnp.concatenate([west_edge, east_perm[:, :, :-1]], 2)
        south_edge = passed_along(north_perm, "px", 1)
        from_south = jnp.concatenate([south_edge, north_perm[:, :-1]], 1)
        return [
            (field[..., :SIDE], field[..., SIDE:], from_west[k], from_south[k])
            for k, field in enumerate((first, second))
        ]

    def jump_and_spread(side_values):
        east_side = side_values[..., :SIDE]
        north_side = side_values[..., SIDE : 2 * SIDE]
        west_side = side_values[..., 2 * SIDE : 3 * SIDE]
        south_side = side_values[..., 3 * SIDE :]
        ones = jnp.broadcast_to(active, east_side.shape)
        east_edge, north_edge = exchanged_together(
            [(west_side, "py", -1), (south_side, "px", -1)]
        )
        from_east = jnp.concatenate([west_side[:, 1:], east_edge], 1)
        from_north = jnp.concatenate([south_side[1:], north_edge], 0)
        east_perm_side = permute_side(east_side, east_flip)
        north_perm_side = permute_side(north_side, north_flip)
        west_sent = passed_along(jnp.stack([east_perm_side, ones]), "py", 1)
        south_sent = passed_along(jnp.stack([north_perm_side, ones]), "px", 1)
        east_term = permute_side(from_east, east_flip)
        north_term = permute_side(from_north, north_flip)
        joined = jnp.concatenate([east_side - east_term, north_side - north_term], 3)
        half_jump = 0.5 * (joined * edge_mask)
        west_edge = 0.5 * ((west_sent[0] - west_side[:, :1]) * west_sent[1])
        south_edge = 0.5 * ((south_sent[0] - south_side[:1]) * south_sent[1])
        local_east = permute_side(half_jump[..., :SIDE], east_flip)
        local_north = permute_side(half_jump[..., SIDE:], north_flip)
        from_west = jnp.concatenate([west_edge, local_east[:, :-1]], 1)
        from_south = jnp.concatenate([south_edge, local_north[:-1]], 0)
        return half_jump, (half_jump[..., :SIDE], half_jump[..., SIDE:], from_west, from_south)

    start_sol = solution * edge_mask
    start_res = residual * edge_mask
    start_dir = direction * edge_mask
    res_parts, dir_parts = spread_pair(0.5 * start_res, start_dir)
    spread = spread_of(res_parts).astype(jnp.bfloat16)
    side_values = patch_products(dual_schur, spread)
    precond, precond_parts = jump_and_spread(side_values)
    rz_current = all_sum(jnp.sum(start_res * precond, axis=(0, 1, 3)))
    step_ratio = rz_current / rz_previous
    ratio = step_ratio[None, None, :, None]
    new_direction = precond + ratio * start_dir
    spread = spread_of(
        tuple(p + ratio * d for p, d in zip(precond_parts, dir_parts))
    ).astype(jnp.bfloat16)
    inner_part = patch_products(dual_inverse, spread)
    corner = (
        jnp.einsum("rpkb,rpcb->rpck", coupling, spread, preferred_element_type=jnp.float32) * active
    )
    flat_corner = corner.reshape(rows_here, cols_here, -1)
    west_column = passed_along(flat_corner, "py", 1)
    with_west = jnp.concatenate([west_column, flat_corner], 1)
    south_row = passed_along(with_west, "px", 1)
    extended = jnp.concatenate([south_row, with_west], 0)
    extended = extended.reshape(rows_here + 1, cols_here + 1, corner.shape[2], corner.shape[3])
    assembled = (
        extended[1:, 1:, :, 0:2]
        + extended[1:, :-1, :, 2:4]
        + extended[:-1, 1:, :, 4:6]
        + extended[:-1, :-1, :, 6:8]
    ) * vertex_mask
    coarse = jnp.einsum(
        "rpxy,rpcy->rpcx", coarse_inverse, assembled, precision=lax.Precision.HIGHEST
    )
    flat_coarse = coarse.reshape(rows_here, cols_here, -1)
    east_column = passed_along(flat_coarse, "py", -1)
    with_east = jnp.concatenate([flat_coarse, east_column], 1)
    north_row = passed_along(with_east, "px", -1)
    beside_all = jnp.concatenate([with_east, north_row], 0)
    beside_all = beside_all.reshape(rows_here + 1, cols_here + 1, coarse.shape[2], 2)
    corners_back = jnp.concatenate(
        [beside_all[:-1, :-1], beside_all[:-1, 1:], beside_all[1:, :-1], beside_all[1:, 1:]], 3
    )
    correction = jnp.einsum(
        "rpkb,rpck->rpcb",
        coupling.astype(jnp.float32),
        corners_back,
        precision=lax.Precision.HIGHEST,
    )
    image = jump_b((inner_part + correction) * active)
    curvature, (res_res, res_img, img_img) = all_sum_mixed(
        jnp.sum(new_direction * image, axis=(0, 1, 3)),
        [df_case_sums(start_res, start_res), df_case_sums(start_res, image), df_case_sums(image, image)],
    )
    step_length = rz_current / curvature
    new_solution = start_sol + step_length[None, None, :, None] * new_direction
    new_residual = start_res - step_length[None, None, :, None] * image
    cross = df_scale(res_img, -2.0 * step_length)
    square = df_scale(df_scale(img_img, step_length), step_length)
    merged = df_add(df_add(res_res, cross), square)
    merged_sq = merged[0] + merged[1]
    scale = res_res[0] + step_length * step_length * img_img[0]
    trusted = jnp.all(jnp.isfinite(scale) & (merged_sq > 0) & (scale <= 1e7 * merged_sq))
    residual_sq = lax.cond(
        trusted,
        lambda: merged_sq,
        lambda: all_sum(jnp.sum(new_residual * new_residual, axis=(0, 1, 3))),
    )
    return (new_solution, new_residual, new_direction, rz_current, residual_sq)


def solution(mesh):
    in_specs = (
        P("px", "py", None, None),
        P("px", "py", None, None),
        P("px", "py", None, None),
        P(),
        P("px", "py", None, None),
        P("px", "py", None, None),
        P("px", "py", None, None),
        P("px", "py", None, None),
        P("px", "py", None, None),
        P("px", "py"),
    )
    out_specs = (
        P("px", "py", None, None),
        P("px", "py", None, None),
        P("px", "py", None, None),
        P(),
        P(),
    )
    return jax.shard_map(
        on_device, mesh=mesh, in_specs=in_specs, out_specs=out_specs, check_vma=False
    )
```

```python
import jax
import jax.numpy as jnp
from jax import lax
from jax.sharding import PartitionSpec as P

SIDE = 68


def passed_along(value, axis, by):
    peers = lax.axis_size(axis)
    pairs = [(i, i + by) for i in range(peers) if 0 <= i + by < peers]
    return lax.ppermute(value, axis, pairs)


def exchanged_together(moves):
    values = lax.optimization_barrier(tuple(value for value, _, _ in moves))
    received = tuple(passed_along(value, axis, by) for value, (_, axis, by) in zip(values, moves))
    return lax.optimization_barrier(received)


INNER = {"py": 2, "px": 4}


def butterfly_rounds(axis):
    peers = lax.axis_size(axis)
    inner = INNER.get(axis, peers)
    if peers % inner or inner & (inner - 1) or (peers // inner) & (peers // inner - 1):
        inner = peers
    rounds = []
    step = 1
    while step < inner:
        rounds.append([(i, i ^ step) for i in range(peers)])
        step *= 2
    outer = peers // inner
    gray = [k ^ (k >> 1) for k in range(outer)]
    place = {g: k for k, g in enumerate(gray)}
    step = 1
    while step < outer:
        rounds.append(
            [(i, place[gray[i // inner] ^ step] * inner + i % inner) for i in range(peers)]
        )
        step *= 2
    return rounds


def all_sum(value):
    for axis in ("py", "px"):
        peers = lax.axis_size(axis)
        if peers & (peers - 1):
            value = lax.psum(value, axis)
            continue
        for pairs in butterfly_rounds(axis):
            value = value + lax.ppermute(value, axis, pairs)
    return value


def two_sum(a, b):
    total = a + b
    back = total - a
    return total, (a - (total - back)) + (b - back)


def split_float(a):
    scaled = 4097.0 * a
    high = scaled - (scaled - a)
    return high, a - high


def two_prod(a, b):
    product = a * b
    a_high, a_low = split_float(a)
    b_high, b_low = split_float(b)
    error = ((a_high * b_high - product) + a_high * b_low + a_low * b_high) + a_low * b_low
    return product, error


def df_add(x, y):
    total, error = two_sum(x[0], y[0])
    error = error + (x[1] + y[1])
    high = total + error
    return high, error - (high - total)


def df_scale(x, factor):
    product, error = two_prod(x[0], factor)
    error = error + x[1] * factor
    high = product + error
    return high, error - (high - product)


def df_case_sums(a, b):
    a = jnp.moveaxis(a, 2, 0).reshape(a.shape[2], -1)
    b = jnp.moveaxis(b, 2, 0).reshape(b.shape[2], -1)
    high, low = two_prod(a, b)
    while high.shape[1] > 1:
        if high.shape[1] % 2:
            high = jnp.pad(high, ((0, 0), (0, 1)))
            low = jnp.pad(low, ((0, 0), (0, 1)))
        half = high.shape[1] // 2
        high, low = df_add((high[:, :half], low[:, :half]), (high[:, half:], low[:, half:]))
    return high[:, 0], low[:, 0]


def all_sum_mixed(plain, pairs):
    for axis in ("py", "px"):
        for partners in butterfly_rounds(axis):
            packed = jnp.stack([plain] + [part for pair in pairs for part in pair])
            other = lax.ppermute(packed, axis, partners)
            plain = plain + other[0]
            pairs = [
                df_add(pair, (other[1 + 2 * k], other[2 + 2 * k])) for k, pair in enumerate(pairs)
            ]
    return plain, pairs


def permute_side(values, flip):
    shape = values.shape
    pairs = values.reshape(shape[:-1] + (shape[-1] // 2, 2))
    reversed_pairs = jnp.flip(pairs, axis=-2).reshape(shape)
    return jnp.where(flip[:, :, None, None], reversed_pairs, values)


def on_device(
    solution,
    residual,
    direction,
    rz_previous,
    dual_inverse,
    dual_schur,
    coupling,
    coarse_inverse,
    matching,
    patch_counts,
):
    rows_here = solution.shape[0]
    cols_here = solution.shape[1]
    total_rows = rows_here * lax.axis_size("px")
    total_cols = cols_here * lax.axis_size("py")
    grid_row = lax.axis_index("px") * rows_here + jnp.arange(rows_here)
    grid_col = lax.axis_index("py") * cols_here + jnp.arange(cols_here)
    local_slot = jnp.arange(rows_here)[:, None] * cols_here + jnp.arange(cols_here)[None, :]
    count_here = patch_counts[0, 0]
    active = (local_slot < count_here).astype(jnp.float32)[:, :, None, None]
    edge_index = jnp.arange(2 * SIDE)
    edge_ok = jnp.where(
        edge_index[None, None, :] < SIDE,
        (grid_col < total_cols - 1)[None, :, None] & (grid_row >= 0)[:, None, None],
        (grid_row < total_rows - 1)[:, None, None] & (grid_col >= 0)[None, :, None],
    )
    edge_mask = active * edge_ok[:, :, None, :].astype(jnp.float32)
    vertex_mask = ((grid_row >= 1)[:, None] & (grid_col >= 1)[None, :]).astype(jnp.float32)[
        :, :, None, None
    ]
    east_flip = matching[:, :, 0, 0] != 0
    north_flip = matching[:, :, 1, 0] != 0

    def spread_parts(vector):
        east_part = vector[..., :SIDE]
        north_part = vector[..., SIDE:]
        east_perm = permute_side(east_part, east_flip)
        north_perm = permute_side(north_part, north_flip)
        west_edge = passed_along(east_perm, "py", 1)
        from_west = jnp.concatenate([west_edge, east_perm[:, :-1]], 1)
        south_edge = passed_along(north_perm, "px", 1)
        from_south = jnp.concatenate([south_edge, north_perm[:-1]], 0)
        return east_part, north_part, from_west, from_south

    def spread_of(parts):
        east_part, north_part, from_west, from_south = parts
        return jnp.concatenate([east_part, north_part, -from_west, -from_south], 3)

    def jump_b(side_values):
        west_side = side_values[..., 2 * SIDE : 3 * SIDE]
        south_side = side_values[..., 3 * SIDE :]
        east_edge, north_edge = exchanged_together(
            [(west_side, "py", -1), (south_side, "px", -1)]
        )
        from_east = jnp.concatenate([west_side[:, 1:], east_edge], 1)
        from_north = jnp.concatenate([south_side[1:], north_edge], 0)
        east_term = permute_side(from_east, east_flip)
        north_term = permute_side(from_north, north_flip)
        joined = jnp.concatenate(
            [side_values[..., :SIDE] - east_term, side_values[..., SIDE : 2 * SIDE] - north_term], 3
        )
        return joined * edge_mask

    def patch_products(matrices, vectors):
        return (
            jnp.einsum("rpab,rpcb->rpca", matrices, vectors, preferred_element_type=jnp.float32)
            * active
        )

    def spread_pair(first, second):
        east_perm = jnp.stack(
            [permute_side(first[..., :SIDE], east_flip), permute_side(second[..., :SIDE], east_flip)]
        )
        north_perm = jnp.stack(
            [permute_side(first[..., SIDE:], north_flip), permute_side(second[..., SIDE:], north_flip)]
        )
        west_edge = passed_along(east_perm, "py", 1)
        from_west = jnp.concatenate([west_edge, east_perm[:, :, :-1]], 2)
        south_edge = passed_along(north_perm, "px", 1)
        from_south = jnp.concatenate([south_edge, north_perm[:, :-1]], 1)
        return [
            (field[..., :SIDE], field[..., SIDE:], from_west[k], from_south[k])
            for k, field in enumerate((first, second))
        ]

    def jump_and_spread(side_values):
        east_side = side_values[..., :SIDE]
        north_side = side_values[..., SIDE : 2 * SIDE]
        west_side = side_values[..., 2 * SIDE : 3 * SIDE]
        south_side = side_values[..., 3 * SIDE :]
        ones = jnp.broadcast_to(active, east_side.shape)
        east_edge, north_edge = exchanged_together(
            [(west_side, "py", -1), (south_side, "px", -1)]
        )
        from_east = jnp.concatenate([west_side[:, 1:], east_edge], 1)
        from_north = jnp.concatenate([south_side[1:], north_edge], 0)
        east_perm_side = permute_side(east_side, east_flip)
        north_perm_side = permute_side(north_side, north_flip)
        west_sent = passed_along(jnp.stack([east_perm_side, ones]), "py", 1)
        south_sent = passed_along(jnp.stack([north_perm_side, ones]), "px", 1)
        east_term = permute_side(from_east, east_flip)
        north_term = permute_side(from_north, north_flip)
        joined = jnp.concatenate([east_side - east_term, north_side - north_term], 3)
        half_jump = 0.5 * (joined * edge_mask)
        west_edge = 0.5 * ((west_sent[0] - west_side[:, :1]) * west_sent[1])
        south_edge = 0.5 * ((south_sent[0] - south_side[:1]) * south_sent[1])
        local_east = permute_side(half_jump[..., :SIDE], east_flip)
        local_north = permute_side(half_jump[..., SIDE:], north_flip)
        from_west = jnp.concatenate([west_edge, local_east[:, :-1]], 1)
        from_south = jnp.concatenate([south_edge, local_north[:-1]], 0)
        return half_jump, (half_jump[..., :SIDE], half_jump[..., SIDE:], from_west, from_south)

    start_sol = solution * edge_mask
    start_res = residual * edge_mask
    start_dir = direction * edge_mask
    res_parts, dir_parts = spread_pair(0.5 * start_res, start_dir)
    spread = spread_of(res_parts).astype(jnp.bfloat16)
    side_values = patch_products(dual_schur, spread)
    precond, precond_parts = jump_and_spread(side_values)
    rz_current = all_sum(jnp.sum(start_res * precond, axis=(0, 1, 3)))
    step_ratio = rz_current / rz_previous
    ratio = step_ratio[None, None, :, None]
    new_direction = precond + ratio * start_dir
    spread = spread_of(
        tuple(p + ratio * d for p, d in zip(precond_parts, dir_parts))
    ).astype(jnp.bfloat16)
    inner_part = patch_products(dual_inverse, spread)
    corner = (
        jnp.einsum("rpkb,rpcb->rpck", coupling, spread, preferred_element_type=jnp.float32) * active
    )
    flat_corner = corner.reshape(rows_here, cols_here, -1)
    west_column = passed_along(flat_corner, "py", 1)
    with_west = jnp.concatenate([west_column, flat_corner], 1)
    south_row = passed_along(with_west, "px", 1)
    extended = jnp.concatenate([south_row, with_west], 0)
    extended = extended.reshape(rows_here + 1, cols_here + 1, corner.shape[2], corner.shape[3])
    assembled = (
        extended[1:, 1:, :, 0:2]
        + extended[1:, :-1, :, 2:4]
        + extended[:-1, 1:, :, 4:6]
        + extended[:-1, :-1, :, 6:8]
    ) * vertex_mask
    coarse = jnp.einsum(
        "rpxy,rpcy->rpcx", coarse_inverse, assembled, precision=lax.Precision.HIGHEST
    )
    flat_coarse = coarse.reshape(rows_here, cols_here, -1)
    east_column = passed_along(flat_coarse, "py", -1)
    with_east = jnp.concatenate([flat_coarse, east_column], 1)
    north_row = passed_along(with_east, "px", -1)
    beside_all = jnp.concatenate([with_east, north_row], 0)
    beside_all = beside_all.reshape(rows_here + 1, cols_here + 1, coarse.shape[2], 2)
    corners_back = jnp.concatenate(
        [beside_all[:-1, :-1], beside_all[:-1, 1:], beside_all[1:, :-1], beside_all[1:, 1:]], 3
    )
    correction = jnp.einsum(
        "rpkb,rpck->rpcb",
        coupling.astype(jnp.float32),
        corners_back,
        precision=lax.Precision.HIGHEST,
    )
    image = jump_b((inner_part + correction) * active)
    curvature, (res_res, res_img, img_img) = all_sum_mixed(
        jnp.sum(new_direction * image, axis=(0, 1, 3)),
        [df_case_sums(start_res, start_res), df_case_sums(start_res, image), df_case_sums(image, image)],
    )
    step_length = rz_current / curvature
    new_solution = start_sol + step_length[None, None, :, None] * new_direction
    new_residual = start_res - step_length[None, None, :, None] * image
    cross = df_scale(res_img, -2.0 * step_length)
    square = df_scale(df_scale(img_img, step_length), step_length)
    merged = df_add(df_add(res_res, cross), square)
    merged_sq = merged[0] + merged[1]
    scale = res_res[0] + step_length * step_length * img_img[0]
    trusted = jnp.all(jnp.isfinite(scale) & (merged_sq > 0) & (scale <= 1e7 * merged_sq))
    residual_sq = lax.cond(
        trusted,
        lambda: merged_sq,
        lambda: all_sum(jnp.sum(new_residual * new_residual, axis=(0, 1, 3))),
    )
    return (new_solution, new_residual, new_direction, rz_current, residual_sq)


def solution(mesh):
    in_specs = (
        P("px", "py", None, None),
        P("px", "py", None, None),
        P("px", "py", None, None),
        P(),
        P("px", "py", None, None),
        P("px", "py", None, None),
        P("px", "py", None, None),
        P("px", "py", None, None),
        P("px", "py", None, None),
        P("px", "py"),
    )
    out_specs = (
        P("px", "py", None, None),
        P("px", "py", None, None),
        P("px", "py", None, None),
        P(),
        P(),
    )
    return jax.shard_map(
        on_device, mesh=mesh, in_specs=in_specs, out_specs=out_specs, check_vma=False
    )
```

```python
import jax
import jax.numpy as jnp
from jax import lax
from jax.sharding import PartitionSpec as P

SIDE = 68


def passed_along(value, axis, by):
    peers = lax.axis_size(axis)
    pairs = [(i, i + by) for i in range(peers) if 0 <= i + by < peers]
    return lax.ppermute(value, axis, pairs)


def exchanged_together(moves):
    values = lax.optimization_barrier(tuple(value for value, _, _ in moves))
    received = tuple(passed_along(value, axis, by) for value, (_, axis, by) in zip(values, moves))
    return lax.optimization_barrier(received)


INNER = {"py": 2, "px": 4}


def butterfly_rounds(axis):
    peers = lax.axis_size(axis)
    inner = INNER.get(axis, peers)
    if peers % inner or inner & (inner - 1) or (peers // inner) & (peers // inner - 1):
        inner = peers
    rounds = []
    step = 1
    while step < inner:
        rounds.append([(i, i ^ step) for i in range(peers)])
        step *= 2
    outer = peers // inner
    gray = [k ^ (k >> 1) for k in range(outer)]
    place = {g: k for k, g in enumerate(gray)}
    step = 1
    while step < outer:
        rounds.append(
            [(i, place[gray[i // inner] ^ step] * inner + i % inner) for i in range(peers)]
        )
        step *= 2
    return rounds


def all_sum(value):
    for axis in ("py", "px"):
        peers = lax.axis_size(axis)
        if peers & (peers - 1):
            value = lax.psum(value, axis)
            continue
        for pairs in butterfly_rounds(axis):
            value = value + lax.ppermute(value, axis, pairs)
    return value


def two_sum(a, b):
    total = a + b
    back = total - a
    return total, (a - (total - back)) + (b - back)


def split_float(a):
    scaled = 4097.0 * a
    high = scaled - (scaled - a)
    return high, a - high


def two_prod(a, b):
    product = a * b
    a_high, a_low = split_float(a)
    b_high, b_low = split_float(b)
    error = ((a_high * b_high - product) + a_high * b_low + a_low * b_high) + a_low * b_low
    return product, error


def df_add(x, y):
    total, error = two_sum(x[0], y[0])
    error = error + (x[1] + y[1])
    high = total + error
    return high, error - (high - total)


def df_scale(x, factor):
    product, error = two_prod(x[0], factor)
    error = error + x[1] * factor
    high = product + error
    return high, error - (high - product)


def df_case_sums(a, b):
    a = jnp.moveaxis(a, 2, 0).reshape(a.shape[2], -1)
    b = jnp.moveaxis(b, 2, 0).reshape(b.shape[2], -1)
    high, low = two_prod(a, b)
    while high.shape[1] > 1:
        if high.shape[1] % 2:
            high = jnp.pad(high, ((0, 0), (0, 1)))
            low = jnp.pad(low, ((0, 0), (0, 1)))
        half = high.shape[1] // 2
        high, low = df_add((high[:, :half], low[:, :half]), (high[:, half:], low[:, half:]))
    return high[:, 0], low[:, 0]


def all_sum_mixed(plain, pairs):
    for axis in ("py", "px"):
        for partners in butterfly_rounds(axis):
            packed = jnp.stack([plain] + [part for pair in pairs for part in pair])
            other = lax.ppermute(packed, axis, partners)
            plain = plain + other[0]
            pairs = [
                df_add(pair, (other[1 + 2 * k], other[2 + 2 * k])) for k, pair in enumerate(pairs)
            ]
    return plain, pairs


def permute_side(values, flip):
    shape = values.shape
    pairs = values.reshape(shape[:-1] + (shape[-1] // 2, 2))
    reversed_pairs = jnp.flip(pairs, axis=-2).reshape(shape)
    return jnp.where(flip[:, :, None, None], reversed_pairs, values)


def on_device(
    solution,
    residual,
    direction,
    rz_previous,
    dual_inverse,
    dual_schur,
    coupling,
    coarse_inverse,
    matching,
    patch_counts,
):
    rows_here = solution.shape[0]
    cols_here = solution.shape[1]
    total_rows = rows_here * lax.axis_size("px")
    total_cols = cols_here * lax.axis_size("py")
    grid_row = lax.axis_index("px") * rows_here + jnp.arange(rows_here)
    grid_col = lax.axis_index("py") * cols_here + jnp.arange(cols_here)
    local_slot = jnp.arange(rows_here)[:, None] * cols_here + jnp.arange(cols_here)[None, :]
    count_here = patch_counts[0, 0]
    active = (local_slot < count_here).astype(jnp.float32)[:, :, None, None]
    edge_index = jnp.arange(2 * SIDE)
    edge_ok = jnp.where(
        edge_index[None, None, :] < SIDE,
        (grid_col < total_cols - 1)[None, :, None] & (grid_row >= 0)[:, None, None],
        (grid_row < total_rows - 1)[:, None, None] & (grid_col >= 0)[None, :, None],
    )
    edge_mask = active * edge_ok[:, :, None, :].astype(jnp.float32)
    vertex_mask = ((grid_row >= 1)[:, None] & (grid_col >= 1)[None, :]).astype(jnp.float32)[
        :, :, None, None
    ]
    east_flip = matching[:, :, 0, 0] != 0
    north_flip = matching[:, :, 1, 0] != 0

    def spread_parts(vector):
        east_part = vector[..., :SIDE]
        north_part = vector[..., SIDE:]
        east_perm = permute_side(east_part, east_flip)
        north_perm = permute_side(north_part, north_flip)
        west_edge = passed_along(east_perm, "py", 1)
        from_west = jnp.concatenate([west_edge, east_perm[:, :-1]], 1)
        south_edge = passed_along(north_perm, "px", 1)
        from_south = jnp.concatenate([south_edge, north_perm[:-1]], 0)
        return east_part, north_part, from_west, from_south

    def spread_of(parts):
        east_part, north_part, from_west, from_south = parts
        return jnp.concatenate([east_part, north_part, -from_west, -from_south], 3)

    def jump_b(side_values):
        west_side = side_values[..., 2 * SIDE : 3 * SIDE]
        south_side = side_values[..., 3 * SIDE :]
        east_edge, north_edge = exchanged_together(
            [(west_side, "py", -1), (south_side, "px", -1)]
        )
        from_east = jnp.concatenate([west_side[:, 1:], east_edge], 1)
        from_north = jnp.concatenate([south_side[1:], north_edge], 0)
        east_term = permute_side(from_east, east_flip)
        north_term = permute_side(from_north, north_flip)
        joined = jnp.concatenate(
            [side_values[..., :SIDE] - east_term, side_values[..., SIDE : 2 * SIDE] - north_term], 3
        )
        return joined * edge_mask

    def patch_products(matrices, vectors):
        return (
            jnp.einsum("rpab,rpcb->rpca", matrices, vectors, preferred_element_type=jnp.float32)
            * active
        )

    def spread_pair(first, second):
        east_perm = jnp.stack(
            [permute_side(first[..., :SIDE], east_flip), permute_side(second[..., :SIDE], east_flip)]
        )
        north_perm = jnp.stack(
            [permute_side(first[..., SIDE:], north_flip), permute_side(second[..., SIDE:], north_flip)]
        )
        west_edge = passed_along(east_perm, "py", 1)
        from_west = jnp.concatenate([west_edge, east_perm[:, :, :-1]], 2)
        south_edge = passed_along(north_perm, "px", 1)
        from_south = jnp.concatenate([south_edge, north_perm[:, :-1]], 1)
        return [
            (field[..., :SIDE], field[..., SIDE:], from_west[k], from_south[k])
            for k, field in enumerate((first, second))
        ]

    def jump_and_spread(side_values):
        east_side = side_values[..., :SIDE]
        north_side = side_values[..., SIDE : 2 * SIDE]
        west_side = side_values[..., 2 * SIDE : 3 * SIDE]
        south_side = side_values[..., 3 * SIDE :]
        ones = jnp.broadcast_to(active, east_side.shape)
        east_edge, north_edge = exchanged_together(
            [(west_side, "py", -1), (south_side, "px", -1)]
        )
        from_east = jnp.concatenate([west_side[:, 1:], east_edge], 1)
        from_north = jnp.concatenate([south_side[1:], north_edge], 0)
        east_perm_side = permute_side(east_side, east_flip)
        north_perm_side = permute_side(north_side, north_flip)
        west_sent = passed_along(jnp.stack([east_perm_side, ones]), "py", 1)
        south_sent = passed_along(jnp.stack([north_perm_side, ones]), "px", 1)
        east_term = permute_side(from_east, east_flip)
        north_term = permute_side(from_north, north_flip)
        joined = jnp.concatenate([east_side - east_term, north_side - north_term], 3)
        half_jump = 0.5 * (joined * edge_mask)
        west_edge = 0.5 * ((west_sent[0] - west_side[:, :1]) * west_sent[1])
        south_edge = 0.5 * ((south_sent[0] - south_side[:1]) * south_sent[1])
        local_east = permute_side(half_jump[..., :SIDE], east_flip)
        local_north = permute_side(half_jump[..., SIDE:], north_flip)
        from_west = jnp.concatenate([west_edge, local_east[:, :-1]], 1)
        from_south = jnp.concatenate([south_edge, local_north[:-1]], 0)
        return half_jump, (half_jump[..., :SIDE], half_jump[..., SIDE:], from_west, from_south)

    start_sol = solution * edge_mask
    start_res = residual * edge_mask
    start_dir = direction * edge_mask
    res_parts, dir_parts = spread_pair(0.5 * start_res, start_dir)
    spread = spread_of(res_parts).astype(jnp.bfloat16)
    side_values = patch_products(dual_schur, spread)
    precond, precond_parts = jump_and_spread(side_values)
    rz_current = all_sum(jnp.sum(start_res * precond, axis=(0, 1, 3)))
    step_ratio = rz_current / rz_previous
    ratio = step_ratio[None, None, :, None]
    new_direction = precond + ratio * start_dir
    spread = spread_of(
        tuple(p + ratio * d for p, d in zip(precond_parts, dir_parts))
    ).astype(jnp.bfloat16)
    inner_part = patch_products(dual_inverse, spread)
    corner = (
        jnp.einsum("rpkb,rpcb->rpck", coupling, spread, preferred_element_type=jnp.float32) * active
    )
    corner_width = corner.shape[2] * corner.shape[3]
    payload = jnp.concatenate(
        [
            corner.reshape(rows_here, cols_here, corner_width),
            coarse_inverse.reshape(rows_here, cols_here, 4),
        ],
        2,
    )
    from_west_col, from_east_col = exchanged_together([(payload, "py", 1), (payload, "py", -1)])
    row = jnp.concatenate([from_west_col[:, -1:], payload, from_east_col[:, :1]], 1)
    from_south_row, from_north_row = exchanged_together([(row, "px", 1), (row, "px", -1)])
    block = jnp.concatenate([from_south_row[-1:], row, from_north_row[:1]], 0)
    corners = block[..., :corner_width].reshape(
        rows_here + 2, cols_here + 2, corner.shape[2], corner.shape[3]
    )
    blocks = block[..., corner_width:].reshape(rows_here + 2, cols_here + 2, 2, 2)
    vertex_row = lax.axis_index("px") * rows_here + jnp.arange(rows_here + 1)
    vertex_col = lax.axis_index("py") * cols_here + jnp.arange(cols_here + 1)
    vertex_ok = ((vertex_row >= 1)[:, None] & (vertex_col >= 1)[None, :]).astype(jnp.float32)[
        :, :, None, None
    ]
    assembled = (
        corners[1:, 1:, :, 0:2]
        + corners[1:, :-1, :, 2:4]
        + corners[:-1, 1:, :, 4:6]
        + corners[:-1, :-1, :, 6:8]
    ) * vertex_ok
    coarse = jnp.einsum(
        "rpxy,rpcy->rpcx", blocks[1:, 1:], assembled, precision=lax.Precision.HIGHEST
    )
    corners_back = jnp.concatenate(
        [coarse[:-1, :-1], coarse[:-1, 1:], coarse[1:, :-1], coarse[1:, 1:]], 3
    )
    correction = jnp.einsum(
        "rpkb,rpck->rpcb",
        coupling.astype(jnp.float32),
        corners_back,
        precision=lax.Precision.HIGHEST,
    )
    image = jump_b((inner_part + correction) * active)
    curvature, (res_res, res_img, img_img) = all_sum_mixed(
        jnp.sum(new_direction * image, axis=(0, 1, 3)),
        [df_case_sums(start_res, start_res), df_case_sums(start_res, image), df_case_sums(image, image)],
    )
    step_length = rz_current / curvature
    new_solution = start_sol + step_length[None, None, :, None] * new_direction
    new_residual = start_res - step_length[None, None, :, None] * image
    cross = df_scale(res_img, -2.0 * step_length)
    square = df_scale(df_scale(img_img, step_length), step_length)
    merged = df_add(df_add(res_res, cross), square)
    merged_sq = merged[0] + merged[1]
    scale = res_res[0] + step_length * step_length * img_img[0]
    trusted = jnp.all(jnp.isfinite(scale) & (merged_sq > 0) & (scale <= 1e7 * merged_sq))
    residual_sq = lax.cond(
        trusted,
        lambda: merged_sq,
        lambda: all_sum(jnp.sum(new_residual * new_residual, axis=(0, 1, 3))),
    )
    return (new_solution, new_residual, new_direction, rz_current, residual_sq)


def solution(mesh):
    in_specs = (
        P("px", "py", None, None),
        P("px", "py", None, None),
        P("px", "py", None, None),
        P(),
        P("px", "py", None, None),
        P("px", "py", None, None),
        P("px", "py", None, None),
        P("px", "py", None, None),
        P("px", "py", None, None),
        P("px", "py"),
    )
    out_specs = (
        P("px", "py", None, None),
        P("px", "py", None, None),
        P("px", "py", None, None),
        P(),
        P(),
    )
    return jax.shard_map(
        on_device, mesh=mesh, in_specs=in_specs, out_specs=out_specs, check_vma=False
    )
```

```python
import jax
import jax.numpy as jnp
from jax import lax
from jax.sharding import PartitionSpec as P

SIDE = 68


def passed_along(value, axis, by):
    peers = lax.axis_size(axis)
    pairs = [(i, i + by) for i in range(peers) if 0 <= i + by < peers]
    return lax.ppermute(value, axis, pairs)


def exchanged_together(moves):
    values = lax.optimization_barrier(tuple(value for value, _, _ in moves))
    received = tuple(passed_along(value, axis, by) for value, (_, axis, by) in zip(values, moves))
    return lax.optimization_barrier(received)


INNER = {"py": 2, "px": 4}


def butterfly_rounds(axis):
    peers = lax.axis_size(axis)
    inner = INNER.get(axis, peers)
    if peers % inner or inner & (inner - 1) or (peers // inner) & (peers // inner - 1):
        inner = peers
    rounds = []
    step = 1
    while step < inner:
        rounds.append([(i, i ^ step) for i in range(peers)])
        step *= 2
    outer = peers // inner
    gray = [k ^ (k >> 1) for k in range(outer)]
    place = {g: k for k, g in enumerate(gray)}
    step = 1
    while step < outer:
        rounds.append(
            [(i, place[gray[i // inner] ^ step] * inner + i % inner) for i in range(peers)]
        )
        step *= 2
    return rounds


def gathered(value, axis):
    peers = lax.axis_size(axis)
    copies = jnp.broadcast_to(value[None], (peers,) + value.shape)
    return lax.all_to_all(copies, axis, 0, 0, tiled=False)


def all_sum(value):
    for axis in ("py", "px"):
        value = jnp.sum(gathered(value, axis), axis=0)
    return value


def two_sum(a, b):
    total = a + b
    back = total - a
    return total, (a - (total - back)) + (b - back)


def split_float(a):
    scaled = 4097.0 * a
    high = scaled - (scaled - a)
    return high, a - high


def two_prod(a, b):
    product = a * b
    a_high, a_low = split_float(a)
    b_high, b_low = split_float(b)
    error = ((a_high * b_high - product) + a_high * b_low + a_low * b_high) + a_low * b_low
    return product, error


def df_add(x, y):
    total, error = two_sum(x[0], y[0])
    error = error + (x[1] + y[1])
    high = total + error
    return high, error - (high - total)


def df_scale(x, factor):
    product, error = two_prod(x[0], factor)
    error = error + x[1] * factor
    high = product + error
    return high, error - (high - product)


def df_case_sums(a, b):
    a = jnp.moveaxis(a, 2, 0).reshape(a.shape[2], -1)
    b = jnp.moveaxis(b, 2, 0).reshape(b.shape[2], -1)
    high, low = two_prod(a, b)
    while high.shape[1] > 1:
        if high.shape[1] % 2:
            high = jnp.pad(high, ((0, 0), (0, 1)))
            low = jnp.pad(low, ((0, 0), (0, 1)))
        half = high.shape[1] // 2
        high, low = df_add((high[:, :half], low[:, :half]), (high[:, half:], low[:, half:]))
    return high[:, 0], low[:, 0]


def df_tree_sum(high, low):
    while high.shape[0] > 1:
        if high.shape[0] % 2:
            high = jnp.concatenate([high, jnp.zeros_like(high[:1])])
            low = jnp.concatenate([low, jnp.zeros_like(low[:1])])
        half = high.shape[0] // 2
        high, low = df_add((high[:half], low[:half]), (high[half:], low[half:]))
    return high[0], low[0]


def all_sum_mixed(plain, pairs):
    for axis in ("py", "px"):
        packed = jnp.stack([plain] + [part for pair in pairs for part in pair])
        every = gathered(packed, axis)
        plain = jnp.sum(every[:, 0], axis=0)
        pairs = [df_tree_sum(every[:, 1 + 2 * k], every[:, 2 + 2 * k]) for k in range(len(pairs))]
    return plain, pairs


def permute_side(values, flip):
    shape = values.shape
    pairs = values.reshape(shape[:-1] + (shape[-1] // 2, 2))
    reversed_pairs = jnp.flip(pairs, axis=-2).reshape(shape)
    return jnp.where(flip[:, :, None, None], reversed_pairs, values)


def on_device(
    solution,
    residual,
    direction,
    rz_previous,
    dual_inverse,
    dual_schur,
    coupling,
    coarse_inverse,
    matching,
    patch_counts,
):
    rows_here = solution.shape[0]
    cols_here = solution.shape[1]
    total_rows = rows_here * lax.axis_size("px")
    total_cols = cols_here * lax.axis_size("py")
    grid_row = lax.axis_index("px") * rows_here + jnp.arange(rows_here)
    grid_col = lax.axis_index("py") * cols_here + jnp.arange(cols_here)
    local_slot = jnp.arange(rows_here)[:, None] * cols_here + jnp.arange(cols_here)[None, :]
    count_here = patch_counts[0, 0]
    active = (local_slot < count_here).astype(jnp.float32)[:, :, None, None]
    edge_index = jnp.arange(2 * SIDE)
    edge_ok = jnp.where(
        edge_index[None, None, :] < SIDE,
        (grid_col < total_cols - 1)[None, :, None] & (grid_row >= 0)[:, None, None],
        (grid_row < total_rows - 1)[:, None, None] & (grid_col >= 0)[None, :, None],
    )
    edge_mask = active * edge_ok[:, :, None, :].astype(jnp.float32)
    vertex_mask = ((grid_row >= 1)[:, None] & (grid_col >= 1)[None, :]).astype(jnp.float32)[
        :, :, None, None
    ]
    east_flip = matching[:, :, 0, 0] != 0
    north_flip = matching[:, :, 1, 0] != 0

    def spread_parts(vector):
        east_part = vector[..., :SIDE]
        north_part = vector[..., SIDE:]
        east_perm = permute_side(east_part, east_flip)
        north_perm = permute_side(north_part, north_flip)
        west_edge = passed_along(east_perm, "py", 1)
        from_west = jnp.concatenate([west_edge, east_perm[:, :-1]], 1)
        south_edge = passed_along(north_perm, "px", 1)
        from_south = jnp.concatenate([south_edge, north_perm[:-1]], 0)
        return east_part, north_part, from_west, from_south

    def spread_of(parts):
        east_part, north_part, from_west, from_south = parts
        return jnp.concatenate([east_part, north_part, -from_west, -from_south], 3)

    def jump_b(side_values):
        west_side = side_values[..., 2 * SIDE : 3 * SIDE]
        south_side = side_values[..., 3 * SIDE :]
        east_edge, north_edge = exchanged_together(
            [(west_side, "py", -1), (south_side, "px", -1)]
        )
        from_east = jnp.concatenate([west_side[:, 1:], east_edge], 1)
        from_north = jnp.concatenate([south_side[1:], north_edge], 0)
        east_term = permute_side(from_east, east_flip)
        north_term = permute_side(from_north, north_flip)
        joined = jnp.concatenate(
            [side_values[..., :SIDE] - east_term, side_values[..., SIDE : 2 * SIDE] - north_term], 3
        )
        return joined * edge_mask

    def patch_products(matrices, vectors):
        return (
            jnp.einsum("rpab,rpcb->rpca", matrices, vectors, preferred_element_type=jnp.float32)
            * active
        )

    def spread_pair(first, second):
        east_perm = jnp.stack(
            [permute_side(first[..., :SIDE], east_flip), permute_side(second[..., :SIDE], east_flip)]
        )
        north_perm = jnp.stack(
            [permute_side(first[..., SIDE:], north_flip), permute_side(second[..., SIDE:], north_flip)]
        )
        west_edge = passed_along(east_perm, "py", 1)
        from_west = jnp.concatenate([west_edge, east_perm[:, :, :-1]], 2)
        south_edge = passed_along(north_perm, "px", 1)
        from_south = jnp.concatenate([south_edge, north_perm[:, :-1]], 1)
        return [
            (field[..., :SIDE], field[..., SIDE:], from_west[k], from_south[k])
            for k, field in enumerate((first, second))
        ]

    def jump_and_spread(side_values):
        east_side = side_values[..., :SIDE]
        north_side = side_values[..., SIDE : 2 * SIDE]
        west_side = side_values[..., 2 * SIDE : 3 * SIDE]
        south_side = side_values[..., 3 * SIDE :]
        ones = jnp.broadcast_to(active, east_side.shape)
        east_edge, north_edge = exchanged_together(
            [(west_side, "py", -1), (south_side, "px", -1)]
        )
        from_east = jnp.concatenate([west_side[:, 1:], east_edge], 1)
        from_north = jnp.concatenate([south_side[1:], north_edge], 0)
        east_perm_side = permute_side(east_side, east_flip)
        north_perm_side = permute_side(north_side, north_flip)
        west_sent = passed_along(jnp.stack([east_perm_side, ones]), "py", 1)
        south_sent = passed_along(jnp.stack([north_perm_side, ones]), "px", 1)
        east_term = permute_side(from_east, east_flip)
        north_term = permute_side(from_north, north_flip)
        joined = jnp.concatenate([east_side - east_term, north_side - north_term], 3)
        half_jump = 0.5 * (joined * edge_mask)
        west_edge = 0.5 * ((west_sent[0] - west_side[:, :1]) * west_sent[1])
        south_edge = 0.5 * ((south_sent[0] - south_side[:1]) * south_sent[1])
        local_east = permute_side(half_jump[..., :SIDE], east_flip)
        local_north = permute_side(half_jump[..., SIDE:], north_flip)
        from_west = jnp.concatenate([west_edge, local_east[:, :-1]], 1)
        from_south = jnp.concatenate([south_edge, local_north[:-1]], 0)
        return half_jump, (half_jump[..., :SIDE], half_jump[..., SIDE:], from_west, from_south)

    start_sol = solution * edge_mask
    start_res = residual * edge_mask
    start_dir = direction * edge_mask
    res_parts, dir_parts = spread_pair(0.5 * start_res, start_dir)
    spread = spread_of(res_parts).astype(jnp.bfloat16)
    side_values = patch_products(dual_schur, spread)
    precond, precond_parts = jump_and_spread(side_values)
    rz_current = all_sum(jnp.sum(start_res * precond, axis=(0, 1, 3)))
    step_ratio = rz_current / rz_previous
    ratio = step_ratio[None, None, :, None]
    new_direction = precond + ratio * start_dir
    spread = spread_of(
        tuple(p + ratio * d for p, d in zip(precond_parts, dir_parts))
    ).astype(jnp.bfloat16)
    inner_part = patch_products(dual_inverse, spread)
    corner = (
        jnp.einsum("rpkb,rpcb->rpck", coupling, spread, preferred_element_type=jnp.float32) * active
    )
    corner_width = corner.shape[2] * corner.shape[3]
    payload = jnp.concatenate(
        [
            corner.reshape(rows_here, cols_here, corner_width),
            coarse_inverse.reshape(rows_here, cols_here, 4),
        ],
        2,
    )
    from_west_col, from_east_col = exchanged_together([(payload, "py", 1), (payload, "py", -1)])
    row = jnp.concatenate([from_west_col[:, -1:], payload, from_east_col[:, :1]], 1)
    from_south_row, from_north_row = exchanged_together([(row, "px", 1), (row, "px", -1)])
    block = jnp.concatenate([from_south_row[-1:], row, from_north_row[:1]], 0)
    corners = block[..., :corner_width].reshape(
        rows_here + 2, cols_here + 2, corner.shape[2], corner.shape[3]
    )
    blocks = block[..., corner_width:].reshape(rows_here + 2, cols_here + 2, 2, 2)
    vertex_row = lax.axis_index("px") * rows_here + jnp.arange(rows_here + 1)
    vertex_col = lax.axis_index("py") * cols_here + jnp.arange(cols_here + 1)
    vertex_ok = ((vertex_row >= 1)[:, None] & (vertex_col >= 1)[None, :]).astype(jnp.float32)[
        :, :, None, None
    ]
    assembled = (
        corners[1:, 1:, :, 0:2]
        + corners[1:, :-1, :, 2:4]
        + corners[:-1, 1:, :, 4:6]
        + corners[:-1, :-1, :, 6:8]
    ) * vertex_ok
    coarse = jnp.einsum(
        "rpxy,rpcy->rpcx", blocks[1:, 1:], assembled, precision=lax.Precision.HIGHEST
    )
    corners_back = jnp.concatenate(
        [coarse[:-1, :-1], coarse[:-1, 1:], coarse[1:, :-1], coarse[1:, 1:]], 3
    )
    correction = jnp.einsum(
        "rpkb,rpck->rpcb",
        coupling.astype(jnp.float32),
        corners_back,
        precision=lax.Precision.HIGHEST,
    )
    image = jump_b((inner_part + correction) * active)
    curvature, (res_res, res_img, img_img) = all_sum_mixed(
        jnp.sum(new_direction * image, axis=(0, 1, 3)),
        [df_case_sums(start_res, start_res), df_case_sums(start_res, image), df_case_sums(image, image)],
    )
    step_length = rz_current / curvature
    new_solution = start_sol + step_length[None, None, :, None] * new_direction
    new_residual = start_res - step_length[None, None, :, None] * image
    cross = df_scale(res_img, -2.0 * step_length)
    square = df_scale(df_scale(img_img, step_length), step_length)
    merged = df_add(df_add(res_res, cross), square)
    merged_sq = merged[0] + merged[1]
    scale = res_res[0] + step_length * step_length * img_img[0]
    trusted = jnp.all(jnp.isfinite(scale) & (merged_sq > 0) & (scale <= 1e7 * merged_sq))
    residual_sq = lax.cond(
        trusted,
        lambda: merged_sq,
        lambda: all_sum(jnp.sum(new_residual * new_residual, axis=(0, 1, 3))),
    )
    return (new_solution, new_residual, new_direction, rz_current, residual_sq)


def solution(mesh):
    in_specs = (
        P("px", "py", None, None),
        P("px", "py", None, None),
        P("px", "py", None, None),
        P(),
        P("px", "py", None, None),
        P("px", "py", None, None),
        P("px", "py", None, None),
        P("px", "py", None, None),
        P("px", "py", None, None),
        P("px", "py"),
    )
    out_specs = (
        P("px", "py", None, None),
        P("px", "py", None, None),
        P("px", "py", None, None),
        P(),
        P(),
    )
    return jax.shard_map(
        on_device, mesh=mesh, in_specs=in_specs, out_specs=out_specs, check_vma=False
    )
```

```python
import math

import jax
import jax.numpy as jnp
from jax import lax
from jax.sharding import PartitionSpec as P

SIDE = 68


def passed_along(value, axis, by):
    peers = lax.axis_size(axis)
    pairs = [(i, i + by) for i in range(peers) if 0 <= i + by < peers]
    return lax.ppermute(value, axis, pairs)


def exchanged_together(moves):
    values = lax.optimization_barrier(tuple(value for value, _, _ in moves))
    received = tuple(passed_along(value, axis, by) for value, (_, axis, by) in zip(values, moves))
    return lax.optimization_barrier(received)


INNER = {"py": 2, "px": 4}


def butterfly_rounds(axis):
    peers = lax.axis_size(axis)
    inner = INNER.get(axis, peers)
    if peers % inner or inner & (inner - 1) or (peers // inner) & (peers // inner - 1):
        inner = peers
    rounds = []
    step = 1
    while step < inner:
        rounds.append([(i, i ^ step) for i in range(peers)])
        step *= 2
    outer = peers // inner
    gray = [k ^ (k >> 1) for k in range(outer)]
    place = {g: k for k, g in enumerate(gray)}
    step = 1
    while step < outer:
        rounds.append(
            [(i, place[gray[i // inner] ^ step] * inner + i % inner) for i in range(peers)]
        )
        step *= 2
    return rounds


def gathered(value, axis):
    peers = lax.axis_size(axis) if isinstance(axis, str) else math.prod(lax.axis_size(a) for a in axis)
    copies = jnp.broadcast_to(value[None], (peers,) + value.shape)
    return lax.all_to_all(copies, axis, 0, 0, tiled=False)


def all_sum(value):
    return jnp.sum(gathered(value, ("px", "py")), axis=0)


def two_sum(a, b):
    total = a + b
    back = total - a
    return total, (a - (total - back)) + (b - back)


def split_float(a):
    scaled = 4097.0 * a
    high = scaled - (scaled - a)
    return high, a - high


def two_prod(a, b):
    product = a * b
    a_high, a_low = split_float(a)
    b_high, b_low = split_float(b)
    error = ((a_high * b_high - product) + a_high * b_low + a_low * b_high) + a_low * b_low
    return product, error


def df_add(x, y):
    total, error = two_sum(x[0], y[0])
    error = error + (x[1] + y[1])
    high = total + error
    return high, error - (high - total)


def df_scale(x, factor):
    product, error = two_prod(x[0], factor)
    error = error + x[1] * factor
    high = product + error
    return high, error - (high - product)


def df_case_sums(a, b):
    a = jnp.moveaxis(a, 2, 0).reshape(a.shape[2], -1)
    b = jnp.moveaxis(b, 2, 0).reshape(b.shape[2], -1)
    high, low = two_prod(a, b)
    while high.shape[1] > 1:
        if high.shape[1] % 2:
            high = jnp.pad(high, ((0, 0), (0, 1)))
            low = jnp.pad(low, ((0, 0), (0, 1)))
        half = high.shape[1] // 2
        high, low = df_add((high[:, :half], low[:, :half]), (high[:, half:], low[:, half:]))
    return high[:, 0], low[:, 0]


def df_tree_sum(high, low):
    while high.shape[0] > 1:
        if high.shape[0] % 2:
            high = jnp.concatenate([high, jnp.zeros_like(high[:1])])
            low = jnp.concatenate([low, jnp.zeros_like(low[:1])])
        half = high.shape[0] // 2
        high, low = df_add((high[:half], low[:half]), (high[half:], low[half:]))
    return high[0], low[0]


def all_sum_mixed(plain, pairs):
    packed = jnp.stack([plain] + [part for pair in pairs for part in pair])
    every = gathered(packed, ("px", "py"))
    plain = jnp.sum(every[:, 0], axis=0)
    pairs = [df_tree_sum(every[:, 1 + 2 * k], every[:, 2 + 2 * k]) for k in range(len(pairs))]
    return plain, pairs


def permute_side(values, flip):
    shape = values.shape
    pairs = values.reshape(shape[:-1] + (shape[-1] // 2, 2))
    reversed_pairs = jnp.flip(pairs, axis=-2).reshape(shape)
    return jnp.where(flip[:, :, None, None], reversed_pairs, values)


def on_device(
    solution,
    residual,
    direction,
    rz_previous,
    dual_inverse,
    dual_schur,
    coupling,
    coarse_inverse,
    matching,
    patch_counts,
):
    rows_here = solution.shape[0]
    cols_here = solution.shape[1]
    total_rows = rows_here * lax.axis_size("px")
    total_cols = cols_here * lax.axis_size("py")
    grid_row = lax.axis_index("px") * rows_here + jnp.arange(rows_here)
    grid_col = lax.axis_index("py") * cols_here + jnp.arange(cols_here)
    local_slot = jnp.arange(rows_here)[:, None] * cols_here + jnp.arange(cols_here)[None, :]
    count_here = patch_counts[0, 0]
    active = (local_slot < count_here).astype(jnp.float32)[:, :, None, None]
    edge_index = jnp.arange(2 * SIDE)
    edge_ok = jnp.where(
        edge_index[None, None, :] < SIDE,
        (grid_col < total_cols - 1)[None, :, None] & (grid_row >= 0)[:, None, None],
        (grid_row < total_rows - 1)[:, None, None] & (grid_col >= 0)[None, :, None],
    )
    edge_mask = active * edge_ok[:, :, None, :].astype(jnp.float32)
    vertex_mask = ((grid_row >= 1)[:, None] & (grid_col >= 1)[None, :]).astype(jnp.float32)[
        :, :, None, None
    ]
    east_flip = matching[:, :, 0, 0] != 0
    north_flip = matching[:, :, 1, 0] != 0

    def spread_parts(vector):
        east_part = vector[..., :SIDE]
        north_part = vector[..., SIDE:]
        east_perm = permute_side(east_part, east_flip)
        north_perm = permute_side(north_part, north_flip)
        west_edge = passed_along(east_perm, "py", 1)
        from_west = jnp.concatenate([west_edge, east_perm[:, :-1]], 1)
        south_edge = passed_along(north_perm, "px", 1)
        from_south = jnp.concatenate([south_edge, north_perm[:-1]], 0)
        return east_part, north_part, from_west, from_south

    def spread_of(parts):
        east_part, north_part, from_west, from_south = parts
        return jnp.concatenate([east_part, north_part, -from_west, -from_south], 3)

    def jump_b(side_values):
        west_side = side_values[..., 2 * SIDE : 3 * SIDE]
        south_side = side_values[..., 3 * SIDE :]
        east_edge, north_edge = exchanged_together(
            [(west_side, "py", -1), (south_side, "px", -1)]
        )
        from_east = jnp.concatenate([west_side[:, 1:], east_edge], 1)
        from_north = jnp.concatenate([south_side[1:], north_edge], 0)
        east_term = permute_side(from_east, east_flip)
        north_term = permute_side(from_north, north_flip)
        joined = jnp.concatenate(
            [side_values[..., :SIDE] - east_term, side_values[..., SIDE : 2 * SIDE] - north_term], 3
        )
        return joined * edge_mask

    def patch_products(matrices, vectors):
        return (
            jnp.einsum("rpab,rpcb->rpca", matrices, vectors, preferred_element_type=jnp.float32)
            * active
        )

    def spread_pair(first, second):
        east_perm = jnp.stack(
            [permute_side(first[..., :SIDE], east_flip), permute_side(second[..., :SIDE], east_flip)]
        )
        north_perm = jnp.stack(
            [permute_side(first[..., SIDE:], north_flip), permute_side(second[..., SIDE:], north_flip)]
        )
        west_edge = passed_along(east_perm, "py", 1)
        from_west = jnp.concatenate([west_edge, east_perm[:, :, :-1]], 2)
        south_edge = passed_along(north_perm, "px", 1)
        from_south = jnp.concatenate([south_edge, north_perm[:, :-1]], 1)
        return [
            (field[..., :SIDE], field[..., SIDE:], from_west[k], from_south[k])
            for k, field in enumerate((first, second))
        ]

    def jump_and_spread(side_values):
        east_side = side_values[..., :SIDE]
        north_side = side_values[..., SIDE : 2 * SIDE]
        west_side = side_values[..., 2 * SIDE : 3 * SIDE]
        south_side = side_values[..., 3 * SIDE :]
        ones = jnp.broadcast_to(active, east_side.shape)
        east_edge, north_edge = exchanged_together(
            [(west_side, "py", -1), (south_side, "px", -1)]
        )
        from_east = jnp.concatenate([west_side[:, 1:], east_edge], 1)
        from_north = jnp.concatenate([south_side[1:], north_edge], 0)
        east_perm_side = permute_side(east_side, east_flip)
        north_perm_side = permute_side(north_side, north_flip)
        west_sent = passed_along(jnp.stack([east_perm_side, ones]), "py", 1)
        south_sent = passed_along(jnp.stack([north_perm_side, ones]), "px", 1)
        east_term = permute_side(from_east, east_flip)
        north_term = permute_side(from_north, north_flip)
        joined = jnp.concatenate([east_side - east_term, north_side - north_term], 3)
        half_jump = 0.5 * (joined * edge_mask)
        west_edge = 0.5 * ((west_sent[0] - west_side[:, :1]) * west_sent[1])
        south_edge = 0.5 * ((south_sent[0] - south_side[:1]) * south_sent[1])
        local_east = permute_side(half_jump[..., :SIDE], east_flip)
        local_north = permute_side(half_jump[..., SIDE:], north_flip)
        from_west = jnp.concatenate([west_edge, local_east[:, :-1]], 1)
        from_south = jnp.concatenate([south_edge, local_north[:-1]], 0)
        return half_jump, (half_jump[..., :SIDE], half_jump[..., SIDE:], from_west, from_south)

    start_sol = solution * edge_mask
    start_res = residual * edge_mask
    start_dir = direction * edge_mask
    res_parts, dir_parts = spread_pair(0.5 * start_res, start_dir)
    spread = spread_of(res_parts).astype(jnp.bfloat16)
    side_values = patch_products(dual_schur, spread)
    precond, precond_parts = jump_and_spread(side_values)
    rz_current = all_sum(jnp.sum(start_res * precond, axis=(0, 1, 3)))
    step_ratio = rz_current / rz_previous
    ratio = step_ratio[None, None, :, None]
    new_direction = precond + ratio * start_dir
    spread = spread_of(
        tuple(p + ratio * d for p, d in zip(precond_parts, dir_parts))
    ).astype(jnp.bfloat16)
    inner_part = patch_products(dual_inverse, spread)
    corner = (
        jnp.einsum("rpkb,rpcb->rpck", coupling, spread, preferred_element_type=jnp.float32) * active
    )
    corner_width = corner.shape[2] * corner.shape[3]
    payload = jnp.concatenate(
        [
            corner.reshape(rows_here, cols_here, corner_width),
            coarse_inverse.reshape(rows_here, cols_here, 4),
        ],
        2,
    )
    from_west_col, from_east_col = exchanged_together([(payload, "py", 1), (payload, "py", -1)])
    row = jnp.concatenate([from_west_col[:, -1:], payload, from_east_col[:, :1]], 1)
    from_south_row, from_north_row = exchanged_together([(row, "px", 1), (row, "px", -1)])
    block = jnp.concatenate([from_south_row[-1:], row, from_north_row[:1]], 0)
    corners = block[..., :corner_width].reshape(
        rows_here + 2, cols_here + 2, corner.shape[2], corner.shape[3]
    )
    blocks = block[..., corner_width:].reshape(rows_here + 2, cols_here + 2, 2, 2)
    vertex_row = lax.axis_index("px") * rows_here + jnp.arange(rows_here + 1)
    vertex_col = lax.axis_index("py") * cols_here + jnp.arange(cols_here + 1)
    vertex_ok = ((vertex_row >= 1)[:, None] & (vertex_col >= 1)[None, :]).astype(jnp.float32)[
        :, :, None, None
    ]
    assembled = (
        corners[1:, 1:, :, 0:2]
        + corners[1:, :-1, :, 2:4]
        + corners[:-1, 1:, :, 4:6]
        + corners[:-1, :-1, :, 6:8]
    ) * vertex_ok
    coarse = jnp.einsum(
        "rpxy,rpcy->rpcx", blocks[1:, 1:], assembled, precision=lax.Precision.HIGHEST
    )
    corners_back = jnp.concatenate(
        [coarse[:-1, :-1], coarse[:-1, 1:], coarse[1:, :-1], coarse[1:, 1:]], 3
    )
    correction = jnp.einsum(
        "rpkb,rpck->rpcb",
        coupling.astype(jnp.float32),
        corners_back,
        precision=lax.Precision.HIGHEST,
    )
    image = jump_b((inner_part + correction) * active)
    curvature, (res_res, res_img, img_img) = all_sum_mixed(
        jnp.sum(new_direction * image, axis=(0, 1, 3)),
        [df_case_sums(start_res, start_res), df_case_sums(start_res, image), df_case_sums(image, image)],
    )
    step_length = rz_current / curvature
    new_solution = start_sol + step_length[None, None, :, None] * new_direction
    new_residual = start_res - step_length[None, None, :, None] * image
    cross = df_scale(res_img, -2.0 * step_length)
    square = df_scale(df_scale(img_img, step_length), step_length)
    merged = df_add(df_add(res_res, cross), square)
    merged_sq = merged[0] + merged[1]
    scale = res_res[0] + step_length * step_length * img_img[0]
    trusted = jnp.all(jnp.isfinite(scale) & (merged_sq > 0) & (scale <= 1e7 * merged_sq))
    residual_sq = lax.cond(
        trusted,
        lambda: merged_sq,
        lambda: all_sum(jnp.sum(new_residual * new_residual, axis=(0, 1, 3))),
    )
    return (new_solution, new_residual, new_direction, rz_current, residual_sq)


def solution(mesh):
    in_specs = (
        P("px", "py", None, None),
        P("px", "py", None, None),
        P("px", "py", None, None),
        P(),
        P("px", "py", None, None),
        P("px", "py", None, None),
        P("px", "py", None, None),
        P("px", "py", None, None),
        P("px", "py", None, None),
        P("px", "py"),
    )
    out_specs = (
        P("px", "py", None, None),
        P("px", "py", None, None),
        P("px", "py", None, None),
        P(),
        P(),
    )
    return jax.shard_map(
        on_device, mesh=mesh, in_specs=in_specs, out_specs=out_specs, check_vma=False
    )
```

```python
import jax
import jax.numpy as jnp
from jax import lax
from jax.sharding import PartitionSpec as P

SIDE = 68


def passed_along(value, axis, by):
    peers = lax.axis_size(axis)
    pairs = [(i, i + by) for i in range(peers) if 0 <= i + by < peers]
    return lax.ppermute(value, axis, pairs)


def exchanged_together(moves):
    values = lax.optimization_barrier(tuple(value for value, _, _ in moves))
    received = tuple(passed_along(value, axis, by) for value, (_, axis, by) in zip(values, moves))
    return lax.optimization_barrier(received)


INNER = {"py": 2, "px": 4}


def butterfly_rounds(axis):
    peers = lax.axis_size(axis)
    inner = INNER.get(axis, peers)
    if peers % inner or inner & (inner - 1) or (peers // inner) & (peers // inner - 1):
        inner = peers
    rounds = []
    step = 1
    while step < inner:
        rounds.append([(i, i ^ step) for i in range(peers)])
        step *= 2
    outer = peers // inner
    gray = [k ^ (k >> 1) for k in range(outer)]
    place = {g: k for k, g in enumerate(gray)}
    step = 1
    while step < outer:
        rounds.append(
            [(i, place[gray[i // inner] ^ step] * inner + i % inner) for i in range(peers)]
        )
        step *= 2
    return rounds


def gathered(value, axis):
    peers = lax.axis_size(axis)
    copies = jnp.broadcast_to(value[None], (peers,) + value.shape)
    return lax.all_to_all(copies, axis, 0, 0, tiled=False)


def all_sum(value):
    for axis in ("py", "px"):
        value = jnp.sum(gathered(value, axis), axis=0)
    return value


def two_sum(a, b):
    total = a + b
    back = total - a
    return total, (a - (total - back)) + (b - back)


def split_float(a):
    scaled = 4097.0 * a
    high = scaled - (scaled - a)
    return high, a - high


def two_prod(a, b):
    product = a * b
    a_high, a_low = split_float(a)
    b_high, b_low = split_float(b)
    error = ((a_high * b_high - product) + a_high * b_low + a_low * b_high) + a_low * b_low
    return product, error


def df_add(x, y):
    total, error = two_sum(x[0], y[0])
    error = error + (x[1] + y[1])
    high = total + error
    return high, error - (high - total)


def df_scale(x, factor):
    product, error = two_prod(x[0], factor)
    error = error + x[1] * factor
    high = product + error
    return high, error - (high - product)


def df_case_sums(a, b):
    a = jnp.moveaxis(a, 2, 0).reshape(a.shape[2], -1)
    b = jnp.moveaxis(b, 2, 0).reshape(b.shape[2], -1)
    high, low = two_prod(a, b)
    while high.shape[1] > 1:
        if high.shape[1] % 2:
            high = jnp.pad(high, ((0, 0), (0, 1)))
            low = jnp.pad(low, ((0, 0), (0, 1)))
        half = high.shape[1] // 2
        high, low = df_add((high[:, :half], low[:, :half]), (high[:, half:], low[:, half:]))
    return high[:, 0], low[:, 0]


def df_tree_sum(high, low):
    while high.shape[0] > 1:
        if high.shape[0] % 2:
            high = jnp.concatenate([high, jnp.zeros_like(high[:1])])
            low = jnp.concatenate([low, jnp.zeros_like(low[:1])])
        half = high.shape[0] // 2
        high, low = df_add((high[:half], low[:half]), (high[half:], low[half:]))
    return high[0], low[0]


def all_sum_mixed(plain, pairs):
    for axis in ("py", "px"):
        packed = jnp.stack([plain] + [part for pair in pairs for part in pair])
        every = gathered(packed, axis)
        plain = jnp.sum(every[:, 0], axis=0)
        pairs = [df_tree_sum(every[:, 1 + 2 * k], every[:, 2 + 2 * k]) for k in range(len(pairs))]
    return plain, pairs


def permute_side(values, flip):
    shape = values.shape
    pairs = values.reshape(shape[:-1] + (shape[-1] // 2, 2))
    reversed_pairs = jnp.flip(pairs, axis=-2).reshape(shape)
    return jnp.where(flip[:, :, None, None], reversed_pairs, values)


def on_device(
    solution,
    residual,
    direction,
    rz_previous,
    dual_inverse,
    dual_schur,
    coupling,
    coarse_inverse,
    matching,
    patch_counts,
):
    rows_here = solution.shape[0]
    cols_here = solution.shape[1]
    total_rows = rows_here * lax.axis_size("px")
    total_cols = cols_here * lax.axis_size("py")
    grid_row = lax.axis_index("px") * rows_here + jnp.arange(rows_here)
    grid_col = lax.axis_index("py") * cols_here + jnp.arange(cols_here)
    local_slot = jnp.arange(rows_here)[:, None] * cols_here + jnp.arange(cols_here)[None, :]
    count_here = patch_counts[0, 0]
    active = (local_slot < count_here).astype(jnp.float32)[:, :, None, None]
    edge_index = jnp.arange(2 * SIDE)
    edge_ok = jnp.where(
        edge_index[None, None, :] < SIDE,
        (grid_col < total_cols - 1)[None, :, None] & (grid_row >= 0)[:, None, None],
        (grid_row < total_rows - 1)[:, None, None] & (grid_col >= 0)[None, :, None],
    )
    edge_mask = active * edge_ok[:, :, None, :].astype(jnp.float32)
    vertex_mask = ((grid_row >= 1)[:, None] & (grid_col >= 1)[None, :]).astype(jnp.float32)[
        :, :, None, None
    ]
    east_flip = matching[:, :, 0, 0] != 0
    north_flip = matching[:, :, 1, 0] != 0

    def spread_parts(vector):
        east_part = vector[..., :SIDE]
        north_part = vector[..., SIDE:]
        east_perm = permute_side(east_part, east_flip)
        north_perm = permute_side(north_part, north_flip)
        west_edge = passed_along(east_perm, "py", 1)
        from_west = jnp.concatenate([west_edge, east_perm[:, :-1]], 1)
        south_edge = passed_along(north_perm, "px", 1)
        from_south = jnp.concatenate([south_edge, north_perm[:-1]], 0)
        return east_part, north_part, from_west, from_south

    def spread_of(parts):
        east_part, north_part, from_west, from_south = parts
        return jnp.concatenate([east_part, north_part, -from_west, -from_south], 3)

    def jump_b(side_values):
        west_side = side_values[..., 2 * SIDE : 3 * SIDE]
        south_side = side_values[..., 3 * SIDE :]
        east_edge, north_edge = exchanged_together(
            [(west_side, "py", -1), (south_side, "px", -1)]
        )
        from_east = jnp.concatenate([west_side[:, 1:], east_edge], 1)
        from_north = jnp.concatenate([south_side[1:], north_edge], 0)
        east_term = permute_side(from_east, east_flip)
        north_term = permute_side(from_north, north_flip)
        joined = jnp.concatenate(
            [side_values[..., :SIDE] - east_term, side_values[..., SIDE : 2 * SIDE] - north_term], 3
        )
        return joined * edge_mask

    def patch_products(matrices, vectors):
        return (
            jnp.einsum("rpab,rpcb->rpca", matrices, vectors, preferred_element_type=jnp.float32)
            * active
        )

    def spread_pair(first, second):
        east_perm = jnp.stack(
            [permute_side(first[..., :SIDE], east_flip), permute_side(second[..., :SIDE], east_flip)]
        )
        north_perm = jnp.stack(
            [permute_side(first[..., SIDE:], north_flip), permute_side(second[..., SIDE:], north_flip)]
        )
        west_edge = passed_along(east_perm, "py", 1)
        from_west = jnp.concatenate([west_edge, east_perm[:, :, :-1]], 2)
        south_edge = passed_along(north_perm, "px", 1)
        from_south = jnp.concatenate([south_edge, north_perm[:, :-1]], 1)
        return [
            (field[..., :SIDE], field[..., SIDE:], from_west[k], from_south[k])
            for k, field in enumerate((first, second))
        ]

    def jump_and_spread(side_values):
        east_side = side_values[..., :SIDE]
        north_side = side_values[..., SIDE : 2 * SIDE]
        west_side = side_values[..., 2 * SIDE : 3 * SIDE]
        south_side = side_values[..., 3 * SIDE :]
        ones = jnp.broadcast_to(active, east_side.shape)
        east_perm_side = permute_side(east_side, east_flip)
        north_perm_side = permute_side(north_side, north_flip)
        east_edge, north_edge, west_sent, south_sent = exchanged_together(
            [
                (west_side, "py", -1),
                (south_side, "px", -1),
                (jnp.stack([east_perm_side, ones]), "py", 1),
                (jnp.stack([north_perm_side, ones]), "px", 1),
            ]
        )
        from_east = jnp.concatenate([west_side[:, 1:], east_edge], 1)
        from_north = jnp.concatenate([south_side[1:], north_edge], 0)
        east_term = permute_side(from_east, east_flip)
        north_term = permute_side(from_north, north_flip)
        joined = jnp.concatenate([east_side - east_term, north_side - north_term], 3)
        half_jump = 0.5 * (joined * edge_mask)
        west_edge = 0.5 * ((west_sent[0] - west_side[:, :1]) * west_sent[1])
        south_edge = 0.5 * ((south_sent[0] - south_side[:1]) * south_sent[1])
        local_east = permute_side(half_jump[..., :SIDE], east_flip)
        local_north = permute_side(half_jump[..., SIDE:], north_flip)
        from_west = jnp.concatenate([west_edge, local_east[:, :-1]], 1)
        from_south = jnp.concatenate([south_edge, local_north[:-1]], 0)
        return half_jump, (half_jump[..., :SIDE], half_jump[..., SIDE:], from_west, from_south)

    start_sol = solution * edge_mask
    start_res = residual * edge_mask
    start_dir = direction * edge_mask
    res_parts, dir_parts = spread_pair(0.5 * start_res, start_dir)
    spread = spread_of(res_parts).astype(jnp.bfloat16)
    side_values = patch_products(dual_schur, spread)
    precond, precond_parts = jump_and_spread(side_values)
    rz_current = all_sum(jnp.sum(start_res * precond, axis=(0, 1, 3)))
    step_ratio = rz_current / rz_previous
    ratio = step_ratio[None, None, :, None]
    new_direction = precond + ratio * start_dir
    spread = spread_of(
        tuple(p + ratio * d for p, d in zip(precond_parts, dir_parts))
    ).astype(jnp.bfloat16)
    inner_part = patch_products(dual_inverse, spread)
    corner = (
        jnp.einsum("rpkb,rpcb->rpck", coupling, spread, preferred_element_type=jnp.float32) * active
    )
    corner_width = corner.shape[2] * corner.shape[3]
    payload = jnp.concatenate(
        [
            corner.reshape(rows_here, cols_here, corner_width),
            coarse_inverse.reshape(rows_here, cols_here, 4),
        ],
        2,
    )
    from_west_col, from_east_col = exchanged_together([(payload, "py", 1), (payload, "py", -1)])
    row = jnp.concatenate([from_west_col[:, -1:], payload, from_east_col[:, :1]], 1)
    from_south_row, from_north_row = exchanged_together([(row, "px", 1), (row, "px", -1)])
    block = jnp.concatenate([from_south_row[-1:], row, from_north_row[:1]], 0)
    corners = block[..., :corner_width].reshape(
        rows_here + 2, cols_here + 2, corner.shape[2], corner.shape[3]
    )
    blocks = block[..., corner_width:].reshape(rows_here + 2, cols_here + 2, 2, 2)
    vertex_row = lax.axis_index("px") * rows_here + jnp.arange(rows_here + 1)
    vertex_col = lax.axis_index("py") * cols_here + jnp.arange(cols_here + 1)
    vertex_ok = ((vertex_row >= 1)[:, None] & (vertex_col >= 1)[None, :]).astype(jnp.float32)[
        :, :, None, None
    ]
    assembled = (
        corners[1:, 1:, :, 0:2]
        + corners[1:, :-1, :, 2:4]
        + corners[:-1, 1:, :, 4:6]
        + corners[:-1, :-1, :, 6:8]
    ) * vertex_ok
    coarse = jnp.einsum(
        "rpxy,rpcy->rpcx", blocks[1:, 1:], assembled, precision=lax.Precision.HIGHEST
    )
    corners_back = jnp.concatenate(
        [coarse[:-1, :-1], coarse[:-1, 1:], coarse[1:, :-1], coarse[1:, 1:]], 3
    )
    correction = jnp.einsum(
        "rpkb,rpck->rpcb",
        coupling.astype(jnp.float32),
        corners_back,
        precision=lax.Precision.HIGHEST,
    )
    image = jump_b((inner_part + correction) * active)
    curvature, (res_res, res_img, img_img) = all_sum_mixed(
        jnp.sum(new_direction * image, axis=(0, 1, 3)),
        [df_case_sums(start_res, start_res), df_case_sums(start_res, image), df_case_sums(image, image)],
    )
    step_length = rz_current / curvature
    new_solution = start_sol + step_length[None, None, :, None] * new_direction
    new_residual = start_res - step_length[None, None, :, None] * image
    cross = df_scale(res_img, -2.0 * step_length)
    square = df_scale(df_scale(img_img, step_length), step_length)
    merged = df_add(df_add(res_res, cross), square)
    merged_sq = merged[0] + merged[1]
    scale = res_res[0] + step_length * step_length * img_img[0]
    trusted = jnp.all(jnp.isfinite(scale) & (merged_sq > 0) & (scale <= 1e7 * merged_sq))
    residual_sq = lax.cond(
        trusted,
        lambda: merged_sq,
        lambda: all_sum(jnp.sum(new_residual * new_residual, axis=(0, 1, 3))),
    )
    return (new_solution, new_residual, new_direction, rz_current, residual_sq)


def solution(mesh):
    in_specs = (
        P("px", "py", None, None),
        P("px", "py", None, None),
        P("px", "py", None, None),
        P(),
        P("px", "py", None, None),
        P("px", "py", None, None),
        P("px", "py", None, None),
        P("px", "py", None, None),
        P("px", "py", None, None),
        P("px", "py"),
    )
    out_specs = (
        P("px", "py", None, None),
        P("px", "py", None, None),
        P("px", "py", None, None),
        P(),
        P(),
    )
    return jax.shard_map(
        on_device, mesh=mesh, in_specs=in_specs, out_specs=out_specs, check_vma=False
    )
```

```python
import jax
import jax.numpy as jnp
from jax import lax
from jax.sharding import PartitionSpec as P

SIDE = 68


def passed_along(value, axis, by):
    peers = lax.axis_size(axis)
    pairs = [(i, i + by) for i in range(peers) if 0 <= i + by < peers]
    return lax.ppermute(value, axis, pairs)


def exchanged_together(moves):
    values = lax.optimization_barrier(tuple(value for value, _, _ in moves))
    received = tuple(passed_along(value, axis, by) for value, (_, axis, by) in zip(values, moves))
    return lax.optimization_barrier(received)


INNER = {"py": 2, "px": 4}


def butterfly_rounds(axis):
    peers = lax.axis_size(axis)
    inner = INNER.get(axis, peers)
    if peers % inner or inner & (inner - 1) or (peers // inner) & (peers // inner - 1):
        inner = peers
    rounds = []
    step = 1
    while step < inner:
        rounds.append([(i, i ^ step) for i in range(peers)])
        step *= 2
    outer = peers // inner
    gray = [k ^ (k >> 1) for k in range(outer)]
    place = {g: k for k, g in enumerate(gray)}
    step = 1
    while step < outer:
        rounds.append(
            [(i, place[gray[i // inner] ^ step] * inner + i % inner) for i in range(peers)]
        )
        step *= 2
    return rounds


def gathered(value, axis):
    peers = lax.axis_size(axis)
    copies = jnp.broadcast_to(value[None], (peers,) + value.shape)
    return lax.all_to_all(copies, axis, 0, 0, tiled=False)


def all_sum(value):
    for axis in ("py", "px"):
        value = jnp.sum(gathered(value, axis), axis=0)
    return value


def two_sum(a, b):
    total = a + b
    back = total - a
    return total, (a - (total - back)) + (b - back)


def split_float(a):
    scaled = 4097.0 * a
    high = scaled - (scaled - a)
    return high, a - high


def two_prod(a, b):
    product = a * b
    a_high, a_low = split_float(a)
    b_high, b_low = split_float(b)
    error = ((a_high * b_high - product) + a_high * b_low + a_low * b_high) + a_low * b_low
    return product, error


def df_add(x, y):
    total, error = two_sum(x[0], y[0])
    error = error + (x[1] + y[1])
    high = total + error
    return high, error - (high - total)


def df_scale(x, factor):
    product, error = two_prod(x[0], factor)
    error = error + x[1] * factor
    high = product + error
    return high, error - (high - product)


def df_case_sums(a, b):
    a = jnp.moveaxis(a, 2, 0).reshape(a.shape[2], -1)
    b = jnp.moveaxis(b, 2, 0).reshape(b.shape[2], -1)
    high, low = two_prod(a, b)
    while high.shape[1] > 1:
        if high.shape[1] % 2:
            high = jnp.pad(high, ((0, 0), (0, 1)))
            low = jnp.pad(low, ((0, 0), (0, 1)))
        half = high.shape[1] // 2
        high, low = df_add((high[:, :half], low[:, :half]), (high[:, half:], low[:, half:]))
    return high[:, 0], low[:, 0]


def df_tree_sum(high, low):
    while high.shape[0] > 1:
        if high.shape[0] % 2:
            high = jnp.concatenate([high, jnp.zeros_like(high[:1])])
            low = jnp.concatenate([low, jnp.zeros_like(low[:1])])
        half = high.shape[0] // 2
        high, low = df_add((high[:half], low[:half]), (high[half:], low[half:]))
    return high[0], low[0]


def all_sum_mixed(plain, pairs):
    for axis in ("py", "px"):
        rows = [plain] + [part for pair in pairs for part in pair]
        width = plain.shape[0]
        every = gathered(jnp.concatenate(rows), axis)
        row = lambda k: every[:, k * width : (k + 1) * width]
        plain = jnp.sum(row(0), axis=0)
        pairs = [df_tree_sum(row(1 + 2 * k), row(2 + 2 * k)) for k in range(len(pairs))]
    return plain, pairs


def permute_side(values, flip):
    shape = values.shape
    pairs = values.reshape(shape[:-1] + (shape[-1] // 2, 2))
    reversed_pairs = jnp.flip(pairs, axis=-2).reshape(shape)
    return jnp.where(flip[:, :, None, None], reversed_pairs, values)


def on_device(
    solution,
    residual,
    direction,
    rz_previous,
    dual_inverse,
    dual_schur,
    coupling,
    coarse_inverse,
    matching,
    patch_counts,
):
    rows_here = solution.shape[0]
    cols_here = solution.shape[1]
    total_rows = rows_here * lax.axis_size("px")
    total_cols = cols_here * lax.axis_size("py")
    grid_row = lax.axis_index("px") * rows_here + jnp.arange(rows_here)
    grid_col = lax.axis_index("py") * cols_here + jnp.arange(cols_here)
    local_slot = jnp.arange(rows_here)[:, None] * cols_here + jnp.arange(cols_here)[None, :]
    count_here = patch_counts[0, 0]
    active = (local_slot < count_here).astype(jnp.float32)[:, :, None, None]
    edge_index = jnp.arange(2 * SIDE)
    edge_ok = jnp.where(
        edge_index[None, None, :] < SIDE,
        (grid_col < total_cols - 1)[None, :, None] & (grid_row >= 0)[:, None, None],
        (grid_row < total_rows - 1)[:, None, None] & (grid_col >= 0)[None, :, None],
    )
    edge_mask = active * edge_ok[:, :, None, :].astype(jnp.float32)
    vertex_mask = ((grid_row >= 1)[:, None] & (grid_col >= 1)[None, :]).astype(jnp.float32)[
        :, :, None, None
    ]
    east_flip = matching[:, :, 0, 0] != 0
    north_flip = matching[:, :, 1, 0] != 0

    def spread_parts(vector):
        east_part = vector[..., :SIDE]
        north_part = vector[..., SIDE:]
        east_perm = permute_side(east_part, east_flip)
        north_perm = permute_side(north_part, north_flip)
        west_edge = passed_along(east_perm, "py", 1)
        from_west = jnp.concatenate([west_edge, east_perm[:, :-1]], 1)
        south_edge = passed_along(north_perm, "px", 1)
        from_south = jnp.concatenate([south_edge, north_perm[:-1]], 0)
        return east_part, north_part, from_west, from_south

    def spread_of(parts):
        east_part, north_part, from_west, from_south = parts
        return jnp.concatenate([east_part, north_part, -from_west, -from_south], 3)

    def jump_b(side_values):
        west_side = side_values[..., 2 * SIDE : 3 * SIDE]
        south_side = side_values[..., 3 * SIDE :]
        east_edge, north_edge = exchanged_together(
            [(west_side, "py", -1), (south_side, "px", -1)]
        )
        from_east = jnp.concatenate([west_side[:, 1:], east_edge], 1)
        from_north = jnp.concatenate([south_side[1:], north_edge], 0)
        east_term = permute_side(from_east, east_flip)
        north_term = permute_side(from_north, north_flip)
        joined = jnp.concatenate(
            [side_values[..., :SIDE] - east_term, side_values[..., SIDE : 2 * SIDE] - north_term], 3
        )
        return joined * edge_mask

    def patch_products(matrices, vectors):
        return (
            jnp.einsum("rpab,rpcb->rpca", matrices, vectors, preferred_element_type=jnp.float32)
            * active
        )

    def spread_pair(first, second):
        east_perm = jnp.stack(
            [permute_side(first[..., :SIDE], east_flip), permute_side(second[..., :SIDE], east_flip)]
        )
        north_perm = jnp.stack(
            [permute_side(first[..., SIDE:], north_flip), permute_side(second[..., SIDE:], north_flip)]
        )
        west_edge = passed_along(east_perm, "py", 1)
        from_west = jnp.concatenate([west_edge, east_perm[:, :, :-1]], 2)
        south_edge = passed_along(north_perm, "px", 1)
        from_south = jnp.concatenate([south_edge, north_perm[:, :-1]], 1)
        return [
            (field[..., :SIDE], field[..., SIDE:], from_west[k], from_south[k])
            for k, field in enumerate((first, second))
        ]

    def jump_and_spread(side_values):
        east_side = side_values[..., :SIDE]
        north_side = side_values[..., SIDE : 2 * SIDE]
        west_side = side_values[..., 2 * SIDE : 3 * SIDE]
        south_side = side_values[..., 3 * SIDE :]
        ones = jnp.broadcast_to(active, east_side.shape)
        east_edge, north_edge = exchanged_together(
            [(west_side, "py", -1), (south_side, "px", -1)]
        )
        from_east = jnp.concatenate([west_side[:, 1:], east_edge], 1)
        from_north = jnp.concatenate([south_side[1:], north_edge], 0)
        east_perm_side = permute_side(east_side, east_flip)
        north_perm_side = permute_side(north_side, north_flip)
        west_sent = passed_along(jnp.stack([east_perm_side, ones]), "py", 1)
        south_sent = passed_along(jnp.stack([north_perm_side, ones]), "px", 1)
        east_term = permute_side(from_east, east_flip)
        north_term = permute_side(from_north, north_flip)
        joined = jnp.concatenate([east_side - east_term, north_side - north_term], 3)
        half_jump = 0.5 * (joined * edge_mask)
        west_edge = 0.5 * ((west_sent[0] - west_side[:, :1]) * west_sent[1])
        south_edge = 0.5 * ((south_sent[0] - south_side[:1]) * south_sent[1])
        local_east = permute_side(half_jump[..., :SIDE], east_flip)
        local_north = permute_side(half_jump[..., SIDE:], north_flip)
        from_west = jnp.concatenate([west_edge, local_east[:, :-1]], 1)
        from_south = jnp.concatenate([south_edge, local_north[:-1]], 0)
        return half_jump, (half_jump[..., :SIDE], half_jump[..., SIDE:], from_west, from_south)

    start_sol = solution * edge_mask
    start_res = residual * edge_mask
    start_dir = direction * edge_mask
    res_parts, dir_parts = spread_pair(0.5 * start_res, start_dir)
    spread = spread_of(res_parts).astype(jnp.bfloat16)
    side_values = patch_products(dual_schur, spread)
    precond, precond_parts = jump_and_spread(side_values)
    rz_current = all_sum(jnp.sum(start_res * precond, axis=(0, 1, 3)))
    step_ratio = rz_current / rz_previous
    ratio = step_ratio[None, None, :, None]
    new_direction = precond + ratio * start_dir
    spread = spread_of(
        tuple(p + ratio * d for p, d in zip(precond_parts, dir_parts))
    ).astype(jnp.bfloat16)
    inner_part = patch_products(dual_inverse, spread)
    corner = (
        jnp.einsum("rpkb,rpcb->rpck", coupling, spread, preferred_element_type=jnp.float32) * active
    )
    corner_width = corner.shape[2] * corner.shape[3]
    payload = jnp.concatenate(
        [
            corner.reshape(rows_here, cols_here, corner_width),
            coarse_inverse.reshape(rows_here, cols_here, 4),
        ],
        2,
    )
    from_west_col, from_east_col = exchanged_together([(payload, "py", 1), (payload, "py", -1)])
    row = jnp.concatenate([from_west_col[:, -1:], payload, from_east_col[:, :1]], 1)
    from_south_row, from_north_row = exchanged_together([(row, "px", 1), (row, "px", -1)])
    block = jnp.concatenate([from_south_row[-1:], row, from_north_row[:1]], 0)
    corners = block[..., :corner_width].reshape(
        rows_here + 2, cols_here + 2, corner.shape[2], corner.shape[3]
    )
    blocks = block[..., corner_width:].reshape(rows_here + 2, cols_here + 2, 2, 2)
    vertex_row = lax.axis_index("px") * rows_here + jnp.arange(rows_here + 1)
    vertex_col = lax.axis_index("py") * cols_here + jnp.arange(cols_here + 1)
    vertex_ok = ((vertex_row >= 1)[:, None] & (vertex_col >= 1)[None, :]).astype(jnp.float32)[
        :, :, None, None
    ]
    assembled = (
        corners[1:, 1:, :, 0:2]
        + corners[1:, :-1, :, 2:4]
        + corners[:-1, 1:, :, 4:6]
        + corners[:-1, :-1, :, 6:8]
    ) * vertex_ok
    coarse = jnp.einsum(
        "rpxy,rpcy->rpcx", blocks[1:, 1:], assembled, precision=lax.Precision.HIGHEST
    )
    corners_back = jnp.concatenate(
        [coarse[:-1, :-1], coarse[:-1, 1:], coarse[1:, :-1], coarse[1:, 1:]], 3
    )
    correction = jnp.einsum(
        "rpkb,rpck->rpcb",
        coupling.astype(jnp.float32),
        corners_back,
        precision=lax.Precision.HIGHEST,
    )
    image = jump_b((inner_part + correction) * active)
    curvature, (res_res, res_img, img_img) = all_sum_mixed(
        jnp.sum(new_direction * image, axis=(0, 1, 3)),
        [df_case_sums(start_res, start_res), df_case_sums(start_res, image), df_case_sums(image, image)],
    )
    step_length = rz_current / curvature
    new_solution = start_sol + step_length[None, None, :, None] * new_direction
    new_residual = start_res - step_length[None, None, :, None] * image
    cross = df_scale(res_img, -2.0 * step_length)
    square = df_scale(df_scale(img_img, step_length), step_length)
    merged = df_add(df_add(res_res, cross), square)
    merged_sq = merged[0] + merged[1]
    scale = res_res[0] + step_length * step_length * img_img[0]
    trusted = jnp.all(jnp.isfinite(scale) & (merged_sq > 0) & (scale <= 1e7 * merged_sq))
    residual_sq = lax.cond(
        trusted,
        lambda: merged_sq,
        lambda: all_sum(jnp.sum(new_residual * new_residual, axis=(0, 1, 3))),
    )
    return (new_solution, new_residual, new_direction, rz_current, residual_sq)


def solution(mesh):
    in_specs = (
        P("px", "py", None, None),
        P("px", "py", None, None),
        P("px", "py", None, None),
        P(),
        P("px", "py", None, None),
        P("px", "py", None, None),
        P("px", "py", None, None),
        P("px", "py", None, None),
        P("px", "py", None, None),
        P("px", "py"),
    )
    out_specs = (
        P("px", "py", None, None),
        P("px", "py", None, None),
        P("px", "py", None, None),
        P(),
        P(),
    )
    return jax.shard_map(
        on_device, mesh=mesh, in_specs=in_specs, out_specs=out_specs, check_vma=False
    )
```

```python
import jax
import jax.numpy as jnp
from jax import lax
from jax.sharding import PartitionSpec as P

SIDE = 68


def passed_along(value, axis, by):
    peers = lax.axis_size(axis)
    pairs = [(i, i + by) for i in range(peers) if 0 <= i + by < peers]
    return lax.ppermute(value, axis, pairs)


def exchanged_together(moves):
    values = lax.optimization_barrier(tuple(value for value, _, _ in moves))
    received = tuple(passed_along(value, axis, by) for value, (_, axis, by) in zip(values, moves))
    return lax.optimization_barrier(received)


INNER = {"py": 2, "px": 4}


def butterfly_rounds(axis):
    peers = lax.axis_size(axis)
    inner = INNER.get(axis, peers)
    if peers % inner or inner & (inner - 1) or (peers // inner) & (peers // inner - 1):
        inner = peers
    rounds = []
    step = 1
    while step < inner:
        rounds.append([(i, i ^ step) for i in range(peers)])
        step *= 2
    outer = peers // inner
    gray = [k ^ (k >> 1) for k in range(outer)]
    place = {g: k for k, g in enumerate(gray)}
    step = 1
    while step < outer:
        rounds.append(
            [(i, place[gray[i // inner] ^ step] * inner + i % inner) for i in range(peers)]
        )
        step *= 2
    return rounds


def gathered(value, axis):
    peers = lax.axis_size(axis)
    copies = jnp.broadcast_to(value[None], (peers,) + value.shape)
    return lax.all_to_all(copies, axis, 0, 0, tiled=False)


def all_sum(value):
    for axis in ("px", "py"):
        value = jnp.sum(gathered(value, axis), axis=0)
    return value


def two_sum(a, b):
    total = a + b
    back = total - a
    return total, (a - (total - back)) + (b - back)


def split_float(a):
    scaled = 4097.0 * a
    high = scaled - (scaled - a)
    return high, a - high


def two_prod(a, b):
    product = a * b
    a_high, a_low = split_float(a)
    b_high, b_low = split_float(b)
    error = ((a_high * b_high - product) + a_high * b_low + a_low * b_high) + a_low * b_low
    return product, error


def df_add(x, y):
    total, error = two_sum(x[0], y[0])
    error = error + (x[1] + y[1])
    high = total + error
    return high, error - (high - total)


def df_scale(x, factor):
    product, error = two_prod(x[0], factor)
    error = error + x[1] * factor
    high = product + error
    return high, error - (high - product)


def df_case_sums(a, b):
    a = jnp.moveaxis(a, 2, 0).reshape(a.shape[2], -1)
    b = jnp.moveaxis(b, 2, 0).reshape(b.shape[2], -1)
    high, low = two_prod(a, b)
    while high.shape[1] > 1:
        if high.shape[1] % 2:
            high = jnp.pad(high, ((0, 0), (0, 1)))
            low = jnp.pad(low, ((0, 0), (0, 1)))
        half = high.shape[1] // 2
        high, low = df_add((high[:, :half], low[:, :half]), (high[:, half:], low[:, half:]))
    return high[:, 0], low[:, 0]


def df_tree_sum(high, low):
    while high.shape[0] > 1:
        if high.shape[0] % 2:
            high = jnp.concatenate([high, jnp.zeros_like(high[:1])])
            low = jnp.concatenate([low, jnp.zeros_like(low[:1])])
        half = high.shape[0] // 2
        high, low = df_add((high[:half], low[:half]), (high[half:], low[half:]))
    return high[0], low[0]


def all_sum_mixed(plain, pairs):
    for axis in ("px", "py"):
        rows = [plain] + [part for pair in pairs for part in pair]
        width = plain.shape[0]
        every = gathered(jnp.concatenate(rows), axis)
        row = lambda k: every[:, k * width : (k + 1) * width]
        plain = jnp.sum(row(0), axis=0)
        pairs = [df_tree_sum(row(1 + 2 * k), row(2 + 2 * k)) for k in range(len(pairs))]
    return plain, pairs


def permute_side(values, flip):
    shape = values.shape
    pairs = values.reshape(shape[:-1] + (shape[-1] // 2, 2))
    reversed_pairs = jnp.flip(pairs, axis=-2).reshape(shape)
    return jnp.where(flip[:, :, None, None], reversed_pairs, values)


def on_device(
    solution,
    residual,
    direction,
    rz_previous,
    dual_inverse,
    dual_schur,
    coupling,
    coarse_inverse,
    matching,
    patch_counts,
):
    rows_here = solution.shape[0]
    cols_here = solution.shape[1]
    total_rows = rows_here * lax.axis_size("px")
    total_cols = cols_here * lax.axis_size("py")
    grid_row = lax.axis_index("px") * rows_here + jnp.arange(rows_here)
    grid_col = lax.axis_index("py") * cols_here + jnp.arange(cols_here)
    local_slot = jnp.arange(rows_here)[:, None] * cols_here + jnp.arange(cols_here)[None, :]
    count_here = patch_counts[0, 0]
    active = (local_slot < count_here).astype(jnp.float32)[:, :, None, None]
    edge_index = jnp.arange(2 * SIDE)
    edge_ok = jnp.where(
        edge_index[None, None, :] < SIDE,
        (grid_col < total_cols - 1)[None, :, None] & (grid_row >= 0)[:, None, None],
        (grid_row < total_rows - 1)[:, None, None] & (grid_col >= 0)[None, :, None],
    )
    edge_mask = active * edge_ok[:, :, None, :].astype(jnp.float32)
    vertex_mask = ((grid_row >= 1)[:, None] & (grid_col >= 1)[None, :]).astype(jnp.float32)[
        :, :, None, None
    ]
    east_flip = matching[:, :, 0, 0] != 0
    north_flip = matching[:, :, 1, 0] != 0

    def spread_parts(vector):
        east_part = vector[..., :SIDE]
        north_part = vector[..., SIDE:]
        east_perm = permute_side(east_part, east_flip)
        north_perm = permute_side(north_part, north_flip)
        west_edge = passed_along(east_perm, "py", 1)
        from_west = jnp.concatenate([west_edge, east_perm[:, :-1]], 1)
        south_edge = passed_along(north_perm, "px", 1)
        from_south = jnp.concatenate([south_edge, north_perm[:-1]], 0)
        return east_part, north_part, from_west, from_south

    def spread_of(parts):
        east_part, north_part, from_west, from_south = parts
        return jnp.concatenate([east_part, north_part, -from_west, -from_south], 3)

    def jump_b(side_values):
        west_side = side_values[..., 2 * SIDE : 3 * SIDE]
        south_side = side_values[..., 3 * SIDE :]
        east_edge, north_edge = exchanged_together(
            [(west_side, "py", -1), (south_side, "px", -1)]
        )
        from_east = jnp.concatenate([west_side[:, 1:], east_edge], 1)
        from_north = jnp.concatenate([south_side[1:], north_edge], 0)
        east_term = permute_side(from_east, east_flip)
        north_term = permute_side(from_north, north_flip)
        joined = jnp.concatenate(
            [side_values[..., :SIDE] - east_term, side_values[..., SIDE : 2 * SIDE] - north_term], 3
        )
        return joined * edge_mask

    def patch_products(matrices, vectors):
        return (
            jnp.einsum("rpab,rpcb->rpca", matrices, vectors, preferred_element_type=jnp.float32)
            * active
        )

    def spread_pair(first, second):
        east_perm = jnp.stack(
            [permute_side(first[..., :SIDE], east_flip), permute_side(second[..., :SIDE], east_flip)]
        )
        north_perm = jnp.stack(
            [permute_side(first[..., SIDE:], north_flip), permute_side(second[..., SIDE:], north_flip)]
        )
        west_edge = passed_along(east_perm, "py", 1)
        from_west = jnp.concatenate([west_edge, east_perm[:, :, :-1]], 2)
        south_edge = passed_along(north_perm, "px", 1)
        from_south = jnp.concatenate([south_edge, north_perm[:, :-1]], 1)
        return [
            (field[..., :SIDE], field[..., SIDE:], from_west[k], from_south[k])
            for k, field in enumerate((first, second))
        ]

    def jump_and_spread(side_values):
        east_side = side_values[..., :SIDE]
        north_side = side_values[..., SIDE : 2 * SIDE]
        west_side = side_values[..., 2 * SIDE : 3 * SIDE]
        south_side = side_values[..., 3 * SIDE :]
        ones = jnp.broadcast_to(active, east_side.shape)
        east_edge, north_edge = exchanged_together(
            [(west_side, "py", -1), (south_side, "px", -1)]
        )
        from_east = jnp.concatenate([west_side[:, 1:], east_edge], 1)
        from_north = jnp.concatenate([south_side[1:], north_edge], 0)
        east_perm_side = permute_side(east_side, east_flip)
        north_perm_side = permute_side(north_side, north_flip)
        west_sent = passed_along(jnp.stack([east_perm_side, ones]), "py", 1)
        south_sent = passed_along(jnp.stack([north_perm_side, ones]), "px", 1)
        east_term = permute_side(from_east, east_flip)
        north_term = permute_side(from_north, north_flip)
        joined = jnp.concatenate([east_side - east_term, north_side - north_term], 3)
        half_jump = 0.5 * (joined * edge_mask)
        west_edge = 0.5 * ((west_sent[0] - west_side[:, :1]) * west_sent[1])
        south_edge = 0.5 * ((south_sent[0] - south_side[:1]) * south_sent[1])
        local_east = permute_side(half_jump[..., :SIDE], east_flip)
        local_north = permute_side(half_jump[..., SIDE:], north_flip)
        from_west = jnp.concatenate([west_edge, local_east[:, :-1]], 1)
        from_south = jnp.concatenate([south_edge, local_north[:-1]], 0)
        return half_jump, (half_jump[..., :SIDE], half_jump[..., SIDE:], from_west, from_south)

    start_sol = solution * edge_mask
    start_res = residual * edge_mask
    start_dir = direction * edge_mask
    res_parts, dir_parts = spread_pair(0.5 * start_res, start_dir)
    spread = spread_of(res_parts).astype(jnp.bfloat16)
    side_values = patch_products(dual_schur, spread)
    precond, precond_parts = jump_and_spread(side_values)
    rz_current = all_sum(jnp.sum(start_res * precond, axis=(0, 1, 3)))
    step_ratio = rz_current / rz_previous
    ratio = step_ratio[None, None, :, None]
    new_direction = precond + ratio * start_dir
    spread = spread_of(
        tuple(p + ratio * d for p, d in zip(precond_parts, dir_parts))
    ).astype(jnp.bfloat16)
    inner_part = patch_products(dual_inverse, spread)
    corner = (
        jnp.einsum("rpkb,rpcb->rpck", coupling, spread, preferred_element_type=jnp.float32) * active
    )
    corner_width = corner.shape[2] * corner.shape[3]
    payload = jnp.concatenate(
        [
            corner.reshape(rows_here, cols_here, corner_width),
            coarse_inverse.reshape(rows_here, cols_here, 4),
        ],
        2,
    )
    from_west_col, from_east_col = exchanged_together([(payload, "py", 1), (payload, "py", -1)])
    row = jnp.concatenate([from_west_col[:, -1:], payload, from_east_col[:, :1]], 1)
    from_south_row, from_north_row = exchanged_together([(row, "px", 1), (row, "px", -1)])
    block = jnp.concatenate([from_south_row[-1:], row, from_north_row[:1]], 0)
    corners = block[..., :corner_width].reshape(
        rows_here + 2, cols_here + 2, corner.shape[2], corner.shape[3]
    )
    blocks = block[..., corner_width:].reshape(rows_here + 2, cols_here + 2, 2, 2)
    vertex_row = lax.axis_index("px") * rows_here + jnp.arange(rows_here + 1)
    vertex_col = lax.axis_index("py") * cols_here + jnp.arange(cols_here + 1)
    vertex_ok = ((vertex_row >= 1)[:, None] & (vertex_col >= 1)[None, :]).astype(jnp.float32)[
        :, :, None, None
    ]
    assembled = (
        corners[1:, 1:, :, 0:2]
        + corners[1:, :-1, :, 2:4]
        + corners[:-1, 1:, :, 4:6]
        + corners[:-1, :-1, :, 6:8]
    ) * vertex_ok
    coarse = jnp.einsum(
        "rpxy,rpcy->rpcx", blocks[1:, 1:], assembled, precision=lax.Precision.HIGHEST
    )
    corners_back = jnp.concatenate(
        [coarse[:-1, :-1], coarse[:-1, 1:], coarse[1:, :-1], coarse[1:, 1:]], 3
    )
    correction = jnp.einsum(
        "rpkb,rpck->rpcb",
        coupling.astype(jnp.float32),
        corners_back,
        precision=lax.Precision.HIGHEST,
    )
    image = jump_b((inner_part + correction) * active)
    curvature, (res_res, res_img, img_img) = all_sum_mixed(
        jnp.sum(new_direction * image, axis=(0, 1, 3)),
        [df_case_sums(start_res, start_res), df_case_sums(start_res, image), df_case_sums(image, image)],
    )
    step_length = rz_current / curvature
    new_solution = start_sol + step_length[None, None, :, None] * new_direction
    new_residual = start_res - step_length[None, None, :, None] * image
    cross = df_scale(res_img, -2.0 * step_length)
    square = df_scale(df_scale(img_img, step_length), step_length)
    merged = df_add(df_add(res_res, cross), square)
    merged_sq = merged[0] + merged[1]
    scale = res_res[0] + step_length * step_length * img_img[0]
    trusted = jnp.all(jnp.isfinite(scale) & (merged_sq > 0) & (scale <= 1e7 * merged_sq))
    residual_sq = lax.cond(
        trusted,
        lambda: merged_sq,
        lambda: all_sum(jnp.sum(new_residual * new_residual, axis=(0, 1, 3))),
    )
    return (new_solution, new_residual, new_direction, rz_current, residual_sq)


def solution(mesh):
    in_specs = (
        P("px", "py", None, None),
        P("px", "py", None, None),
        P("px", "py", None, None),
        P(),
        P("px", "py", None, None),
        P("px", "py", None, None),
        P("px", "py", None, None),
        P("px", "py", None, None),
        P("px", "py", None, None),
        P("px", "py"),
    )
    out_specs = (
        P("px", "py", None, None),
        P("px", "py", None, None),
        P("px", "py", None, None),
        P(),
        P(),
    )
    return jax.shard_map(
        on_device, mesh=mesh, in_specs=in_specs, out_specs=out_specs, check_vma=False
    )
```

```python
import jax
import jax.numpy as jnp
from jax import lax
from jax.sharding import PartitionSpec as P

SIDE = 68


def passed_along(value, axis, by):
    peers = lax.axis_size(axis)
    pairs = [(i, i + by) for i in range(peers) if 0 <= i + by < peers]
    return lax.ppermute(value, axis, pairs)


def exchanged_together(moves):
    values = lax.optimization_barrier(tuple(value for value, _, _ in moves))
    received = tuple(passed_along(value, axis, by) for value, (_, axis, by) in zip(values, moves))
    return lax.optimization_barrier(received)


INNER = {"py": 2, "px": 4}


def butterfly_rounds(axis):
    peers = lax.axis_size(axis)
    inner = INNER.get(axis, peers)
    if peers % inner or inner & (inner - 1) or (peers // inner) & (peers // inner - 1):
        inner = peers
    rounds = []
    step = 1
    while step < inner:
        rounds.append([(i, i ^ step) for i in range(peers)])
        step *= 2
    outer = peers // inner
    gray = [k ^ (k >> 1) for k in range(outer)]
    place = {g: k for k, g in enumerate(gray)}
    step = 1
    while step < outer:
        rounds.append(
            [(i, place[gray[i // inner] ^ step] * inner + i % inner) for i in range(peers)]
        )
        step *= 2
    return rounds


def gathered(value, axis):
    peers = lax.axis_size(axis)
    copies = jnp.broadcast_to(value[None], (peers,) + value.shape)
    return lax.all_to_all(copies, axis, 0, 0, tiled=False)


def all_sum(value):
    for axis in ("py", "px"):
        value = jnp.sum(gathered(value, axis), axis=0)
    return value


def all_sum_carrying(value, sends):
    received = []
    for axis, extra in zip(("py", "px"), sends):
        width = value.shape[0]
        every = gathered(jnp.concatenate([value, extra.reshape(-1)]), axis)
        value = jnp.sum(every[:, :width], axis=0)
        here = lax.axis_index(axis)
        got = lax.dynamic_index_in_dim(every[:, width:], jnp.maximum(here - 1, 0), 0, keepdims=False)
        received.append(jnp.where(here >= 1, got, 0.0).reshape(extra.shape))
    return value, received


def two_sum(a, b):
    total = a + b
    back = total - a
    return total, (a - (total - back)) + (b - back)


def split_float(a):
    scaled = 4097.0 * a
    high = scaled - (scaled - a)
    return high, a - high


def two_prod(a, b):
    product = a * b
    a_high, a_low = split_float(a)
    b_high, b_low = split_float(b)
    error = ((a_high * b_high - product) + a_high * b_low + a_low * b_high) + a_low * b_low
    return product, error


def df_add(x, y):
    total, error = two_sum(x[0], y[0])
    error = error + (x[1] + y[1])
    high = total + error
    return high, error - (high - total)


def df_scale(x, factor):
    product, error = two_prod(x[0], factor)
    error = error + x[1] * factor
    high = product + error
    return high, error - (high - product)


def df_case_sums(a, b):
    a = jnp.moveaxis(a, 2, 0).reshape(a.shape[2], -1)
    b = jnp.moveaxis(b, 2, 0).reshape(b.shape[2], -1)
    high, low = two_prod(a, b)
    while high.shape[1] > 1:
        if high.shape[1] % 2:
            high = jnp.pad(high, ((0, 0), (0, 1)))
            low = jnp.pad(low, ((0, 0), (0, 1)))
        half = high.shape[1] // 2
        high, low = df_add((high[:, :half], low[:, :half]), (high[:, half:], low[:, half:]))
    return high[:, 0], low[:, 0]


def df_tree_sum(high, low):
    while high.shape[0] > 1:
        if high.shape[0] % 2:
            high = jnp.concatenate([high, jnp.zeros_like(high[:1])])
            low = jnp.concatenate([low, jnp.zeros_like(low[:1])])
        half = high.shape[0] // 2
        high, low = df_add((high[:half], low[:half]), (high[half:], low[half:]))
    return high[0], low[0]


def all_sum_mixed(plain, pairs):
    for axis in ("py", "px"):
        rows = [plain] + [part for pair in pairs for part in pair]
        width = plain.shape[0]
        every = gathered(jnp.concatenate(rows), axis)
        row = lambda k: every[:, k * width : (k + 1) * width]
        plain = jnp.sum(row(0), axis=0)
        pairs = [df_tree_sum(row(1 + 2 * k), row(2 + 2 * k)) for k in range(len(pairs))]
    return plain, pairs


def permute_side(values, flip):
    shape = values.shape
    pairs = values.reshape(shape[:-1] + (shape[-1] // 2, 2))
    reversed_pairs = jnp.flip(pairs, axis=-2).reshape(shape)
    return jnp.where(flip[:, :, None, None], reversed_pairs, values)


def on_device(
    solution,
    residual,
    direction,
    rz_previous,
    dual_inverse,
    dual_schur,
    coupling,
    coarse_inverse,
    matching,
    patch_counts,
):
    rows_here = solution.shape[0]
    cols_here = solution.shape[1]
    total_rows = rows_here * lax.axis_size("px")
    total_cols = cols_here * lax.axis_size("py")
    grid_row = lax.axis_index("px") * rows_here + jnp.arange(rows_here)
    grid_col = lax.axis_index("py") * cols_here + jnp.arange(cols_here)
    local_slot = jnp.arange(rows_here)[:, None] * cols_here + jnp.arange(cols_here)[None, :]
    count_here = patch_counts[0, 0]
    active = (local_slot < count_here).astype(jnp.float32)[:, :, None, None]
    edge_index = jnp.arange(2 * SIDE)
    edge_ok = jnp.where(
        edge_index[None, None, :] < SIDE,
        (grid_col < total_cols - 1)[None, :, None] & (grid_row >= 0)[:, None, None],
        (grid_row < total_rows - 1)[:, None, None] & (grid_col >= 0)[None, :, None],
    )
    edge_mask = active * edge_ok[:, :, None, :].astype(jnp.float32)
    vertex_mask = ((grid_row >= 1)[:, None] & (grid_col >= 1)[None, :]).astype(jnp.float32)[
        :, :, None, None
    ]
    east_flip = matching[:, :, 0, 0] != 0
    north_flip = matching[:, :, 1, 0] != 0

    def spread_parts(vector):
        east_part = vector[..., :SIDE]
        north_part = vector[..., SIDE:]
        east_perm = permute_side(east_part, east_flip)
        north_perm = permute_side(north_part, north_flip)
        west_edge = passed_along(east_perm, "py", 1)
        from_west = jnp.concatenate([west_edge, east_perm[:, :-1]], 1)
        south_edge = passed_along(north_perm, "px", 1)
        from_south = jnp.concatenate([south_edge, north_perm[:-1]], 0)
        return east_part, north_part, from_west, from_south

    def spread_of(parts):
        east_part, north_part, from_west, from_south = parts
        return jnp.concatenate([east_part, north_part, -from_west, -from_south], 3)

    def jump_b(side_values):
        west_side = side_values[..., 2 * SIDE : 3 * SIDE]
        south_side = side_values[..., 3 * SIDE :]
        east_edge, north_edge = exchanged_together(
            [(west_side, "py", -1), (south_side, "px", -1)]
        )
        from_east = jnp.concatenate([west_side[:, 1:], east_edge], 1)
        from_north = jnp.concatenate([south_side[1:], north_edge], 0)
        east_term = permute_side(from_east, east_flip)
        north_term = permute_side(from_north, north_flip)
        joined = jnp.concatenate(
            [side_values[..., :SIDE] - east_term, side_values[..., SIDE : 2 * SIDE] - north_term], 3
        )
        return joined * edge_mask

    def patch_products(matrices, vectors):
        return (
            jnp.einsum("rpab,rpcb->rpca", matrices, vectors, preferred_element_type=jnp.float32)
            * active
        )

    def spread_pair(first, second):
        east_perm = jnp.stack(
            [permute_side(first[..., :SIDE], east_flip), permute_side(second[..., :SIDE], east_flip)]
        )
        north_perm = jnp.stack(
            [permute_side(first[..., SIDE:], north_flip), permute_side(second[..., SIDE:], north_flip)]
        )
        west_edge = passed_along(east_perm, "py", 1)
        from_west = jnp.concatenate([west_edge, east_perm[:, :, :-1]], 2)
        south_edge = passed_along(north_perm, "px", 1)
        from_south = jnp.concatenate([south_edge, north_perm[:, :-1]], 1)
        return [
            (field[..., :SIDE], field[..., SIDE:], from_west[k], from_south[k])
            for k, field in enumerate((first, second))
        ]

    def jump_and_spread(side_values):
        east_side = side_values[..., :SIDE]
        north_side = side_values[..., SIDE : 2 * SIDE]
        west_side = side_values[..., 2 * SIDE : 3 * SIDE]
        south_side = side_values[..., 3 * SIDE :]
        ones = jnp.broadcast_to(active, east_side.shape)
        east_edge, north_edge = exchanged_together(
            [(west_side, "py", -1), (south_side, "px", -1)]
        )
        from_east = jnp.concatenate([west_side[:, 1:], east_edge], 1)
        from_north = jnp.concatenate([south_side[1:], north_edge], 0)
        east_perm_side = permute_side(east_side, east_flip)
        north_perm_side = permute_side(north_side, north_flip)
        east_term = permute_side(from_east, east_flip)
        north_term = permute_side(from_north, north_flip)
        joined = jnp.concatenate([east_side - east_term, north_side - north_term], 3)
        half_jump = 0.5 * (joined * edge_mask)
        def finish(west_sent, south_sent):
            west_edge = 0.5 * ((west_sent[0] - west_side[:, :1]) * west_sent[1])
            south_edge = 0.5 * ((south_sent[0] - south_side[:1]) * south_sent[1])
            local_east = permute_side(half_jump[..., :SIDE], east_flip)
            local_north = permute_side(half_jump[..., SIDE:], north_flip)
            from_west = jnp.concatenate([west_edge, local_east[:, :-1]], 1)
            from_south = jnp.concatenate([south_edge, local_north[:-1]], 0)
            return (half_jump[..., :SIDE], half_jump[..., SIDE:], from_west, from_south)

        sends = (jnp.stack([east_perm_side, ones]), jnp.stack([north_perm_side, ones]))
        return half_jump, finish, sends

    start_sol = solution * edge_mask
    start_res = residual * edge_mask
    start_dir = direction * edge_mask
    res_parts, dir_parts = spread_pair(0.5 * start_res, start_dir)
    spread = spread_of(res_parts).astype(jnp.bfloat16)
    side_values = patch_products(dual_schur, spread)
    precond, finish_parts, sends = jump_and_spread(side_values)
    rz_current, received = all_sum_carrying(jnp.sum(start_res * precond, axis=(0, 1, 3)), sends)
    precond_parts = finish_parts(*received)
    step_ratio = rz_current / rz_previous
    ratio = step_ratio[None, None, :, None]
    new_direction = precond + ratio * start_dir
    spread = spread_of(
        tuple(p + ratio * d for p, d in zip(precond_parts, dir_parts))
    ).astype(jnp.bfloat16)
    inner_part = patch_products(dual_inverse, spread)
    corner = (
        jnp.einsum("rpkb,rpcb->rpck", coupling, spread, preferred_element_type=jnp.float32) * active
    )
    corner_width = corner.shape[2] * corner.shape[3]
    payload = jnp.concatenate(
        [
            corner.reshape(rows_here, cols_here, corner_width),
            coarse_inverse.reshape(rows_here, cols_here, 4),
        ],
        2,
    )
    from_west_col, from_east_col = exchanged_together([(payload, "py", 1), (payload, "py", -1)])
    row = jnp.concatenate([from_west_col[:, -1:], payload, from_east_col[:, :1]], 1)
    from_south_row, from_north_row = exchanged_together([(row, "px", 1), (row, "px", -1)])
    block = jnp.concatenate([from_south_row[-1:], row, from_north_row[:1]], 0)
    corners = block[..., :corner_width].reshape(
        rows_here + 2, cols_here + 2, corner.shape[2], corner.shape[3]
    )
    blocks = block[..., corner_width:].reshape(rows_here + 2, cols_here + 2, 2, 2)
    vertex_row = lax.axis_index("px") * rows_here + jnp.arange(rows_here + 1)
    vertex_col = lax.axis_index("py") * cols_here + jnp.arange(cols_here + 1)
    vertex_ok = ((vertex_row >= 1)[:, None] & (vertex_col >= 1)[None, :]).astype(jnp.float32)[
        :, :, None, None
    ]
    assembled = (
        corners[1:, 1:, :, 0:2]
        + corners[1:, :-1, :, 2:4]
        + corners[:-1, 1:, :, 4:6]
        + corners[:-1, :-1, :, 6:8]
    ) * vertex_ok
    coarse = jnp.einsum(
        "rpxy,rpcy->rpcx", blocks[1:, 1:], assembled, precision=lax.Precision.HIGHEST
    )
    corners_back = jnp.concatenate(
        [coarse[:-1, :-1], coarse[:-1, 1:], coarse[1:, :-1], coarse[1:, 1:]], 3
    )
    correction = jnp.einsum(
        "rpkb,rpck->rpcb",
        coupling.astype(jnp.float32),
        corners_back,
        precision=lax.Precision.HIGHEST,
    )
    image = jump_b((inner_part + correction) * active)
    curvature, (res_res, res_img, img_img) = all_sum_mixed(
        jnp.sum(new_direction * image, axis=(0, 1, 3)),
        [df_case_sums(start_res, start_res), df_case_sums(start_res, image), df_case_sums(image, image)],
    )
    step_length = rz_current / curvature
    new_solution = start_sol + step_length[None, None, :, None] * new_direction
    new_residual = start_res - step_length[None, None, :, None] * image
    cross = df_scale(res_img, -2.0 * step_length)
    square = df_scale(df_scale(img_img, step_length), step_length)
    merged = df_add(df_add(res_res, cross), square)
    merged_sq = merged[0] + merged[1]
    scale = res_res[0] + step_length * step_length * img_img[0]
    trusted = jnp.all(jnp.isfinite(scale) & (merged_sq > 0) & (scale <= 1e7 * merged_sq))
    residual_sq = lax.cond(
        trusted,
        lambda: merged_sq,
        lambda: all_sum(jnp.sum(new_residual * new_residual, axis=(0, 1, 3))),
    )
    return (new_solution, new_residual, new_direction, rz_current, residual_sq)


def solution(mesh):
    in_specs = (
        P("px", "py", None, None),
        P("px", "py", None, None),
        P("px", "py", None, None),
        P(),
        P("px", "py", None, None),
        P("px", "py", None, None),
        P("px", "py", None, None),
        P("px", "py", None, None),
        P("px", "py", None, None),
        P("px", "py"),
    )
    out_specs = (
        P("px", "py", None, None),
        P("px", "py", None, None),
        P("px", "py", None, None),
        P(),
        P(),
    )
    return jax.shard_map(
        on_device, mesh=mesh, in_specs=in_specs, out_specs=out_specs, check_vma=False
    )
```

```python
import jax
import jax.numpy as jnp
from jax import lax
from jax.sharding import PartitionSpec as P

SIDE = 68


def passed_along(value, axis, by):
    peers = lax.axis_size(axis)
    pairs = [(i, i + by) for i in range(peers) if 0 <= i + by < peers]
    return lax.ppermute(value, axis, pairs)


def exchanged_together(moves):
    values = lax.optimization_barrier(tuple(value for value, _, _ in moves))
    received = tuple(passed_along(value, axis, by) for value, (_, axis, by) in zip(values, moves))
    return lax.optimization_barrier(received)


INNER = {"py": 2, "px": 4}


def butterfly_rounds(axis):
    peers = lax.axis_size(axis)
    inner = INNER.get(axis, peers)
    if peers % inner or inner & (inner - 1) or (peers // inner) & (peers // inner - 1):
        inner = peers
    rounds = []
    step = 1
    while step < inner:
        rounds.append([(i, i ^ step) for i in range(peers)])
        step *= 2
    outer = peers // inner
    gray = [k ^ (k >> 1) for k in range(outer)]
    place = {g: k for k, g in enumerate(gray)}
    step = 1
    while step < outer:
        rounds.append(
            [(i, place[gray[i // inner] ^ step] * inner + i % inner) for i in range(peers)]
        )
        step *= 2
    return rounds


def gathered(value, axis):
    peers = lax.axis_size(axis)
    copies = jnp.broadcast_to(value[None], (peers,) + value.shape)
    return lax.all_to_all(copies, axis, 0, 0, tiled=False)


def all_sum(value):
    for axis in ("py", "px"):
        value = jnp.sum(gathered(value, axis), axis=0)
    return value


def two_sum(a, b):
    total = a + b
    back = total - a
    return total, (a - (total - back)) + (b - back)


def split_float(a):
    scaled = 4097.0 * a
    high = scaled - (scaled - a)
    return high, a - high


def two_prod(a, b):
    product = a * b
    a_high, a_low = split_float(a)
    b_high, b_low = split_float(b)
    error = ((a_high * b_high - product) + a_high * b_low + a_low * b_high) + a_low * b_low
    return product, error


def df_add(x, y):
    total, error = two_sum(x[0], y[0])
    error = error + (x[1] + y[1])
    high = total + error
    return high, error - (high - total)


def df_scale(x, factor):
    product, error = two_prod(x[0], factor)
    error = error + x[1] * factor
    high = product + error
    return high, error - (high - product)


def df_case_sums(a, b):
    a = jnp.moveaxis(a, 2, 0).reshape(a.shape[2], -1)
    b = jnp.moveaxis(b, 2, 0).reshape(b.shape[2], -1)
    high, low = two_prod(a, b)
    while high.shape[1] > 1:
        if high.shape[1] % 2:
            high = jnp.pad(high, ((0, 0), (0, 1)))
            low = jnp.pad(low, ((0, 0), (0, 1)))
        half = high.shape[1] // 2
        high, low = df_add((high[:, :half], low[:, :half]), (high[:, half:], low[:, half:]))
    return high[:, 0], low[:, 0]


def df_case_sums_stacked(a, b):
    count, cases = a.shape[0], a.shape[3]
    a = jnp.moveaxis(a, 3, 1).reshape(count, cases, -1)
    b = jnp.moveaxis(b, 3, 1).reshape(count, cases, -1)
    high, low = two_prod(a, b)
    while high.shape[2] > 1:
        if high.shape[2] % 2:
            high = jnp.pad(high, ((0, 0), (0, 0), (0, 1)))
            low = jnp.pad(low, ((0, 0), (0, 0), (0, 1)))
        half = high.shape[2] // 2
        high, low = df_add(
            (high[:, :, :half], low[:, :, :half]), (high[:, :, half:], low[:, :, half:])
        )
    return [(high[k, :, 0], low[k, :, 0]) for k in range(count)]


def df_tree_sum(high, low):
    while high.shape[0] > 1:
        if high.shape[0] % 2:
            high = jnp.concatenate([high, jnp.zeros_like(high[:1])])
            low = jnp.concatenate([low, jnp.zeros_like(low[:1])])
        half = high.shape[0] // 2
        high, low = df_add((high[:half], low[:half]), (high[half:], low[half:]))
    return high[0], low[0]


def all_sum_mixed(plain, pairs):
    for axis in ("py", "px"):
        rows = [plain] + [part for pair in pairs for part in pair]
        width = plain.shape[0]
        every = gathered(jnp.concatenate(rows), axis)
        row = lambda k: every[:, k * width : (k + 1) * width]
        plain = jnp.sum(row(0), axis=0)
        pairs = [df_tree_sum(row(1 + 2 * k), row(2 + 2 * k)) for k in range(len(pairs))]
    return plain, pairs


def permute_side(values, flip):
    shape = values.shape
    pairs = values.reshape(shape[:-1] + (shape[-1] // 2, 2))
    reversed_pairs = jnp.flip(pairs, axis=-2).reshape(shape)
    return jnp.where(flip[:, :, None, None], reversed_pairs, values)


def on_device(
    solution,
    residual,
    direction,
    rz_previous,
    dual_inverse,
    dual_schur,
    coupling,
    coarse_inverse,
    matching,
    patch_counts,
):
    rows_here = solution.shape[0]
    cols_here = solution.shape[1]
    total_rows = rows_here * lax.axis_size("px")
    total_cols = cols_here * lax.axis_size("py")
    grid_row = lax.axis_index("px") * rows_here + jnp.arange(rows_here)
    grid_col = lax.axis_index("py") * cols_here + jnp.arange(cols_here)
    local_slot = jnp.arange(rows_here)[:, None] * cols_here + jnp.arange(cols_here)[None, :]
    count_here = patch_counts[0, 0]
    active = (local_slot < count_here).astype(jnp.float32)[:, :, None, None]
    edge_index = jnp.arange(2 * SIDE)
    edge_ok = jnp.where(
        edge_index[None, None, :] < SIDE,
        (grid_col < total_cols - 1)[None, :, None] & (grid_row >= 0)[:, None, None],
        (grid_row < total_rows - 1)[:, None, None] & (grid_col >= 0)[None, :, None],
    )
    edge_mask = active * edge_ok[:, :, None, :].astype(jnp.float32)
    vertex_mask = ((grid_row >= 1)[:, None] & (grid_col >= 1)[None, :]).astype(jnp.float32)[
        :, :, None, None
    ]
    east_flip = matching[:, :, 0, 0] != 0
    north_flip = matching[:, :, 1, 0] != 0

    def spread_parts(vector):
        east_part = vector[..., :SIDE]
        north_part = vector[..., SIDE:]
        east_perm = permute_side(east_part, east_flip)
        north_perm = permute_side(north_part, north_flip)
        west_edge = passed_along(east_perm, "py", 1)
        from_west = jnp.concatenate([west_edge, east_perm[:, :-1]], 1)
        south_edge = passed_along(north_perm, "px", 1)
        from_south = jnp.concatenate([south_edge, north_perm[:-1]], 0)
        return east_part, north_part, from_west, from_south

    def spread_of(parts):
        east_part, north_part, from_west, from_south = parts
        return jnp.concatenate([east_part, north_part, -from_west, -from_south], 3)

    def jump_b(side_values):
        west_side = side_values[..., 2 * SIDE : 3 * SIDE]
        south_side = side_values[..., 3 * SIDE :]
        east_edge, north_edge = exchanged_together(
            [(west_side, "py", -1), (south_side, "px", -1)]
        )
        from_east = jnp.concatenate([west_side[:, 1:], east_edge], 1)
        from_north = jnp.concatenate([south_side[1:], north_edge], 0)
        east_term = permute_side(from_east, east_flip)
        north_term = permute_side(from_north, north_flip)
        joined = jnp.concatenate(
            [side_values[..., :SIDE] - east_term, side_values[..., SIDE : 2 * SIDE] - north_term], 3
        )
        return joined * edge_mask

    def patch_products(matrices, vectors):
        return (
            jnp.einsum("rpab,rpcb->rpca", matrices, vectors, preferred_element_type=jnp.float32)
            * active
        )

    def spread_pair(first, second):
        east_perm = jnp.stack(
            [permute_side(first[..., :SIDE], east_flip), permute_side(second[..., :SIDE], east_flip)]
        )
        north_perm = jnp.stack(
            [permute_side(first[..., SIDE:], north_flip), permute_side(second[..., SIDE:], north_flip)]
        )
        west_edge = passed_along(east_perm, "py", 1)
        from_west = jnp.concatenate([west_edge, east_perm[:, :, :-1]], 2)
        south_edge = passed_along(north_perm, "px", 1)
        from_south = jnp.concatenate([south_edge, north_perm[:, :-1]], 1)
        return [
            (field[..., :SIDE], field[..., SIDE:], from_west[k], from_south[k])
            for k, field in enumerate((first, second))
        ]

    def jump_and_spread(side_values):
        east_side = side_values[..., :SIDE]
        north_side = side_values[..., SIDE : 2 * SIDE]
        west_side = side_values[..., 2 * SIDE : 3 * SIDE]
        south_side = side_values[..., 3 * SIDE :]
        ones = jnp.broadcast_to(active, east_side.shape)
        east_edge, north_edge = exchanged_together(
            [(west_side, "py", -1), (south_side, "px", -1)]
        )
        from_east = jnp.concatenate([west_side[:, 1:], east_edge], 1)
        from_north = jnp.concatenate([south_side[1:], north_edge], 0)
        east_perm_side = permute_side(east_side, east_flip)
        north_perm_side = permute_side(north_side, north_flip)
        west_sent = passed_along(jnp.stack([east_perm_side, ones]), "py", 1)
        south_sent = passed_along(jnp.stack([north_perm_side, ones]), "px", 1)
        east_term = permute_side(from_east, east_flip)
        north_term = permute_side(from_north, north_flip)
        joined = jnp.concatenate([east_side - east_term, north_side - north_term], 3)
        half_jump = 0.5 * (joined * edge_mask)
        west_edge = 0.5 * ((west_sent[0] - west_side[:, :1]) * west_sent[1])
        south_edge = 0.5 * ((south_sent[0] - south_side[:1]) * south_sent[1])
        local_east = permute_side(half_jump[..., :SIDE], east_flip)
        local_north = permute_side(half_jump[..., SIDE:], north_flip)
        from_west = jnp.concatenate([west_edge, local_east[:, :-1]], 1)
        from_south = jnp.concatenate([south_edge, local_north[:-1]], 0)
        return half_jump, (half_jump[..., :SIDE], half_jump[..., SIDE:], from_west, from_south)

    start_sol = solution * edge_mask
    start_res = residual * edge_mask
    start_dir = direction * edge_mask
    res_parts, dir_parts = spread_pair(0.5 * start_res, start_dir)
    spread = spread_of(res_parts).astype(jnp.bfloat16)
    side_values = patch_products(dual_schur, spread)
    precond, precond_parts = jump_and_spread(side_values)
    rz_current = all_sum(jnp.sum(start_res * precond, axis=(0, 1, 3)))
    step_ratio = rz_current / rz_previous
    ratio = step_ratio[None, None, :, None]
    new_direction = precond + ratio * start_dir
    spread = spread_of(
        tuple(p + ratio * d for p, d in zip(precond_parts, dir_parts))
    ).astype(jnp.bfloat16)
    inner_part = patch_products(dual_inverse, spread)
    corner = (
        jnp.einsum("rpkb,rpcb->rpck", coupling, spread, preferred_element_type=jnp.float32) * active
    )
    corner_width = corner.shape[2] * corner.shape[3]
    payload = jnp.concatenate(
        [
            corner.reshape(rows_here, cols_here, corner_width),
            coarse_inverse.reshape(rows_here, cols_here, 4),
        ],
        2,
    )
    from_west_col, from_east_col = exchanged_together([(payload, "py", 1), (payload, "py", -1)])
    row = jnp.concatenate([from_west_col[:, -1:], payload, from_east_col[:, :1]], 1)
    from_south_row, from_north_row = exchanged_together([(row, "px", 1), (row, "px", -1)])
    block = jnp.concatenate([from_south_row[-1:], row, from_north_row[:1]], 0)
    corners = block[..., :corner_width].reshape(
        rows_here + 2, cols_here + 2, corner.shape[2], corner.shape[3]
    )
    blocks = block[..., corner_width:].reshape(rows_here + 2, cols_here + 2, 2, 2)
    vertex_row = lax.axis_index("px") * rows_here + jnp.arange(rows_here + 1)
    vertex_col = lax.axis_index("py") * cols_here + jnp.arange(cols_here + 1)
    vertex_ok = ((vertex_row >= 1)[:, None] & (vertex_col >= 1)[None, :]).astype(jnp.float32)[
        :, :, None, None
    ]
    assembled = (
        corners[1:, 1:, :, 0:2]
        + corners[1:, :-1, :, 2:4]
        + corners[:-1, 1:, :, 4:6]
        + corners[:-1, :-1, :, 6:8]
    ) * vertex_ok
    coarse = jnp.einsum(
        "rpxy,rpcy->rpcx", blocks[1:, 1:], assembled, precision=lax.Precision.HIGHEST
    )
    corners_back = jnp.concatenate(
        [coarse[:-1, :-1], coarse[:-1, 1:], coarse[1:, :-1], coarse[1:, 1:]], 3
    )
    correction = jnp.einsum(
        "rpkb,rpck->rpcb",
        coupling.astype(jnp.float32),
        corners_back,
        precision=lax.Precision.HIGHEST,
    )
    image = jump_b((inner_part + correction) * active)
    curvature, (res_res, res_img, img_img) = all_sum_mixed(
        jnp.sum(new_direction * image, axis=(0, 1, 3)),
        df_case_sums_stacked(
            jnp.stack([start_res, start_res, image]), jnp.stack([start_res, image, image])
        ),
    )
    step_length = rz_current / curvature
    new_solution = start_sol + step_length[None, None, :, None] * new_direction
    new_residual = start_res - step_length[None, None, :, None] * image
    cross = df_scale(res_img, -2.0 * step_length)
    square = df_scale(df_scale(img_img, step_length), step_length)
    merged = df_add(df_add(res_res, cross), square)
    merged_sq = merged[0] + merged[1]
    scale = res_res[0] + step_length * step_length * img_img[0]
    trusted = jnp.all(jnp.isfinite(scale) & (merged_sq > 0) & (scale <= 1e7 * merged_sq))
    residual_sq = lax.cond(
        trusted,
        lambda: merged_sq,
        lambda: all_sum(jnp.sum(new_residual * new_residual, axis=(0, 1, 3))),
    )
    return (new_solution, new_residual, new_direction, rz_current, residual_sq)


def solution(mesh):
    in_specs = (
        P("px", "py", None, None),
        P("px", "py", None, None),
        P("px", "py", None, None),
        P(),
        P("px", "py", None, None),
        P("px", "py", None, None),
        P("px", "py", None, None),
        P("px", "py", None, None),
        P("px", "py", None, None),
        P("px", "py"),
    )
    out_specs = (
        P("px", "py", None, None),
        P("px", "py", None, None),
        P("px", "py", None, None),
        P(),
        P(),
    )
    return jax.shard_map(
        on_device, mesh=mesh, in_specs=in_specs, out_specs=out_specs, check_vma=False
    )
```

```python
import jax
import jax.numpy as jnp
from jax import lax
from jax.sharding import PartitionSpec as P

SIDE = 68


def passed_along(value, axis, by):
    peers = lax.axis_size(axis)
    pairs = [(i, i + by) for i in range(peers) if 0 <= i + by < peers]
    return lax.ppermute(value, axis, pairs)


def exchanged_together(moves):
    values = lax.optimization_barrier(tuple(value for value, _, _ in moves))
    received = tuple(passed_along(value, axis, by) for value, (_, axis, by) in zip(values, moves))
    return lax.optimization_barrier(received)


INNER = {"py": 2, "px": 4}


def butterfly_rounds(axis):
    peers = lax.axis_size(axis)
    inner = INNER.get(axis, peers)
    if peers % inner or inner & (inner - 1) or (peers // inner) & (peers // inner - 1):
        inner = peers
    rounds = []
    step = 1
    while step < inner:
        rounds.append([(i, i ^ step) for i in range(peers)])
        step *= 2
    outer = peers // inner
    gray = [k ^ (k >> 1) for k in range(outer)]
    place = {g: k for k, g in enumerate(gray)}
    step = 1
    while step < outer:
        rounds.append(
            [(i, place[gray[i // inner] ^ step] * inner + i % inner) for i in range(peers)]
        )
        step *= 2
    return rounds


def gathered(value, axis):
    peers = lax.axis_size(axis)
    copies = jnp.broadcast_to(value[None], (peers,) + value.shape)
    return lax.all_to_all(copies, axis, 0, 0, tiled=False)


def all_sum(value):
    for axis in ("py", "px"):
        value = jnp.sum(gathered(value, axis), axis=0)
    return value


def two_sum(a, b):
    total = a + b
    back = total - a
    return total, (a - (total - back)) + (b - back)


def split_float(a):
    scaled = 4097.0 * a
    high = scaled - (scaled - a)
    return high, a - high


def two_prod(a, b):
    product = a * b
    a_high, a_low = split_float(a)
    b_high, b_low = split_float(b)
    error = ((a_high * b_high - product) + a_high * b_low + a_low * b_high) + a_low * b_low
    return product, error


def df_add(x, y):
    total, error = two_sum(x[0], y[0])
    error = error + (x[1] + y[1])
    high = total + error
    return high, error - (high - total)


def df_scale(x, factor):
    product, error = two_prod(x[0], factor)
    error = error + x[1] * factor
    high = product + error
    return high, error - (high - product)


def df_case_sums(a, b):
    a = jnp.moveaxis(a, 2, 0).reshape(a.shape[2], -1)
    b = jnp.moveaxis(b, 2, 0).reshape(b.shape[2], -1)
    high, low = two_prod(a, b)
    while high.shape[1] > 1:
        if high.shape[1] % 2:
            high = jnp.pad(high, ((0, 0), (0, 1)))
            low = jnp.pad(low, ((0, 0), (0, 1)))
        half = high.shape[1] // 2
        high, low = df_add((high[:, :half], low[:, :half]), (high[:, half:], low[:, half:]))
    return high[:, 0], low[:, 0]


def df_case_sums_stacked(a, b):
    count, cases = a.shape[0], a.shape[3]
    a = jnp.moveaxis(a, 3, 1).reshape(count, cases, -1)
    b = jnp.moveaxis(b, 3, 1).reshape(count, cases, -1)
    high, low = two_prod(a, b)
    while high.shape[2] > 1:
        if high.shape[2] % 2:
            high = jnp.pad(high, ((0, 0), (0, 0), (0, 1)))
            low = jnp.pad(low, ((0, 0), (0, 0), (0, 1)))
        half = high.shape[2] // 2
        high, low = df_add(
            (high[:, :, :half], low[:, :, :half]), (high[:, :, half:], low[:, :, half:])
        )
    return [(high[k, :, 0], low[k, :, 0]) for k in range(count)]


def df_tree_sum(high, low):
    while high.shape[0] > 1:
        if high.shape[0] % 2:
            high = jnp.concatenate([high, jnp.zeros_like(high[:1])])
            low = jnp.concatenate([low, jnp.zeros_like(low[:1])])
        half = high.shape[0] // 2
        high, low = df_add((high[:half], low[:half]), (high[half:], low[half:]))
    return high[0], low[0]


def all_sum_mixed(plain, pairs):
    for axis in ("py", "px"):
        rows = [plain] + [part for pair in pairs for part in pair]
        width = plain.shape[0]
        every = gathered(jnp.concatenate(rows), axis)
        row = lambda k: every[:, k * width : (k + 1) * width]
        plain = jnp.sum(row(0), axis=0)
        high, low = df_tree_sum(
            jnp.stack([row(1 + 2 * k) for k in range(len(pairs))], 1),
            jnp.stack([row(2 + 2 * k) for k in range(len(pairs))], 1),
        )
        pairs = [(high[k], low[k]) for k in range(len(pairs))]
    return plain, pairs


def permute_side(values, flip):
    shape = values.shape
    pairs = values.reshape(shape[:-1] + (shape[-1] // 2, 2))
    reversed_pairs = jnp.flip(pairs, axis=-2).reshape(shape)
    return jnp.where(flip[:, :, None, None], reversed_pairs, values)


def on_device(
    solution,
    residual,
    direction,
    rz_previous,
    dual_inverse,
    dual_schur,
    coupling,
    coarse_inverse,
    matching,
    patch_counts,
):
    rows_here = solution.shape[0]
    cols_here = solution.shape[1]
    total_rows = rows_here * lax.axis_size("px")
    total_cols = cols_here * lax.axis_size("py")
    grid_row = lax.axis_index("px") * rows_here + jnp.arange(rows_here)
    grid_col = lax.axis_index("py") * cols_here + jnp.arange(cols_here)
    local_slot = jnp.arange(rows_here)[:, None] * cols_here + jnp.arange(cols_here)[None, :]
    count_here = patch_counts[0, 0]
    active = (local_slot < count_here).astype(jnp.float32)[:, :, None, None]
    edge_index = jnp.arange(2 * SIDE)
    edge_ok = jnp.where(
        edge_index[None, None, :] < SIDE,
        (grid_col < total_cols - 1)[None, :, None] & (grid_row >= 0)[:, None, None],
        (grid_row < total_rows - 1)[:, None, None] & (grid_col >= 0)[None, :, None],
    )
    edge_mask = active * edge_ok[:, :, None, :].astype(jnp.float32)
    vertex_mask = ((grid_row >= 1)[:, None] & (grid_col >= 1)[None, :]).astype(jnp.float32)[
        :, :, None, None
    ]
    east_flip = matching[:, :, 0, 0] != 0
    north_flip = matching[:, :, 1, 0] != 0

    def spread_parts(vector):
        east_part = vector[..., :SIDE]
        north_part = vector[..., SIDE:]
        east_perm = permute_side(east_part, east_flip)
        north_perm = permute_side(north_part, north_flip)
        west_edge = passed_along(east_perm, "py", 1)
        from_west = jnp.concatenate([west_edge, east_perm[:, :-1]], 1)
        south_edge = passed_along(north_perm, "px", 1)
        from_south = jnp.concatenate([south_edge, north_perm[:-1]], 0)
        return east_part, north_part, from_west, from_south

    def spread_of(parts):
        east_part, north_part, from_west, from_south = parts
        return jnp.concatenate([east_part, north_part, -from_west, -from_south], 3)

    def jump_b(side_values):
        west_side = side_values[..., 2 * SIDE : 3 * SIDE]
        south_side = side_values[..., 3 * SIDE :]
        east_edge, north_edge = exchanged_together(
            [(west_side, "py", -1), (south_side, "px", -1)]
        )
        from_east = jnp.concatenate([west_side[:, 1:], east_edge], 1)
        from_north = jnp.concatenate([south_side[1:], north_edge], 0)
        east_term = permute_side(from_east, east_flip)
        north_term = permute_side(from_north, north_flip)
        joined = jnp.concatenate(
            [side_values[..., :SIDE] - east_term, side_values[..., SIDE : 2 * SIDE] - north_term], 3
        )
        return joined * edge_mask

    def patch_products(matrices, vectors):
        return (
            jnp.einsum("rpab,rpcb->rpca", matrices, vectors, preferred_element_type=jnp.float32)
            * active
        )

    def spread_pair(first, second):
        east_perm = jnp.stack(
            [permute_side(first[..., :SIDE], east_flip), permute_side(second[..., :SIDE], east_flip)]
        )
        north_perm = jnp.stack(
            [permute_side(first[..., SIDE:], north_flip), permute_side(second[..., SIDE:], north_flip)]
        )
        west_edge = passed_along(east_perm, "py", 1)
        from_west = jnp.concatenate([west_edge, east_perm[:, :, :-1]], 2)
        south_edge = passed_along(north_perm, "px", 1)
        from_south = jnp.concatenate([south_edge, north_perm[:, :-1]], 1)
        return [
            (field[..., :SIDE], field[..., SIDE:], from_west[k], from_south[k])
            for k, field in enumerate((first, second))
        ]

    def jump_and_spread(side_values):
        east_side = side_values[..., :SIDE]
        north_side = side_values[..., SIDE : 2 * SIDE]
        west_side = side_values[..., 2 * SIDE : 3 * SIDE]
        south_side = side_values[..., 3 * SIDE :]
        ones = jnp.broadcast_to(active, east_side.shape)
        east_edge, north_edge = exchanged_together(
            [(west_side, "py", -1), (south_side, "px", -1)]
        )
        from_east = jnp.concatenate([west_side[:, 1:], east_edge], 1)
        from_north = jnp.concatenate([south_side[1:], north_edge], 0)
        east_perm_side = permute_side(east_side, east_flip)
        north_perm_side = permute_side(north_side, north_flip)
        west_sent = passed_along(jnp.stack([east_perm_side, ones]), "py", 1)
        south_sent = passed_along(jnp.stack([north_perm_side, ones]), "px", 1)
        east_term = permute_side(from_east, east_flip)
        north_term = permute_side(from_north, north_flip)
        joined = jnp.concatenate([east_side - east_term, north_side - north_term], 3)
        half_jump = 0.5 * (joined * edge_mask)
        west_edge = 0.5 * ((west_sent[0] - west_side[:, :1]) * west_sent[1])
        south_edge = 0.5 * ((south_sent[0] - south_side[:1]) * south_sent[1])
        local_east = permute_side(half_jump[..., :SIDE], east_flip)
        local_north = permute_side(half_jump[..., SIDE:], north_flip)
        from_west = jnp.concatenate([west_edge, local_east[:, :-1]], 1)
        from_south = jnp.concatenate([south_edge, local_north[:-1]], 0)
        return half_jump, (half_jump[..., :SIDE], half_jump[..., SIDE:], from_west, from_south)

    start_sol = solution * edge_mask
    start_res = residual * edge_mask
    start_dir = direction * edge_mask
    res_parts, dir_parts = spread_pair(0.5 * start_res, start_dir)
    spread = spread_of(res_parts).astype(jnp.bfloat16)
    side_values = patch_products(dual_schur, spread)
    precond, precond_parts = jump_and_spread(side_values)
    rz_current = all_sum(jnp.sum(start_res * precond, axis=(0, 1, 3)))
    step_ratio = rz_current / rz_previous
    ratio = step_ratio[None, None, :, None]
    new_direction = precond + ratio * start_dir
    spread = spread_of(
        tuple(p + ratio * d for p, d in zip(precond_parts, dir_parts))
    ).astype(jnp.bfloat16)
    inner_part = patch_products(dual_inverse, spread)
    corner = (
        jnp.einsum("rpkb,rpcb->rpck", coupling, spread, preferred_element_type=jnp.float32) * active
    )
    corner_width = corner.shape[2] * corner.shape[3]
    payload = jnp.concatenate(
        [
            corner.reshape(rows_here, cols_here, corner_width),
            coarse_inverse.reshape(rows_here, cols_here, 4),
        ],
        2,
    )
    from_west_col, from_east_col = exchanged_together([(payload, "py", 1), (payload, "py", -1)])
    row = jnp.concatenate([from_west_col[:, -1:], payload, from_east_col[:, :1]], 1)
    from_south_row, from_north_row = exchanged_together([(row, "px", 1), (row, "px", -1)])
    block = jnp.concatenate([from_south_row[-1:], row, from_north_row[:1]], 0)
    corners = block[..., :corner_width].reshape(
        rows_here + 2, cols_here + 2, corner.shape[2], corner.shape[3]
    )
    blocks = block[..., corner_width:].reshape(rows_here + 2, cols_here + 2, 2, 2)
    vertex_row = lax.axis_index("px") * rows_here + jnp.arange(rows_here + 1)
    vertex_col = lax.axis_index("py") * cols_here + jnp.arange(cols_here + 1)
    vertex_ok = ((vertex_row >= 1)[:, None] & (vertex_col >= 1)[None, :]).astype(jnp.float32)[
        :, :, None, None
    ]
    assembled = (
        corners[1:, 1:, :, 0:2]
        + corners[1:, :-1, :, 2:4]
        + corners[:-1, 1:, :, 4:6]
        + corners[:-1, :-1, :, 6:8]
    ) * vertex_ok
    coarse = jnp.einsum(
        "rpxy,rpcy->rpcx", blocks[1:, 1:], assembled, precision=lax.Precision.HIGHEST
    )
    corners_back = jnp.concatenate(
        [coarse[:-1, :-1], coarse[:-1, 1:], coarse[1:, :-1], coarse[1:, 1:]], 3
    )
    correction = jnp.einsum(
        "rpkb,rpck->rpcb",
        coupling.astype(jnp.float32),
        corners_back,
        precision=lax.Precision.HIGHEST,
    )
    image = jump_b((inner_part + correction) * active)
    curvature, (res_res, res_img, img_img) = all_sum_mixed(
        jnp.sum(new_direction * image, axis=(0, 1, 3)),
        df_case_sums_stacked(
            jnp.stack([start_res, start_res, image]), jnp.stack([start_res, image, image])
        ),
    )
    step_length = rz_current / curvature
    new_solution = start_sol + step_length[None, None, :, None] * new_direction
    new_residual = start_res - step_length[None, None, :, None] * image
    cross = df_scale(res_img, -2.0 * step_length)
    square = df_scale(df_scale(img_img, step_length), step_length)
    merged = df_add(df_add(res_res, cross), square)
    merged_sq = merged[0] + merged[1]
    scale = res_res[0] + step_length * step_length * img_img[0]
    trusted = jnp.all(jnp.isfinite(scale) & (merged_sq > 0) & (scale <= 1e7 * merged_sq))
    residual_sq = lax.cond(
        trusted,
        lambda: merged_sq,
        lambda: all_sum(jnp.sum(new_residual * new_residual, axis=(0, 1, 3))),
    )
    return (new_solution, new_residual, new_direction, rz_current, residual_sq)


def solution(mesh):
    in_specs = (
        P("px", "py", None, None),
        P("px", "py", None, None),
        P("px", "py", None, None),
        P(),
        P("px", "py", None, None),
        P("px", "py", None, None),
        P("px", "py", None, None),
        P("px", "py", None, None),
        P("px", "py", None, None),
        P("px", "py"),
    )
    out_specs = (
        P("px", "py", None, None),
        P("px", "py", None, None),
        P("px", "py", None, None),
        P(),
        P(),
    )
    return jax.shard_map(
        on_device, mesh=mesh, in_specs=in_specs, out_specs=out_specs, check_vma=False
    )
```

```python
import jax
import jax.numpy as jnp
from jax import lax
from jax.sharding import PartitionSpec as P

SIDE = 68


def passed_along(value, axis, by):
    peers = lax.axis_size(axis)
    pairs = [(i, i + by) for i in range(peers) if 0 <= i + by < peers]
    return lax.ppermute(value, axis, pairs)


def exchanged_together(moves):
    values = lax.optimization_barrier(tuple(value for value, _, _ in moves))
    received = tuple(passed_along(value, axis, by) for value, (_, axis, by) in zip(values, moves))
    return lax.optimization_barrier(received)


INNER = {"py": 2, "px": 4}


def butterfly_rounds(axis):
    peers = lax.axis_size(axis)
    inner = INNER.get(axis, peers)
    if peers % inner or inner & (inner - 1) or (peers // inner) & (peers // inner - 1):
        inner = peers
    rounds = []
    step = 1
    while step < inner:
        rounds.append([(i, i ^ step) for i in range(peers)])
        step *= 2
    outer = peers // inner
    gray = [k ^ (k >> 1) for k in range(outer)]
    place = {g: k for k, g in enumerate(gray)}
    step = 1
    while step < outer:
        rounds.append(
            [(i, place[gray[i // inner] ^ step] * inner + i % inner) for i in range(peers)]
        )
        step *= 2
    return rounds


def gathered(value, axis):
    peers = lax.axis_size(axis)
    copies = jnp.broadcast_to(value[None], (peers,) + value.shape)
    return lax.all_to_all(copies, axis, 0, 0, tiled=False)


def all_sum(value):
    for axis in ("py", "px"):
        value = jnp.sum(gathered(value, axis), axis=0)
    return value


def two_sum(a, b):
    total = a + b
    back = total - a
    return total, (a - (total - back)) + (b - back)


def split_float(a):
    scaled = 4097.0 * a
    high = scaled - (scaled - a)
    return high, a - high


def two_prod(a, b):
    product = a * b
    a_high, a_low = split_float(a)
    b_high, b_low = split_float(b)
    error = ((a_high * b_high - product) + a_high * b_low + a_low * b_high) + a_low * b_low
    return product, error


def df_add(x, y):
    total, error = two_sum(x[0], y[0])
    error = error + (x[1] + y[1])
    high = total + error
    return high, error - (high - total)


def df_scale(x, factor):
    product, error = two_prod(x[0], factor)
    error = error + x[1] * factor
    high = product + error
    return high, error - (high - product)


def df_case_sums(a, b):
    a = jnp.moveaxis(a, 2, 0).reshape(a.shape[2], -1)
    b = jnp.moveaxis(b, 2, 0).reshape(b.shape[2], -1)
    high, low = two_prod(a, b)
    while high.shape[1] > 1:
        if high.shape[1] % 2:
            high = jnp.pad(high, ((0, 0), (0, 1)))
            low = jnp.pad(low, ((0, 0), (0, 1)))
        half = high.shape[1] // 2
        high, low = df_add((high[:, :half], low[:, :half]), (high[:, half:], low[:, half:]))
    return high[:, 0], low[:, 0]


def df_case_sums_stacked(a, b):
    count, cases = a.shape[0], a.shape[3]
    a = jnp.moveaxis(a, 3, 1).reshape(count, cases, -1)
    b = jnp.moveaxis(b, 3, 1).reshape(count, cases, -1)
    high, low = two_prod(a, b)
    while high.shape[2] > 1:
        if high.shape[2] % 2:
            high = jnp.pad(high, ((0, 0), (0, 0), (0, 1)))
            low = jnp.pad(low, ((0, 0), (0, 0), (0, 1)))
        half = high.shape[2] // 2
        high, low = df_add(
            (high[:, :, :half], low[:, :, :half]), (high[:, :, half:], low[:, :, half:])
        )
    return [(high[k, :, 0], low[k, :, 0]) for k in range(count)]


def df_tree_sum(high, low):
    while high.shape[0] > 1:
        if high.shape[0] % 2:
            high = jnp.concatenate([high, jnp.zeros_like(high[:1])])
            low = jnp.concatenate([low, jnp.zeros_like(low[:1])])
        half = high.shape[0] // 2
        high, low = df_add((high[:half], low[:half]), (high[half:], low[half:]))
    return high[0], low[0]


def all_sum_mixed(plain, pairs):
    for axis in ("py", "px"):
        rows = [plain] + [part for pair in pairs for part in pair]
        width = plain.shape[0]
        every = gathered(jnp.concatenate(rows), axis)
        row = lambda k: every[:, k * width : (k + 1) * width]
        plain = jnp.sum(row(0), axis=0)
        high, low = df_tree_sum(
            jnp.stack([row(1 + 2 * k) for k in range(len(pairs))], 1),
            jnp.stack([row(2 + 2 * k) for k in range(len(pairs))], 1),
        )
        pairs = [(high[k], low[k]) for k in range(len(pairs))]
    return plain, pairs


def permute_side(values, flip):
    shape = values.shape
    pairs = values.reshape(shape[:-1] + (shape[-1] // 2, 2))
    reversed_pairs = jnp.flip(pairs, axis=-2).reshape(shape)
    return jnp.where(flip[:, :, None, None], reversed_pairs, values)


def on_device(
    solution,
    residual,
    direction,
    rz_previous,
    dual_inverse,
    dual_schur,
    coupling,
    coarse_inverse,
    matching,
    patch_counts,
):
    rows_here = solution.shape[0]
    cols_here = solution.shape[1]
    total_rows = rows_here * lax.axis_size("px")
    total_cols = cols_here * lax.axis_size("py")
    grid_row = lax.axis_index("px") * rows_here + jnp.arange(rows_here)
    grid_col = lax.axis_index("py") * cols_here + jnp.arange(cols_here)
    local_slot = jnp.arange(rows_here)[:, None] * cols_here + jnp.arange(cols_here)[None, :]
    count_here = patch_counts[0, 0]
    active = (local_slot < count_here).astype(jnp.float32)[:, :, None, None]
    edge_index = jnp.arange(2 * SIDE)
    edge_ok = jnp.where(
        edge_index[None, None, :] < SIDE,
        (grid_col < total_cols - 1)[None, :, None] & (grid_row >= 0)[:, None, None],
        (grid_row < total_rows - 1)[:, None, None] & (grid_col >= 0)[None, :, None],
    )
    edge_mask = active * edge_ok[:, :, None, :].astype(jnp.float32)
    vertex_mask = ((grid_row >= 1)[:, None] & (grid_col >= 1)[None, :]).astype(jnp.float32)[
        :, :, None, None
    ]
    east_flip = matching[:, :, 0, 0] != 0
    north_flip = matching[:, :, 1, 0] != 0

    def spread_parts(vector):
        east_part = vector[..., :SIDE]
        north_part = vector[..., SIDE:]
        east_perm = permute_side(east_part, east_flip)
        north_perm = permute_side(north_part, north_flip)
        west_edge = passed_along(east_perm, "py", 1)
        from_west = jnp.concatenate([west_edge, east_perm[:, :-1]], 1)
        south_edge = passed_along(north_perm, "px", 1)
        from_south = jnp.concatenate([south_edge, north_perm[:-1]], 0)
        return east_part, north_part, from_west, from_south

    def spread_of(parts):
        east_part, north_part, from_west, from_south = parts
        return jnp.concatenate([east_part, north_part, -from_west, -from_south], 3)

    def jump_b(side_values):
        west_side = side_values[..., 2 * SIDE : 3 * SIDE]
        south_side = side_values[..., 3 * SIDE :]
        east_edge, north_edge = exchanged_together(
            [(west_side, "py", -1), (south_side, "px", -1)]
        )
        from_east = jnp.concatenate([west_side[:, 1:], east_edge], 1)
        from_north = jnp.concatenate([south_side[1:], north_edge], 0)
        east_term = permute_side(from_east, east_flip)
        north_term = permute_side(from_north, north_flip)
        joined = jnp.concatenate(
            [side_values[..., :SIDE] - east_term, side_values[..., SIDE : 2 * SIDE] - north_term], 3
        )
        return joined * edge_mask

    def patch_products(matrices, vectors):
        return (
            jnp.einsum("rpab,rpcb->rpca", matrices, vectors, preferred_element_type=jnp.float32)
            * active
        )

    def spread_pair(first, second):
        east_perm = jnp.stack(
            [permute_side(first[..., :SIDE], east_flip), permute_side(second[..., :SIDE], east_flip)]
        )
        north_perm = jnp.stack(
            [permute_side(first[..., SIDE:], north_flip), permute_side(second[..., SIDE:], north_flip)]
        )
        west_edge = passed_along(east_perm, "py", 1)
        from_west = jnp.concatenate([west_edge, east_perm[:, :, :-1]], 2)
        south_edge = passed_along(north_perm, "px", 1)
        from_south = jnp.concatenate([south_edge, north_perm[:, :-1]], 1)
        return [
            (field[..., :SIDE], field[..., SIDE:], from_west[k], from_south[k])
            for k, field in enumerate((first, second))
        ]

    def jump_and_spread(side_values):
        east_side = side_values[..., :SIDE]
        north_side = side_values[..., SIDE : 2 * SIDE]
        west_side = side_values[..., 2 * SIDE : 3 * SIDE]
        south_side = side_values[..., 3 * SIDE :]
        ones = jnp.broadcast_to(active, east_side.shape)
        east_edge, north_edge = exchanged_together(
            [(west_side, "py", -1), (south_side, "px", -1)]
        )
        from_east = jnp.concatenate([west_side[:, 1:], east_edge], 1)
        from_north = jnp.concatenate([south_side[1:], north_edge], 0)
        east_perm_side = permute_side(east_side, east_flip)
        north_perm_side = permute_side(north_side, north_flip)
        east_term = permute_side(from_east, east_flip)
        north_term = permute_side(from_north, north_flip)
        joined = jnp.concatenate([east_side - east_term, north_side - north_term], 3)
        half_jump = 0.5 * (joined * edge_mask)
        rz_partial = jnp.sum(start_res * half_jump, axis=(0, 1, 3))
        rz_py = jnp.sum(gathered(rz_partial, "py"), axis=0)
        rz_py, west_load, south_load = lax.optimization_barrier(
            (rz_py, jnp.stack([east_perm_side, ones]), jnp.stack([north_perm_side, ones]))
        )
        west_sent = passed_along(west_load, "py", 1)
        south_sent = passed_along(south_load, "px", 1)
        west_edge = 0.5 * ((west_sent[0] - west_side[:, :1]) * west_sent[1])
        south_edge = 0.5 * ((south_sent[0] - south_side[:1]) * south_sent[1])
        local_east = permute_side(half_jump[..., :SIDE], east_flip)
        local_north = permute_side(half_jump[..., SIDE:], north_flip)
        from_west = jnp.concatenate([west_edge, local_east[:, :-1]], 1)
        from_south = jnp.concatenate([south_edge, local_north[:-1]], 0)
        return half_jump, (half_jump[..., :SIDE], half_jump[..., SIDE:], from_west, from_south), rz_py

    start_sol = solution * edge_mask
    start_res = residual * edge_mask
    start_dir = direction * edge_mask
    res_parts, dir_parts = spread_pair(0.5 * start_res, start_dir)
    spread = spread_of(res_parts).astype(jnp.bfloat16)
    side_values = patch_products(dual_schur, spread)
    precond, precond_parts, rz_py = jump_and_spread(side_values)
    rz_current = jnp.sum(gathered(rz_py, "px"), axis=0)
    step_ratio = rz_current / rz_previous
    ratio = step_ratio[None, None, :, None]
    new_direction = precond + ratio * start_dir
    spread = spread_of(
        tuple(p + ratio * d for p, d in zip(precond_parts, dir_parts))
    ).astype(jnp.bfloat16)
    inner_part = patch_products(dual_inverse, spread)
    corner = (
        jnp.einsum("rpkb,rpcb->rpck", coupling, spread, preferred_element_type=jnp.float32) * active
    )
    corner_width = corner.shape[2] * corner.shape[3]
    payload = jnp.concatenate(
        [
            corner.reshape(rows_here, cols_here, corner_width),
            coarse_inverse.reshape(rows_here, cols_here, 4),
        ],
        2,
    )
    from_west_col, from_east_col = exchanged_together([(payload, "py", 1), (payload, "py", -1)])
    row = jnp.concatenate([from_west_col[:, -1:], payload, from_east_col[:, :1]], 1)
    from_south_row, from_north_row = exchanged_together([(row, "px", 1), (row, "px", -1)])
    block = jnp.concatenate([from_south_row[-1:], row, from_north_row[:1]], 0)
    corners = block[..., :corner_width].reshape(
        rows_here + 2, cols_here + 2, corner.shape[2], corner.shape[3]
    )
    blocks = block[..., corner_width:].reshape(rows_here + 2, cols_here + 2, 2, 2)
    vertex_row = lax.axis_index("px") * rows_here + jnp.arange(rows_here + 1)
    vertex_col = lax.axis_index("py") * cols_here + jnp.arange(cols_here + 1)
    vertex_ok = ((vertex_row >= 1)[:, None] & (vertex_col >= 1)[None, :]).astype(jnp.float32)[
        :, :, None, None
    ]
    assembled = (
        corners[1:, 1:, :, 0:2]
        + corners[1:, :-1, :, 2:4]
        + corners[:-1, 1:, :, 4:6]
        + corners[:-1, :-1, :, 6:8]
    ) * vertex_ok
    coarse = jnp.einsum(
        "rpxy,rpcy->rpcx", blocks[1:, 1:], assembled, precision=lax.Precision.HIGHEST
    )
    corners_back = jnp.concatenate(
        [coarse[:-1, :-1], coarse[:-1, 1:], coarse[1:, :-1], coarse[1:, 1:]], 3
    )
    correction = jnp.einsum(
        "rpkb,rpck->rpcb",
        coupling.astype(jnp.float32),
        corners_back,
        precision=lax.Precision.HIGHEST,
    )
    image = jump_b((inner_part + correction) * active)
    curvature, (res_res, res_img, img_img) = all_sum_mixed(
        jnp.sum(new_direction * image, axis=(0, 1, 3)),
        df_case_sums_stacked(
            jnp.stack([start_res, start_res, image]), jnp.stack([start_res, image, image])
        ),
    )
    step_length = rz_current / curvature
    new_solution = start_sol + step_length[None, None, :, None] * new_direction
    new_residual = start_res - step_length[None, None, :, None] * image
    cross = df_scale(res_img, -2.0 * step_length)
    square = df_scale(df_scale(img_img, step_length), step_length)
    merged = df_add(df_add(res_res, cross), square)
    merged_sq = merged[0] + merged[1]
    scale = res_res[0] + step_length * step_length * img_img[0]
    trusted = jnp.all(jnp.isfinite(scale) & (merged_sq > 0) & (scale <= 1e7 * merged_sq))
    residual_sq = lax.cond(
        trusted,
        lambda: merged_sq,
        lambda: all_sum(jnp.sum(new_residual * new_residual, axis=(0, 1, 3))),
    )
    return (new_solution, new_residual, new_direction, rz_current, residual_sq)


def solution(mesh):
    in_specs = (
        P("px", "py", None, None),
        P("px", "py", None, None),
        P("px", "py", None, None),
        P(),
        P("px", "py", None, None),
        P("px", "py", None, None),
        P("px", "py", None, None),
        P("px", "py", None, None),
        P("px", "py", None, None),
        P("px", "py"),
    )
    out_specs = (
        P("px", "py", None, None),
        P("px", "py", None, None),
        P("px", "py", None, None),
        P(),
        P(),
    )
    return jax.shard_map(
        on_device, mesh=mesh, in_specs=in_specs, out_specs=out_specs, check_vma=False
    )
```
